128 devices in a mesh: tx: 8 (over z, core), ty: 16 (over y, x).
Axes of the slice: x: 4, y: 4, z: 4, core: 2. Of those that a mesh axis runs over, the one named last changes fastest.
Arguments:
- object_init: float32 [4, 2048, 4096], P(None, 'tx', 'ty'), may hold values from -5 to 5
- probe: float32 [2, 128, 128], replicated, may hold values from -4 to 4
- propagator_phase: float32 [128, 128], replicated, may hold values from -3.140625 to 3.140625
- measured: bfloat16 [8, 16, 16, 2, 128, 128], P('tx', 'ty'), may hold values from 0 to 1.5
- corners: int32 [8, 16, 16, 2], P('tx', 'ty'), may hold values from 0 to 128
- owner_column: int32 [8, 16, 16, 1], P('tx', 'ty'), may hold values from 0 to 15; in each aligned block of 16 rows (0 to 15, 16 to 31, ..., all dimensions but the last counted through in order) at most 2 rows name the same one
Outputs:
- object_final: float32 [4, 2048, 4096], P(None, 'tx', 'ty')
The draws below stay inside these ranges and needn't reach their ends.
Inputs may be any that keep to these rules, and one draw needn't show every extreme that they name: `owner_column`: at most 2 of the 16 positions of one tile name the same owner column.
All inputs are finite; a program needn't handle non-finite values.
Results may differ from the reference program's by a relative error of at most 0.0049.
Values may be sent and summed in bfloat16 or wider, within the bound.
No kernel may reach another device: no remote copies, remote signals or barrier semaphores. Data moves between devices by JAX's collectives and lax.ppermute only.
A program may use at most 128 MiB of HBM per device.

```python
import math
import jax
import jax.numpy as jnp
import numpy as np
from jax import lax

WINDOW = 128
SLICES = 2
TILE = 256
PATCH_DEV = 16
CAP = 2
ITERS = 1
NR = 2048
NC = 4096
N_TX = 8
N_TY = 16


def set_ends(array, own_key, low, high):
    index_at = [jax.random.randint(jax.random.fold_in(own_key, axis), (), 0, length) for axis, length in enumerate(array.shape)]
    longest = array.shape.index(max(array.shape))
    beside = index_at[:longest] + [(index_at[longest] + 1) % array.shape[longest]] + index_at[longest + 1:]
    return array.at[tuple(index_at)].set(low).at[tuple(beside)].set(high)


def block_levels(stream_key, shape, split, least, largest):
    def one(position, blocks):
        heights = jax.random.uniform(jax.random.fold_in(jax.random.fold_in(stream_key, 6), position), (blocks,), jnp.float32, least / len(split), largest / len(split))
        return jnp.repeat(jnp.exp(heights), shape[position] // blocks).reshape((-1,) + (1,) * (len(shape) - position - 1))

    level = one(*split[0])
    for cut in split[1:]:
        level = level * one(*cut)
    return level


def routed_block(rng, own, number, rows, count, top, bound, slope):
    ranking = jax.random.permutation(rng, count)
    crowded, ordinary = shares(count, rows * top, bound, slope, True), shares(count, rows * top, bound, slope, False)
    places = jnp.arange(count)

    def named(sizes, turn):
        used = int((sizes > 0).sum())
        fixed = max(1, used // 4)
        moved = fixed + (places - fixed + turn * (used - fixed)) % max(1, count - fixed)
        return jnp.zeros((count,), jnp.int32).at[ranking[jnp.where(places < fixed, places, moved)]].set(jnp.asarray(sizes, jnp.int32))

    sizes = jnp.where(number % 4 == 0, named(crowded, number // 4), named(ordinary, number - number // 4 - 1))
    mixed = jax.random.permutation(jax.random.fold_in(own, 3), count)
    giver, taker = mixed[0:count // 2 * 2:2], mixed[1:count // 2 * 2:2]
    room = jnp.minimum(sizes[giver] - 1, bound - sizes[taker]) // 2
    room = jnp.where((giver == ranking[0]) | (taker == ranking[0]) | (sizes[taker] == 0), 0, jnp.maximum(room, 0))
    moved = jax.random.randint(jax.random.fold_in(own, 4), (count // 2,), 0, 1 << 20) % (room + 1)
    sizes = sizes.at[giver].add(-moved).at[taker].add(moved)
    members = jnp.searchsorted(jnp.cumsum(sizes), jnp.arange(rows * top), side="right").astype(jnp.int32)
    table = members.reshape(top, rows).T
    table = table[jax.random.permutation(jax.random.fold_in(own, 1), rows)]
    turn = jax.random.randint(jax.random.fold_in(own, 2), (rows, 1), 0, top)
    return jnp.take_along_axis(table, (jnp.arange(top)[None, :] + turn) % top, axis=1)


def shares(amount, total, most, slope, full):
    loads = [(1 << 20) // math.isqrt(rank ** slope) + 1 for rank in range(1, amount + 1)]
    largest = most if full else min(most, max(-(-total // amount), total * loads[0] // sum(loads)))
    least = 1 if total - largest >= amount - 1 else 0
    given, spare = [largest] + [least] * (amount - 1), total - largest - least * (amount - 1)
    while spare > 0:
        free = [i for i in range(1, amount) if given[i] < largest] or [i for i in range(1, amount) if given[i] < most]
        pool, remaining = sum([loads[i] for i in free]), spare
        for i in free:
            addition = min(most - given[i], max(1, remaining * loads[i] // pool), spare)
            given[i] = given[i] + addition
            spare = spare - addition
    return np.array(given)


def bell_draw(rng, shape, scale, most, split=(), held_as=jnp.bfloat16):
    entries = scale * jax.random.normal(rng, shape, jnp.float32)
    if split:
        entries = entries * block_levels(rng, shape, split, -0.22, 0.18)
    return jnp.clip(entries, -most, most).astype(held_as)


def setup_inputs(seed: int = 0) -> dict:
    splits = jax.random.split(jax.random.key(seed), 7)
    object_init = bell_draw(splits[0], (2 * SLICES, NR, NC), 0.7, 5.0, ((1, 8), (2, 16)), jnp.float32)
    probe = bell_draw(splits[1], (2, WINDOW, WINDOW), 0.5, 4.0, (), jnp.float32)
    propagator_phase = jnp.clip(jax.random.uniform(splits[2], (WINDOW, WINDOW), jnp.float32, -3.140625, 3.140625), -3.140625, 3.140625)
    measured = jnp.clip(1.5 * jax.random.uniform(splits[3], (N_TX, N_TY, N_TY, CAP, WINDOW, WINDOW), jnp.float32) ** block_levels(splits[3], (N_TX, N_TY, N_TY, CAP, WINDOW, WINDOW), ((0, 8), (1, 16)), -0.2, 0.2), 0.0, 1.5).astype(jnp.bfloat16)
    corners = set_ends(jax.random.randint(splits[4], (N_TX, N_TY, PATCH_DEV, 2), 0, TILE - WINDOW + 1), jax.random.fold_in(splits[4], 1), 0, TILE - WINDOW).astype(jnp.int32)
    owner_column_keys = jax.random.split(jax.random.fold_in(splits[5], 1), N_TX * N_TY * PATCH_DEV // PATCH_DEV)
    owner_column_turns = jax.random.permutation(jax.random.fold_in(splits[5], 3), N_TX * N_TY * PATCH_DEV // PATCH_DEV)
    owner_column = jax.vmap(lambda own, number: routed_block(jax.random.fold_in(splits[5], 2), own, number, PATCH_DEV, N_TY, 1, CAP, 2))(owner_column_keys, owner_column_turns).reshape((N_TX, N_TY, PATCH_DEV, 1))
    return {"object_init": object_init, "probe": probe, "propagator_phase": propagator_phase, "measured": measured, "corners": corners, "owner_column": owner_column}


exact = lax.Precision.HIGHEST
step_rate = 0.5
smooth_rate = 0.2

def dft_tables(width):
    index = jnp.arange(width)
    product = index[:, None] * index[None, :] % width
    angles = product.astype(jnp.float32) * (2.0 * math.pi / width)
    scale = 1.0 / math.sqrt(width)
    return (jnp.cos(angles) * scale, jnp.sin(angles) * scale)

def left_apply(matrix, field):
    return jnp.einsum('ij,...jk->...ik', matrix, field, precision=exact)

def right_apply(field, matrix):
    return jnp.einsum('...ij,jk->...ik', field, matrix, precision=exact)

def transform(pair, cosine, sine, sign):
    real_part, imag_part = pair
    imag_table = sign * sine
    left_real = left_apply(cosine, real_part) - left_apply(imag_table, imag_part)
    left_imag = left_apply(cosine, imag_part) + left_apply(imag_table, real_part)
    return (right_apply(left_real, cosine) - right_apply(left_imag, imag_table), right_apply(left_real, imag_table) + right_apply(left_imag, cosine))

def times_complex(first, second):
    return (first[0] * second[0] - first[1] * second[1], first[0] * second[1] + first[1] * second[0])

def conjugate_times(first, second):
    return (first[0] * second[0] + first[1] * second[1], first[0] * second[1] - first[1] * second[0])

def window_gradients(windows, amplitude, probe, phase, cosine, sine):
    slices = windows.shape[1] // 2
    layers = [(windows[:, 2 * layer], windows[:, 2 * layer + 1]) for layer in range(slices)]
    probe_pair = (probe[0], probe[1])
    kernel = (jnp.cos(phase), jnp.sin(phase))
    kernel_conj = (kernel[0], -kernel[1])

    def propagate(field, factor):
        spectrum = transform(field, cosine, sine, -1.0)
        return transform(times_complex(factor, spectrum), cosine, sine, 1.0)
    wave = times_complex(probe_pair, layers[0])
    incoming = []
    for layer in range(1, slices):
        moved = propagate(wave, kernel)
        incoming.append(moved)
        wave = times_complex(layers[layer], moved)
    far_field = transform(wave, cosine, sine, -1.0)
    magnitude = jnp.sqrt(far_field[0] * far_field[0] + far_field[1] * far_field[1] + 1.0)
    factor = 1.0 - amplitude / magnitude
    back = transform((far_field[0] * factor, far_field[1] * factor), cosine, sine, 1.0)
    grads = [None] * slices
    for layer in range(slices - 1, 0, -1):
        grads[layer] = conjugate_times(incoming[layer - 1], back)
        back = propagate(conjugate_times(layers[layer], back), kernel_conj)
    grads[0] = conjugate_times(probe_pair, back)
    return jnp.stack([part for pair in grads for part in pair], axis=1)

def slot_table(owner):
    order = jnp.arange(owner.shape[0])
    same = owner[:, None] == owner[None, :]
    earlier = order[None, :] < order[:, None]
    return lax.optimization_barrier(jnp.sum(jnp.where(same & earlier, 1, 0), axis=1)).astype(jnp.int32)

def smooth_padded(padded):
    center = padded[:, 1:-1, 1:-1]
    views = [padded[:, 2:, 1:-1], padded[:, :-2, 1:-1], padded[:, 1:-1, 2:], padded[:, 1:-1, :-2]]
    slices = center.shape[0] // 2
    total = jnp.zeros_like(center)
    for view in views:
        pairs = (view - center).reshape((slices, 2) + center.shape[1:])
        weight = 1.0 / jnp.sqrt(1.0 + pairs[:, 0] * pairs[:, 0] + pairs[:, 1] * pairs[:, 1])
        total = total + (pairs * weight[:, None]).reshape(center.shape)
    return center + smooth_rate * total

def accumulate(total, grads, tops, lefts):
    zero_index = jnp.zeros((), jnp.int32)

    def add_one(index, acc):
        piece = grads[index].astype(jnp.float32)
        start = (zero_index, tops[index].astype(jnp.int32), lefts[index].astype(jnp.int32))
        current = lax.dynamic_slice(acc, start, piece.shape)
        return lax.dynamic_update_slice(acc, current + piece, start)
    return lax.fori_loop(0, grads.shape[0], add_one, total)

def reference(object_init, probe, propagator_phase, measured, corners, owner_column):
    cosine, sine = dft_tables(WINDOW)
    field = object_init
    channels = field.shape[0]
    zero_index = jnp.zeros((), jnp.int32)
    for iteration in range(ITERS):

        def tile_step(index, total):
            index = jnp.asarray(index).astype(jnp.int32)
            row_tile = index // N_TY
            col_tile = index % N_TY
            tops = (corners[row_tile, col_tile, :, 0] + row_tile * TILE).astype(jnp.int32)
            lefts = (corners[row_tile, col_tile, :, 1] + col_tile * TILE).astype(jnp.int32)
            windows = jax.vmap(lambda top, left: lax.dynamic_slice(field, (zero_index, top, left), (channels, WINDOW, WINDOW)))(tops, lefts)
            windows = windows.astype(jnp.bfloat16)
            owner = owner_column[row_tile, col_tile, :, 0]
            slot = slot_table(owner)
            amplitude = measured[row_tile, owner, col_tile, slot]
            grads = window_gradients(windows.astype(jnp.float32), amplitude.astype(jnp.float32), probe, propagator_phase, cosine, sine)
            return accumulate(total, grads.astype(jnp.bfloat16), tops, lefts)
        total = lax.fori_loop(0, N_TX * N_TY, tile_step, jnp.zeros(field.shape, jnp.float32))
        updated = field - step_rate * total
        field = smooth_padded(jnp.pad(updated, ((0, 0), (1, 1), (1, 1))))
    return field
```

```python
import math

import jax
import jax.numpy as jnp
from jax import lax
from jax.sharding import PartitionSpec as P

exact = lax.Precision.HIGHEST
step_rate = 0.5
smooth_rate = 0.2


def dft_tables(width):
    index = jnp.arange(width)
    product = index[:, None] * index[None, :] % width
    angles = product.astype(jnp.float32) * (2.0 * math.pi / width)
    scale = 1.0 / math.sqrt(width)
    return (jnp.cos(angles) * scale, jnp.sin(angles) * scale)


def left_apply(matrix, field):
    return jnp.einsum("ij,...jk->...ik", matrix, field, precision=exact)


def right_apply(field, matrix):
    return jnp.einsum("...ij,jk->...ik", field, matrix, precision=exact)


def transform(pair, cosine, sine, sign):
    real_part, imag_part = pair
    imag_table = sign * sine
    left_real = left_apply(cosine, real_part) - left_apply(imag_table, imag_part)
    left_imag = left_apply(cosine, imag_part) + left_apply(imag_table, real_part)
    return (
        right_apply(left_real, cosine) - right_apply(left_imag, imag_table),
        right_apply(left_real, imag_table) + right_apply(left_imag, cosine),
    )


def times_complex(first, second):
    return (
        first[0] * second[0] - first[1] * second[1],
        first[0] * second[1] + first[1] * second[0],
    )


def conjugate_times(first, second):
    return (
        first[0] * second[0] + first[1] * second[1],
        first[0] * second[1] - first[1] * second[0],
    )


def window_gradients(windows, amplitude, probe, phase, cosine, sine):
    slices = windows.shape[1] // 2
    layers = [(windows[:, 2 * layer], windows[:, 2 * layer + 1]) for layer in range(slices)]
    probe_pair = (probe[0], probe[1])
    kernel = (jnp.cos(phase), jnp.sin(phase))
    kernel_conj = (kernel[0], -kernel[1])

    def propagate(field, factor):
        spectrum = transform(field, cosine, sine, -1.0)
        return transform(times_complex(factor, spectrum), cosine, sine, 1.0)

    wave = times_complex(probe_pair, layers[0])
    incoming = []
    for layer in range(1, slices):
        moved = propagate(wave, kernel)
        incoming.append(moved)
        wave = times_complex(layers[layer], moved)
    far_field = transform(wave, cosine, sine, -1.0)
    magnitude = jnp.sqrt(far_field[0] * far_field[0] + far_field[1] * far_field[1] + 1.0)
    factor = 1.0 - amplitude / magnitude
    back = transform((far_field[0] * factor, far_field[1] * factor), cosine, sine, 1.0)
    grads = [None] * slices
    for layer in range(slices - 1, 0, -1):
        grads[layer] = conjugate_times(incoming[layer - 1], back)
        back = propagate(conjugate_times(layers[layer], back), kernel_conj)
    grads[0] = conjugate_times(probe_pair, back)
    return jnp.stack([part for pair in grads for part in pair], axis=1)


def slot_table(owner):
    order = jnp.arange(owner.shape[0])
    same = owner[:, None] == owner[None, :]
    earlier = order[None, :] < order[:, None]
    return jnp.sum(jnp.where(same & earlier, 1, 0), axis=1).astype(jnp.int32)


def shifted_neighbours(updated):
    rows_axis = "tx"
    cols_axis = "ty"
    n_rows = lax.axis_size(rows_axis)
    n_cols = lax.axis_size(cols_axis)
    up_rows = [(i, i + 1) for i in range(n_rows - 1)]
    down_rows = [(i + 1, i) for i in range(n_rows - 1)]
    up_cols = [(i, i + 1) for i in range(n_cols - 1)]
    down_cols = [(i + 1, i) for i in range(n_cols - 1)]
    above = lax.ppermute(updated[:, -1:, :], rows_axis, up_rows)
    below = lax.ppermute(updated[:, :1, :], rows_axis, down_rows)
    left = lax.ppermute(updated[:, :, -1:], cols_axis, up_cols)
    right = lax.ppermute(updated[:, :, :1], cols_axis, down_cols)
    north = jnp.concatenate([above, updated[:, :-1, :]], axis=1)
    south = jnp.concatenate([updated[:, 1:, :], below], axis=1)
    west = jnp.concatenate([left, updated[:, :, :-1]], axis=2)
    east = jnp.concatenate([updated[:, :, 1:], right], axis=2)
    return south, north, east, west


def smooth(center):
    slices = center.shape[0] // 2
    total = jnp.zeros_like(center)
    for view in shifted_neighbours(center):
        pairs = (view - center).reshape((slices, 2) + center.shape[1:])
        weight = 1.0 / jnp.sqrt(1.0 + pairs[:, 0] * pairs[:, 0] + pairs[:, 1] * pairs[:, 1])
        total = total + (pairs * weight[:, None]).reshape(center.shape)
    return center + smooth_rate * total


def per_device(object_init, probe, propagator_phase, measured, corners, owner_column):
    width = probe.shape[-1]
    cosine, sine = dft_tables(width)
    field = object_init
    tile = field.shape[1]
    capacity = measured.shape[3]
    columns = lax.axis_size("ty")
    tops = corners[0, 0, :, 0]
    lefts = corners[0, 0, :, 1]
    owner = owner_column[0, 0, :, 0]
    slot = slot_table(owner)
    target = owner * capacity + slot
    gathered = lax.all_to_all(measured[0, 0], "ty", split_axis=0, concat_axis=0, tiled=True)
    gathered = gathered.reshape(columns * capacity, width, width)
    pick = (jnp.arange(columns * capacity)[None, :] == target[:, None]).astype(jnp.bfloat16)
    amplitude = jnp.einsum("km,mij->kij", pick, gathered, preferred_element_type=jnp.float32)
    offsets = jnp.arange(width)
    cells = jnp.arange(tile)
    row_pick = (cells[None, None, :] == (tops[:, None, None] + offsets[None, :, None])).astype(
        jnp.bfloat16
    )
    col_pick = (cells[None, :, None] == (lefts[:, None, None] + offsets[None, None, :])).astype(
        jnp.bfloat16
    )
    field_low = field.astype(jnp.bfloat16)
    rows = jnp.einsum(
        "kir,crs->kcis", row_pick, field_low, preferred_element_type=jnp.float32
    ).astype(jnp.bfloat16)
    windows = jnp.einsum("kcis,ksj->kcij", rows, col_pick, preferred_element_type=jnp.float32)
    grads = window_gradients(
        windows, amplitude, probe, propagator_phase, cosine, sine
    ).astype(jnp.bfloat16)
    spread = jnp.einsum(
        "kcij,ksj->kcis", grads, col_pick, preferred_element_type=jnp.float32
    ).astype(jnp.bfloat16)
    total = jnp.einsum("kir,kcis->crs", row_pick, spread, preferred_element_type=jnp.float32)
    updated = field - step_rate * total
    return smooth(updated)


def solution(mesh):
    placed = (
        P(None, "tx", "ty"),
        P(),
        P(),
        P("tx", "ty", None, None, None, None),
        P("tx", "ty", None, None),
        P("tx", "ty", None, None),
    )
    return jax.shard_map(
        per_device, mesh=mesh, in_specs=placed, out_specs=P(None, "tx", "ty"), check_vma=False
    )
```

```python
import math

import jax
import jax.numpy as jnp
from jax import lax
from jax.experimental import pallas as pl
from jax.sharding import PartitionSpec as P

exact = lax.Precision.HIGHEST
step_rate = 0.5
smooth_rate = 0.2


def dft_tables(width):
    index = jnp.arange(width)
    product = index[:, None] * index[None, :] % width
    angles = product.astype(jnp.float32) * (2.0 * math.pi / width)
    scale = 1.0 / math.sqrt(width)
    return (jnp.cos(angles) * scale, jnp.sin(angles) * scale)


def left_apply(matrix, field):
    return jnp.einsum("ij,...jk->...ik", matrix, field, precision=exact)


def right_apply(field, matrix):
    return jnp.einsum("...ij,jk->...ik", field, matrix, precision=exact)


def transform(pair, cosine, sine, sign):
    real_part, imag_part = pair
    imag_table = sign * sine
    left_real = left_apply(cosine, real_part) - left_apply(imag_table, imag_part)
    left_imag = left_apply(cosine, imag_part) + left_apply(imag_table, real_part)
    return (
        right_apply(left_real, cosine) - right_apply(left_imag, imag_table),
        right_apply(left_real, imag_table) + right_apply(left_imag, cosine),
    )


def times_complex(first, second):
    return (
        first[0] * second[0] - first[1] * second[1],
        first[0] * second[1] + first[1] * second[0],
    )


def conjugate_times(first, second):
    return (
        first[0] * second[0] + first[1] * second[1],
        first[0] * second[1] - first[1] * second[0],
    )


def window_gradients(windows, amplitude, probe, phase, cosine, sine):
    slices = windows.shape[1] // 2
    layers = [(windows[:, 2 * layer], windows[:, 2 * layer + 1]) for layer in range(slices)]
    probe_pair = (probe[0], probe[1])
    kernel = (jnp.cos(phase), jnp.sin(phase))
    kernel_conj = (kernel[0], -kernel[1])

    def propagate(field, factor):
        spectrum = transform(field, cosine, sine, -1.0)
        return transform(times_complex(factor, spectrum), cosine, sine, 1.0)

    wave = times_complex(probe_pair, layers[0])
    incoming = []
    for layer in range(1, slices):
        moved = propagate(wave, kernel)
        incoming.append(moved)
        wave = times_complex(layers[layer], moved)
    far_field = transform(wave, cosine, sine, -1.0)
    magnitude = jnp.sqrt(far_field[0] * far_field[0] + far_field[1] * far_field[1] + 1.0)
    factor = 1.0 - amplitude / magnitude
    back = transform((far_field[0] * factor, far_field[1] * factor), cosine, sine, 1.0)
    grads = [None] * slices
    for layer in range(slices - 1, 0, -1):
        grads[layer] = conjugate_times(incoming[layer - 1], back)
        back = propagate(conjugate_times(layers[layer], back), kernel_conj)
    grads[0] = conjugate_times(probe_pair, back)
    return jnp.stack([part for pair in grads for part in pair], axis=1)


def slot_table(owner):
    order = jnp.arange(owner.shape[0])
    same = owner[:, None] == owner[None, :]
    earlier = order[None, :] < order[:, None]
    return jnp.sum(jnp.where(same & earlier, 1, 0), axis=1).astype(jnp.int32)


def shifted_neighbours(updated):
    rows_axis = "tx"
    cols_axis = "ty"
    n_rows = lax.axis_size(rows_axis)
    n_cols = lax.axis_size(cols_axis)
    up_rows = [(i, i + 1) for i in range(n_rows - 1)]
    down_rows = [(i + 1, i) for i in range(n_rows - 1)]
    up_cols = [(i, i + 1) for i in range(n_cols - 1)]
    down_cols = [(i + 1, i) for i in range(n_cols - 1)]
    above = lax.ppermute(updated[:, -1:, :], rows_axis, up_rows)
    below = lax.ppermute(updated[:, :1, :], rows_axis, down_rows)
    left = lax.ppermute(updated[:, :, -1:], cols_axis, up_cols)
    right = lax.ppermute(updated[:, :, :1], cols_axis, down_cols)
    north = jnp.concatenate([above, updated[:, :-1, :]], axis=1)
    south = jnp.concatenate([updated[:, 1:, :], below], axis=1)
    west = jnp.concatenate([left, updated[:, :, :-1]], axis=2)
    east = jnp.concatenate([updated[:, :, 1:], right], axis=2)
    return south, north, east, west


def smooth(center):
    slices = center.shape[0] // 2
    total = jnp.zeros_like(center)
    for view in shifted_neighbours(center):
        pairs = (view - center).reshape((slices, 2) + center.shape[1:])
        weight = 1.0 / jnp.sqrt(1.0 + pairs[:, 0] * pairs[:, 0] + pairs[:, 1] * pairs[:, 1])
        total = total + (pairs * weight[:, None]).reshape(center.shape)
    return center + smooth_rate * total


def block_tables(cosine, sine):
    plus = jnp.block([[cosine, -sine], [sine, cosine]])
    minus = jnp.block([[cosine, sine], [-sine, cosine]])
    tables = []
    for table in (plus, minus):
        high = lax.reduce_precision(table, exponent_bits=8, mantissa_bits=7)
        low = (table - high).astype(jnp.bfloat16)
        tables += [high.astype(jnp.bfloat16), low]
    return jnp.stack(tables)


def _split(x):
    high = x.astype(jnp.bfloat16)
    low = (x - high.astype(jnp.float32)).astype(jnp.bfloat16)
    return high, low


def _dot(a, b):
    return jnp.dot(a, b, preferred_element_type=jnp.float32)


def _gradient_kernel(win_ref, amp_ref, probe_ref, prop_ref, tab_ref, out_ref):
    width = probe_ref.shape[-1]
    slices = win_ref.shape[1] // 2

    def left(index, x):
        high, low = _split(x)
        return _dot(tab_ref[index], high) + _dot(tab_ref[index + 1], high) + _dot(tab_ref[index], low)

    def right(x, index):
        high, low = _split(x)
        return _dot(high, tab_ref[index]) + _dot(high, tab_ref[index + 1]) + _dot(low, tab_ref[index])

    def transform(pair, sign):
        first, second = (2, 0) if sign < 0 else (0, 2)
        stacked = jnp.concatenate([pair[0], pair[1]], axis=0)
        rows = left(first, stacked)
        joined = jnp.concatenate([rows[:width], rows[width:]], axis=1)
        out = right(joined, second)
        return out[:, :width], out[:, width:]

    def times(a, b):
        return (a[0] * b[0] - a[1] * b[1], a[0] * b[1] + a[1] * b[0])

    def conj_times(a, b):
        return (a[0] * b[0] + a[1] * b[1], a[0] * b[1] - a[1] * b[0])

    layers = [
        (win_ref[0, 2 * s].astype(jnp.float32), win_ref[0, 2 * s + 1].astype(jnp.float32))
        for s in range(slices)
    ]
    probe = (probe_ref[0], probe_ref[1])
    kernel = (prop_ref[0], prop_ref[1])
    kernel_conj = (prop_ref[0], -prop_ref[1])

    def propagate(field, factor):
        return transform(times(factor, transform(field, -1)), 1)

    wave = times(probe, layers[0])
    incoming = []
    for s in range(1, slices):
        moved = propagate(wave, kernel)
        incoming.append(moved)
        wave = times(layers[s], moved)
    far = transform(wave, -1)
    magnitude = jnp.sqrt(far[0] * far[0] + far[1] * far[1] + 1.0)
    factor = 1.0 - amp_ref[0].astype(jnp.float32) / magnitude
    back = transform((far[0] * factor, far[1] * factor), 1)
    grads = [None] * slices
    for s in range(slices - 1, 0, -1):
        grads[s] = conj_times(incoming[s - 1], back)
        back = propagate(conj_times(layers[s], back), kernel_conj)
    grads[0] = conj_times(probe, back)
    for s in range(slices):
        out_ref[0, 2 * s] = grads[s][0].astype(out_ref.dtype)
        out_ref[0, 2 * s + 1] = grads[s][1].astype(out_ref.dtype)


def fused_gradients(windows, amplitude, probe, phase, tables):
    count, channels, width, _ = windows.shape
    kernel = jnp.stack([jnp.cos(phase), jnp.sin(phase)])
    return pl.pallas_call(
        _gradient_kernel,
        grid=(count,),
        in_specs=[
            pl.BlockSpec((1, channels, width, width), lambda k: (k, 0, 0, 0)),
            pl.BlockSpec((1, width, width), lambda k: (k, 0, 0)),
            pl.BlockSpec((2, width, width), lambda k: (0, 0, 0)),
            pl.BlockSpec((2, width, width), lambda k: (0, 0, 0)),
            pl.BlockSpec((4, 2 * width, 2 * width), lambda k: (0, 0, 0)),
        ],
        out_specs=pl.BlockSpec((1, channels, width, width), lambda k: (k, 0, 0, 0)),
        out_shape=jax.ShapeDtypeStruct((count, channels, width, width), jnp.bfloat16),
    )(windows, amplitude, probe, kernel, tables)


def per_device(object_init, probe, propagator_phase, measured, corners, owner_column):
    width = probe.shape[-1]
    cosine, sine = dft_tables(width)
    field = object_init
    tile = field.shape[1]
    capacity = measured.shape[3]
    columns = lax.axis_size("ty")
    tops = corners[0, 0, :, 0]
    lefts = corners[0, 0, :, 1]
    owner = owner_column[0, 0, :, 0]
    slot = slot_table(owner)
    target = owner * capacity + slot
    gathered = lax.all_to_all(measured[0, 0], "ty", split_axis=0, concat_axis=0, tiled=True)
    gathered = gathered.reshape(columns * capacity, width, width)
    pick = (jnp.arange(columns * capacity)[None, :] == target[:, None]).astype(jnp.bfloat16)
    amplitude = jnp.einsum(
        "km,mij->kij", pick, gathered, preferred_element_type=jnp.float32
    ).astype(jnp.bfloat16)
    offsets = jnp.arange(width)
    cells = jnp.arange(tile)
    row_pick = (cells[None, None, :] == (tops[:, None, None] + offsets[None, :, None])).astype(
        jnp.bfloat16
    )
    col_pick = (cells[None, :, None] == (lefts[:, None, None] + offsets[None, None, :])).astype(
        jnp.bfloat16
    )
    field_low = field.astype(jnp.bfloat16)
    rows = jnp.einsum(
        "kir,crs->kcis", row_pick, field_low, preferred_element_type=jnp.float32
    ).astype(jnp.bfloat16)
    windows = jnp.einsum(
        "kcis,ksj->kcij", rows, col_pick, preferred_element_type=jnp.float32
    ).astype(jnp.bfloat16)
    tables = block_tables(cosine, sine)
    grads = fused_gradients(windows, amplitude, probe, propagator_phase, tables)
    spread = jnp.einsum(
        "kcij,ksj->kcis", grads, col_pick, preferred_element_type=jnp.float32
    ).astype(jnp.bfloat16)
    total = jnp.einsum("kir,kcis->crs", row_pick, spread, preferred_element_type=jnp.float32)
    updated = field - step_rate * total
    return smooth(updated)


def solution(mesh):
    placed = (
        P(None, "tx", "ty"),
        P(),
        P(),
        P("tx", "ty", None, None, None, None),
        P("tx", "ty", None, None),
        P("tx", "ty", None, None),
    )
    return jax.shard_map(
        per_device, mesh=mesh, in_specs=placed, out_specs=P(None, "tx", "ty"), check_vma=False
    )
```

```python
import math

import jax
import jax.numpy as jnp
from jax import lax
from jax.experimental import pallas as pl
from jax.sharding import PartitionSpec as P

step_rate = 0.5
smooth_rate = 0.2


def dft_tables(width):
    index = jnp.arange(width)
    product = index[:, None] * index[None, :] % width
    angles = product.astype(jnp.float32) * (2.0 * math.pi / width)
    scale = 1.0 / math.sqrt(width)
    return (jnp.cos(angles) * scale, jnp.sin(angles) * scale)


def slot_table(owner):
    order = jnp.arange(owner.shape[0])
    same = owner[:, None] == owner[None, :]
    earlier = order[None, :] < order[:, None]
    return jnp.sum(jnp.where(same & earlier, 1, 0), axis=1).astype(jnp.int32)


def shifted_neighbours(updated):
    rows_axis = "tx"
    cols_axis = "ty"
    n_rows = lax.axis_size(rows_axis)
    n_cols = lax.axis_size(cols_axis)
    up_rows = [(i, i + 1) for i in range(n_rows - 1)]
    down_rows = [(i + 1, i) for i in range(n_rows - 1)]
    up_cols = [(i, i + 1) for i in range(n_cols - 1)]
    down_cols = [(i + 1, i) for i in range(n_cols - 1)]
    above = lax.ppermute(updated[:, -1, :], rows_axis, up_rows)
    below = lax.ppermute(updated[:, 0, :], rows_axis, down_rows)
    left = lax.ppermute(updated[:, :, -1], cols_axis, up_cols)
    right = lax.ppermute(updated[:, :, 0], cols_axis, down_cols)
    north = jnp.concatenate([above[:, None, :], updated[:, :-1, :]], axis=1)
    south = jnp.concatenate([updated[:, 1:, :], below[:, None, :]], axis=1)
    west = jnp.concatenate([left[:, :, None], updated[:, :, :-1]], axis=2)
    east = jnp.concatenate([updated[:, :, 1:], right[:, :, None]], axis=2)
    return south, north, east, west


def smooth(center):
    slices = center.shape[0] // 2
    total = jnp.zeros_like(center)
    for view in shifted_neighbours(center):
        pairs = (view - center).reshape((slices, 2) + center.shape[1:])
        weight = 1.0 / jnp.sqrt(1.0 + pairs[:, 0] * pairs[:, 0] + pairs[:, 1] * pairs[:, 1])
        total = total + (pairs * weight[:, None]).reshape(center.shape)
    return center + smooth_rate * total


def block_tables(cosine, sine):
    plus = jnp.block([[cosine, -sine], [sine, cosine]])
    minus = jnp.block([[cosine, sine], [-sine, cosine]])
    lefts, rights = [], []
    for table in (plus, minus):
        high = lax.reduce_precision(table, exponent_bits=8, mantissa_bits=7)
        low = (table - high).astype(jnp.bfloat16)
        high = high.astype(jnp.bfloat16)
        lefts.append(jnp.concatenate([high, low, high], axis=1))
        rights.append(jnp.concatenate([high, low, high], axis=0))
    return jnp.stack(lefts), jnp.stack(rights)


def _split(x):
    high = x.astype(jnp.bfloat16)
    low = (x - high.astype(jnp.float32)).astype(jnp.bfloat16)
    return high, low


def _dot(a, b):
    return jnp.dot(a, b, preferred_element_type=jnp.float32)


def _gradient_kernel(win_ref, amp_ref, probe_ref, prop_ref, left_ref, right_ref, out_ref):
    group = win_ref.shape[0]
    width = probe_ref.shape[-1]
    slices = win_ref.shape[1] // 2

    def transform(pair, sign):
        first, second = (1, 0) if sign < 0 else (0, 1)
        stacked = jnp.concatenate(
            [jnp.concatenate([pair[0][g], pair[1][g]], axis=0) for g in range(group)], axis=1
        )
        high, low = _split(stacked)
        rows = _dot(left_ref[first], jnp.concatenate([high, high, low], axis=0))
        joined = jnp.concatenate(
            [
                jnp.concatenate(
                    [rows[:width, g * width:(g + 1) * width], rows[width:, g * width:(g + 1) * width]],
                    axis=1,
                )
                for g in range(group)
            ],
            axis=0,
        )
        high, low = _split(joined)
        out = _dot(jnp.concatenate([high, high, low], axis=1), right_ref[second])
        return (
            out[:, :width].reshape(group, width, width),
            out[:, width:].reshape(group, width, width),
        )

    def times(a, b):
        return (a[0] * b[0] - a[1] * b[1], a[0] * b[1] + a[1] * b[0])

    def conj_times(a, b):
        return (a[0] * b[0] + a[1] * b[1], a[0] * b[1] - a[1] * b[0])

    layers = [
        (win_ref[:, 2 * s].astype(jnp.float32), win_ref[:, 2 * s + 1].astype(jnp.float32))
        for s in range(slices)
    ]
    probe = (probe_ref[0][None], probe_ref[1][None])
    kernel = (prop_ref[0][None], prop_ref[1][None])
    kernel_conj = (prop_ref[0][None], -prop_ref[1][None])

    def propagate(field, factor):
        return transform(times(factor, transform(field, -1)), 1)

    wave = times(probe, layers[0])
    incoming = []
    for s in range(1, slices):
        moved = propagate(wave, kernel)
        incoming.append(moved)
        wave = times(layers[s], moved)
    far = transform(wave, -1)
    magnitude = jnp.sqrt(far[0] * far[0] + far[1] * far[1] + 1.0)
    factor = 1.0 - amp_ref[...].astype(jnp.float32) / magnitude
    back = transform((far[0] * factor, far[1] * factor), 1)
    grads = [None] * slices
    for s in range(slices - 1, 0, -1):
        grads[s] = conj_times(incoming[s - 1], back)
        back = propagate(conj_times(layers[s], back), kernel_conj)
    grads[0] = conj_times(probe, back)
    for s in range(slices):
        out_ref[:, 2 * s] = grads[s][0].astype(out_ref.dtype)
        out_ref[:, 2 * s + 1] = grads[s][1].astype(out_ref.dtype)


def fused_gradients(windows, amplitude, probe, phase, tables, group=8):
    count, channels, width, _ = windows.shape
    group = math.gcd(count, group)
    kernel = jnp.stack([jnp.cos(phase), jnp.sin(phase)])
    left_tables, right_tables = tables
    return pl.pallas_call(
        _gradient_kernel,
        grid=(count // group,),
        in_specs=[
            pl.BlockSpec((group, channels, width, width), lambda k: (k, 0, 0, 0)),
            pl.BlockSpec((group, width, width), lambda k: (k, 0, 0)),
            pl.BlockSpec((2, width, width), lambda k: (0, 0, 0)),
            pl.BlockSpec((2, width, width), lambda k: (0, 0, 0)),
            pl.BlockSpec(left_tables.shape, lambda k: (0, 0, 0)),
            pl.BlockSpec(right_tables.shape, lambda k: (0, 0, 0)),
        ],
        out_specs=pl.BlockSpec((group, channels, width, width), lambda k: (k, 0, 0, 0)),
        out_shape=jax.ShapeDtypeStruct((count, channels, width, width), jnp.bfloat16),
    )(windows, amplitude, probe, kernel, left_tables, right_tables)


def per_device(object_init, probe, propagator_phase, measured, corners, owner_column):
    width = probe.shape[-1]
    cosine, sine = dft_tables(width)
    field = object_init
    tile = field.shape[1]
    capacity = measured.shape[3]
    columns = lax.axis_size("ty")
    tops = corners[0, 0, :, 0]
    lefts = corners[0, 0, :, 1]
    owner = owner_column[0, 0, :, 0]
    slot = slot_table(owner)
    target = owner * capacity + slot
    gathered = lax.all_to_all(measured[0, 0], "ty", split_axis=0, concat_axis=0, tiled=True)
    gathered = gathered.reshape(columns * capacity, width, width)
    pick = (jnp.arange(columns * capacity)[None, :] == target[:, None]).astype(jnp.bfloat16)
    amplitude = jnp.einsum(
        "km,mij->kij", pick, gathered, preferred_element_type=jnp.float32
    ).astype(jnp.bfloat16)
    offsets = jnp.arange(width)
    cells = jnp.arange(tile)
    row_pick = (cells[None, None, :] == (tops[:, None, None] + offsets[None, :, None])).astype(
        jnp.bfloat16
    )
    col_pick = (cells[None, :, None] == (lefts[:, None, None] + offsets[None, None, :])).astype(
        jnp.bfloat16
    )
    field_low = field.astype(jnp.bfloat16)
    rows = jnp.einsum(
        "kir,crs->kcis", row_pick, field_low, preferred_element_type=jnp.float32
    ).astype(jnp.bfloat16)
    windows = jnp.einsum(
        "kcis,ksj->kcij", rows, col_pick, preferred_element_type=jnp.float32
    ).astype(jnp.bfloat16)
    tables = block_tables(cosine, sine)
    grads = fused_gradients(windows, amplitude, probe, propagator_phase, tables)
    spread = jnp.einsum(
        "kcij,ksj->kcis", grads, col_pick, preferred_element_type=jnp.float32
    ).astype(jnp.bfloat16)
    total = jnp.einsum("kir,kcis->crs", row_pick, spread, preferred_element_type=jnp.float32)
    updated = field - step_rate * total
    return smooth(updated)


def solution(mesh):
    placed = (
        P(None, "tx", "ty"),
        P(),
        P(),
        P("tx", "ty", None, None, None, None),
        P("tx", "ty", None, None),
        P("tx", "ty", None, None),
    )
    return jax.shard_map(
        per_device, mesh=mesh, in_specs=placed, out_specs=P(None, "tx", "ty"), check_vma=False
    )
```

```python
import math

import jax
import jax.numpy as jnp
from jax import lax
from jax.experimental import pallas as pl
from jax.experimental.pallas import tpu as pltpu
from jax.sharding import PartitionSpec as P

step_rate = 0.5
smooth_rate = 0.2


def dft_tables(width):
    index = jnp.arange(width)
    product = index[:, None] * index[None, :] % width
    angles = product.astype(jnp.float32) * (2.0 * math.pi / width)
    scale = 1.0 / math.sqrt(width)
    return (jnp.cos(angles) * scale, jnp.sin(angles) * scale)


def slot_table(owner):
    order = jnp.arange(owner.shape[0])
    same = owner[:, None] == owner[None, :]
    earlier = order[None, :] < order[:, None]
    return jnp.sum(jnp.where(same & earlier, 1, 0), axis=1).astype(jnp.int32)


def shifted_neighbours(updated):
    rows_axis = "tx"
    cols_axis = "ty"
    n_rows = lax.axis_size(rows_axis)
    n_cols = lax.axis_size(cols_axis)
    up_rows = [(i, i + 1) for i in range(n_rows - 1)]
    down_rows = [(i + 1, i) for i in range(n_rows - 1)]
    up_cols = [(i, i + 1) for i in range(n_cols - 1)]
    down_cols = [(i + 1, i) for i in range(n_cols - 1)]
    above = lax.ppermute(updated[:, -1, :], rows_axis, up_rows)
    below = lax.ppermute(updated[:, 0, :], rows_axis, down_rows)
    left = lax.ppermute(updated[:, :, -1], cols_axis, up_cols)
    right = lax.ppermute(updated[:, :, 0], cols_axis, down_cols)
    north = jnp.concatenate([above[:, None, :], updated[:, :-1, :]], axis=1)
    south = jnp.concatenate([updated[:, 1:, :], below[:, None, :]], axis=1)
    west = jnp.concatenate([left[:, :, None], updated[:, :, :-1]], axis=2)
    east = jnp.concatenate([updated[:, :, 1:], right[:, :, None]], axis=2)
    return south, north, east, west


def smooth(center):
    slices = center.shape[0] // 2
    total = jnp.zeros_like(center)
    for view in shifted_neighbours(center):
        pairs = (view - center).reshape((slices, 2) + center.shape[1:])
        weight = 1.0 / jnp.sqrt(1.0 + pairs[:, 0] * pairs[:, 0] + pairs[:, 1] * pairs[:, 1])
        total = total + (pairs * weight[:, None]).reshape(center.shape)
    return center + smooth_rate * total


def block_tables(cosine, sine):
    plus = jnp.block([[cosine, -sine], [sine, cosine]])
    minus = jnp.block([[cosine, sine], [-sine, cosine]])
    lefts, rights = [], []
    for table in (plus, minus):
        high = lax.reduce_precision(table, exponent_bits=8, mantissa_bits=7)
        low = (table - high).astype(jnp.bfloat16)
        high = high.astype(jnp.bfloat16)
        lefts.append(jnp.concatenate([high, low, high], axis=1))
        rights.append(jnp.concatenate([high, low, high], axis=0))
    return jnp.stack(lefts), jnp.stack(rights)


def _split(x):
    high = x.astype(jnp.bfloat16)
    low = (x - high.astype(jnp.float32)).astype(jnp.bfloat16)
    return high, low


def _dot(a, b):
    return jnp.dot(a, b, preferred_element_type=jnp.float32)


def _times(a, b):
    return (a[0] * b[0] - a[1] * b[1], a[0] * b[1] + a[1] * b[0])


def _conj_times(a, b):
    return (a[0] * b[0] + a[1] * b[1], a[0] * b[1] - a[1] * b[0])


def _transformer(left_ref, right_ref, group, width):
    def transform(pair, sign):
        first, second = (1, 0) if sign < 0 else (0, 1)
        stacked = jnp.concatenate(
            [jnp.concatenate([pair[0][g], pair[1][g]], axis=0) for g in range(group)], axis=1
        )
        high, low = _split(stacked)
        rows = _dot(left_ref[first], jnp.concatenate([high, high, low], axis=0))
        joined = jnp.concatenate(
            [
                jnp.concatenate(
                    [rows[:width, g * width:(g + 1) * width], rows[width:, g * width:(g + 1) * width]],
                    axis=1,
                )
                for g in range(group)
            ],
            axis=0,
        )
        high, low = _split(joined)
        out = _dot(jnp.concatenate([high, high, low], axis=1), right_ref[second])
        return (
            out[:, :width].reshape(group, width, width),
            out[:, width:].reshape(group, width, width),
        )

    return transform


def _layers(win_ref):
    slices = win_ref.shape[1] // 2
    return [
        (win_ref[:, 2 * s].astype(jnp.float32), win_ref[:, 2 * s + 1].astype(jnp.float32))
        for s in range(slices)
    ]


def _forward_kernel(win_ref, probe_ref, prop_ref, left_ref, right_ref, far_ref, inc_ref):
    group, width = win_ref.shape[0], probe_ref.shape[-1]
    transform = _transformer(left_ref, right_ref, group, width)
    layers = _layers(win_ref)
    probe = (probe_ref[0][None], probe_ref[1][None])
    kernel = (prop_ref[0][None], prop_ref[1][None])
    wave = _times(probe, layers[0])
    for s in range(1, len(layers)):
        moved = transform(_times(kernel, transform(wave, -1)), 1)
        inc_ref[:, 2 * (s - 1)] = moved[0]
        inc_ref[:, 2 * (s - 1) + 1] = moved[1]
        wave = _times(layers[s], moved)
    far = transform(wave, -1)
    far_ref[:, 0] = far[0]
    far_ref[:, 1] = far[1]


def _backward_kernel(
    target_ref, amp_ref, far_ref, inc_ref, win_ref, probe_ref, prop_ref, left_ref, right_ref, out_ref
):
    group, width = win_ref.shape[0], probe_ref.shape[-1]
    step = pl.program_id(0)
    transform = _transformer(left_ref, right_ref, group, width)
    layers = _layers(win_ref)
    slices = len(layers)
    probe = (probe_ref[0][None], probe_ref[1][None])
    kernel_conj = (prop_ref[0][None], -prop_ref[1][None])
    amplitude = jnp.stack(
        [amp_ref[target_ref[step * group + g]].astype(jnp.float32) for g in range(group)]
    )
    far = (far_ref[:, 0], far_ref[:, 1])
    magnitude = jnp.sqrt(far[0] * far[0] + far[1] * far[1] + 1.0)
    factor = 1.0 - amplitude / magnitude
    back = transform((far[0] * factor, far[1] * factor), 1)
    grads = [None] * slices
    for s in range(slices - 1, 0, -1):
        grads[s] = _conj_times((inc_ref[:, 2 * (s - 1)], inc_ref[:, 2 * (s - 1) + 1]), back)
        back = transform(_times(kernel_conj, transform(_conj_times(layers[s], back), -1)), 1)
    grads[0] = _conj_times(probe, back)
    for s in range(slices):
        out_ref[:, 2 * s] = grads[s][0].astype(out_ref.dtype)
        out_ref[:, 2 * s + 1] = grads[s][1].astype(out_ref.dtype)


def forward_waves(windows, probe, kernel, tables, group=8):
    count, channels, width, _ = windows.shape
    group = math.gcd(count, group)
    left_tables, right_tables = tables
    fixed = lambda k: (0, 0, 0)
    return pl.pallas_call(
        _forward_kernel,
        grid=(count // group,),
        in_specs=[
            pl.BlockSpec((group, channels, width, width), lambda k: (k, 0, 0, 0)),
            pl.BlockSpec((2, width, width), fixed),
            pl.BlockSpec((2, width, width), fixed),
            pl.BlockSpec(left_tables.shape, fixed),
            pl.BlockSpec(right_tables.shape, fixed),
        ],
        out_specs=[
            pl.BlockSpec((group, 2, width, width), lambda k: (k, 0, 0, 0)),
            pl.BlockSpec((group, channels - 2, width, width), lambda k: (k, 0, 0, 0)),
        ],
        out_shape=[
            jax.ShapeDtypeStruct((count, 2, width, width), jnp.float32),
            jax.ShapeDtypeStruct((count, channels - 2, width, width), jnp.float32),
        ],
    )(windows, probe, kernel, left_tables, right_tables)


def backward_gradients(target, amplitudes, far, incoming, windows, probe, kernel, tables, group=8):
    count, channels, width, _ = windows.shape
    group = math.gcd(count, group)
    left_tables, right_tables = tables
    fixed = lambda k, t: (0, 0, 0)
    batch = lambda k, t: (k, 0, 0, 0)
    grid_spec = pltpu.PrefetchScalarGridSpec(
        num_scalar_prefetch=1,
        grid=(count // group,),
        in_specs=[
            pl.BlockSpec(amplitudes.shape, fixed),
            pl.BlockSpec((group, 2, width, width), batch),
            pl.BlockSpec((group, channels - 2, width, width), batch),
            pl.BlockSpec((group, channels, width, width), batch),
            pl.BlockSpec((2, width, width), fixed),
            pl.BlockSpec((2, width, width), fixed),
            pl.BlockSpec(left_tables.shape, fixed),
            pl.BlockSpec(right_tables.shape, fixed),
        ],
        out_specs=pl.BlockSpec((group, channels, width, width), batch),
    )
    return pl.pallas_call(
        _backward_kernel,
        grid_spec=grid_spec,
        out_shape=jax.ShapeDtypeStruct((count, channels, width, width), jnp.bfloat16),
    )(target, amplitudes, far, incoming, windows, probe, kernel, left_tables, right_tables)


def per_device(object_init, probe, propagator_phase, measured, corners, owner_column):
    width = probe.shape[-1]
    cosine, sine = dft_tables(width)
    field = object_init
    tile = field.shape[1]
    capacity = measured.shape[3]
    columns = lax.axis_size("ty")
    tops = corners[0, 0, :, 0]
    lefts = corners[0, 0, :, 1]
    owner = owner_column[0, 0, :, 0]
    slot = slot_table(owner)
    target = jnp.clip(owner * capacity + slot, 0, columns * capacity - 1)
    gathered = lax.all_to_all(measured[0, 0], "ty", split_axis=0, concat_axis=0, tiled=True)
    gathered = gathered.reshape(columns * capacity, width, width)
    offsets = jnp.arange(width)
    cells = jnp.arange(tile)
    row_pick = (cells[None, None, :] == (tops[:, None, None] + offsets[None, :, None])).astype(
        jnp.bfloat16
    )
    col_pick = (cells[None, :, None] == (lefts[:, None, None] + offsets[None, None, :])).astype(
        jnp.bfloat16
    )
    field_low = field.astype(jnp.bfloat16)
    rows = jnp.einsum(
        "kir,crs->kcis", row_pick, field_low, preferred_element_type=jnp.float32
    ).astype(jnp.bfloat16)
    windows = jnp.einsum(
        "kcis,ksj->kcij", rows, col_pick, preferred_element_type=jnp.float32
    ).astype(jnp.bfloat16)
    tables = block_tables(cosine, sine)
    kernel = jnp.stack([jnp.cos(propagator_phase), jnp.sin(propagator_phase)])
    far, incoming = forward_waves(windows, probe, kernel, tables)
    grads = backward_gradients(target, gathered, far, incoming, windows, probe, kernel, tables)
    placed_rows = jnp.einsum(
        "kir,kcij->kcrj", row_pick, grads, preferred_element_type=jnp.float32
    ).astype(jnp.bfloat16)
    total = jnp.einsum("kcrj,ksj->crs", placed_rows, col_pick, preferred_element_type=jnp.float32)
    updated = field - step_rate * total
    return smooth(updated)


def solution(mesh):
    placed = (
        P(None, "tx", "ty"),
        P(),
        P(),
        P("tx", "ty", None, None, None, None),
        P("tx", "ty", None, None),
        P("tx", "ty", None, None),
    )
    return jax.shard_map(
        per_device, mesh=mesh, in_specs=placed, out_specs=P(None, "tx", "ty"), check_vma=False
    )
```

```python
import math

import jax
import numpy as np
import jax.numpy as jnp
from jax import lax
from jax.experimental import pallas as pl
from jax.experimental.pallas import tpu as pltpu
from jax.sharding import PartitionSpec as P

step_rate = 0.5
smooth_rate = 0.2


def slot_table(owner):
    order = jnp.arange(owner.shape[0])
    same = owner[:, None] == owner[None, :]
    earlier = order[None, :] < order[:, None]
    return jnp.sum(jnp.where(same & earlier, 1, 0), axis=1).astype(jnp.int32)


def _bent(diff):
    slices = diff.shape[0] // 2
    pairs = diff.reshape((slices, 2) + diff.shape[1:])
    weight = 1.0 / jnp.sqrt(1.0 + pairs[:, 0] * pairs[:, 0] + pairs[:, 1] * pairs[:, 1])
    return (pairs * weight[:, None]).reshape(diff.shape)


def exchange_edges(top, bottom, first, last):
    n_rows = lax.axis_size("tx")
    n_cols = lax.axis_size("ty")
    up_rows = [(i, i + 1) for i in range(n_rows - 1)]
    down_rows = [(i + 1, i) for i in range(n_rows - 1)]
    up_cols = [(i, i + 1) for i in range(n_cols - 1)]
    down_cols = [(i + 1, i) for i in range(n_cols - 1)]
    above = lax.ppermute(bottom, "tx", up_rows)
    below = lax.ppermute(top, "tx", down_rows)
    left = lax.ppermute(last, "ty", up_cols)
    right = lax.ppermute(first, "ty", down_cols)
    return above, below, left, right


def smooth(center, halos):
    above, below, left, right = halos
    zero = ((0, 0), (0, 0), (0, 0))
    rows_pad = lambda lo, hi: ((0, 0), (lo, hi), (0, 0))
    cols_pad = lambda lo, hi: ((0, 0), (0, 0), (lo, hi))
    south = jnp.pad(center[:, 1:] - center[:, :-1], rows_pad(0, 1))
    north = jnp.pad(center[:, :-1] - center[:, 1:], rows_pad(1, 0))
    east = jnp.pad(center[:, :, 1:] - center[:, :, :-1], cols_pad(0, 1))
    west = jnp.pad(center[:, :, :-1] - center[:, :, 1:], cols_pad(1, 0))
    inner = _bent(south) + _bent(north) + _bent(east) + _bent(west)
    size = center.shape[1] - 1
    edge_north = _bent(above - center[:, 0, :])[:, None, :]
    edge_south = _bent(below - center[:, -1, :])[:, None, :]
    edge_west = _bent(left - center[:, :, 0])[:, :, None]
    edge_east = _bent(right - center[:, :, -1])[:, :, None]
    edges = (
        jnp.pad(edge_north, rows_pad(0, size))
        + jnp.pad(edge_south, rows_pad(size, 0))
        + jnp.pad(edge_west, cols_pad(0, size))
        + jnp.pad(edge_east, cols_pad(size, 0))
    )
    return center + smooth_rate * (inner + edges)


def block_tables(width):
    index = np.arange(width)
    angles = (index[:, None] * index[None, :] % width) * (2.0 * math.pi / width)
    scale = 1.0 / math.sqrt(width)
    cosine, sine = np.cos(angles) * scale, np.sin(angles) * scale
    plus = np.block([[cosine, -sine], [sine, cosine]])
    minus = np.block([[cosine, sine], [-sine, cosine]])
    lefts, rights = [], []
    for table in (plus, minus):
        high = table.astype(jnp.bfloat16)
        low = (table - high.astype(np.float64)).astype(jnp.bfloat16)
        lefts.append(np.concatenate([high, low, high], axis=1))
        rights.append(np.concatenate([high, low, high], axis=0))
    return jnp.asarray(np.stack(lefts)), jnp.asarray(np.stack(rights))


def _split(x):
    high = x.astype(jnp.bfloat16)
    low = (x - high.astype(jnp.float32)).astype(jnp.bfloat16)
    return high, low


def _dot(a, b):
    return jnp.dot(a, b, preferred_element_type=jnp.float32)


def _times(a, b):
    return (a[0] * b[0] - a[1] * b[1], a[0] * b[1] + a[1] * b[0])


def _conj_times(a, b):
    return (a[0] * b[0] + a[1] * b[1], a[0] * b[1] - a[1] * b[0])


def _transformer(left_ref, right_ref, group, width):
    def transform(pair, sign):
        first, second = (1, 0) if sign < 0 else (0, 1)
        stacked = jnp.concatenate(
            [jnp.concatenate([pair[0][g], pair[1][g]], axis=0) for g in range(group)], axis=1
        )
        high, low = _split(stacked)
        rows = _dot(left_ref[first], jnp.concatenate([high, high, low], axis=0))
        joined = jnp.concatenate(
            [
                jnp.concatenate(
                    [rows[:width, g * width:(g + 1) * width], rows[width:, g * width:(g + 1) * width]],
                    axis=1,
                )
                for g in range(group)
            ],
            axis=0,
        )
        high, low = _split(joined)
        out = _dot(jnp.concatenate([high, high, low], axis=1), right_ref[second])
        return (
            out[:, :width].reshape(group, width, width),
            out[:, width:].reshape(group, width, width),
        )

    return transform


def _layers(win_ref):
    slices = win_ref.shape[1] // 2
    return [
        (win_ref[:, 2 * s].astype(jnp.float32), win_ref[:, 2 * s + 1].astype(jnp.float32))
        for s in range(slices)
    ]


def _forward_kernel(win_ref, probe_ref, prop_ref, left_ref, right_ref, far_ref, inc_ref):
    group, width = win_ref.shape[0], probe_ref.shape[-1]
    transform = _transformer(left_ref, right_ref, group, width)
    layers = _layers(win_ref)
    probe = (probe_ref[0][None], probe_ref[1][None])
    kernel = (prop_ref[0][None], prop_ref[1][None])
    wave = _times(probe, layers[0])
    for s in range(1, len(layers)):
        moved = transform(_times(kernel, transform(wave, -1)), 1)
        inc_ref[:, 2 * (s - 1)] = moved[0]
        inc_ref[:, 2 * (s - 1) + 1] = moved[1]
        wave = _times(layers[s], moved)
    far = transform(wave, -1)
    far_ref[:, 0] = far[0]
    far_ref[:, 1] = far[1]


def _backward_kernel(
    target_ref, amp_ref, far_ref, inc_ref, win_ref, probe_ref, prop_ref, left_ref, right_ref, out_ref
):
    group, width = win_ref.shape[0], probe_ref.shape[-1]
    step = pl.program_id(0)
    transform = _transformer(left_ref, right_ref, group, width)
    layers = _layers(win_ref)
    slices = len(layers)
    probe = (probe_ref[0][None], probe_ref[1][None])
    kernel_conj = (prop_ref[0][None], -prop_ref[1][None])
    amplitude = jnp.stack(
        [amp_ref[target_ref[step * group + g]].astype(jnp.float32) for g in range(group)]
    )
    far = (far_ref[:, 0], far_ref[:, 1])
    magnitude = jnp.sqrt(far[0] * far[0] + far[1] * far[1] + 1.0)
    factor = 1.0 - amplitude / magnitude
    back = transform((far[0] * factor, far[1] * factor), 1)
    grads = [None] * slices
    for s in range(slices - 1, 0, -1):
        grads[s] = _conj_times((inc_ref[:, 2 * (s - 1)], inc_ref[:, 2 * (s - 1) + 1]), back)
        back = transform(_times(kernel_conj, transform(_conj_times(layers[s], back), -1)), 1)
    grads[0] = _conj_times(probe, back)
    for s in range(slices):
        out_ref[:, 2 * s] = grads[s][0].astype(out_ref.dtype)
        out_ref[:, 2 * s + 1] = grads[s][1].astype(out_ref.dtype)


def forward_waves(windows, probe, kernel, tables, group=8):
    count, channels, width, _ = windows.shape
    group = math.gcd(count, group)
    left_tables, right_tables = tables
    fixed = lambda k: (0, 0, 0)
    return pl.pallas_call(
        _forward_kernel,
        grid=(count // group,),
        in_specs=[
            pl.BlockSpec((group, channels, width, width), lambda k: (k, 0, 0, 0)),
            pl.BlockSpec((2, width, width), fixed),
            pl.BlockSpec((2, width, width), fixed),
            pl.BlockSpec(left_tables.shape, fixed),
            pl.BlockSpec(right_tables.shape, fixed),
        ],
        out_specs=[
            pl.BlockSpec((group, 2, width, width), lambda k: (k, 0, 0, 0)),
            pl.BlockSpec((group, channels - 2, width, width), lambda k: (k, 0, 0, 0)),
        ],
        out_shape=[
            jax.ShapeDtypeStruct((count, 2, width, width), jnp.float32),
            jax.ShapeDtypeStruct((count, channels - 2, width, width), jnp.float32),
        ],
    )(windows, probe, kernel, left_tables, right_tables)


def backward_gradients(target, amplitudes, far, incoming, windows, probe, kernel, tables, group=8):
    count, channels, width, _ = windows.shape
    group = math.gcd(count, group)
    left_tables, right_tables = tables
    fixed = lambda k, t: (0, 0, 0)
    batch = lambda k, t: (k, 0, 0, 0)
    grid_spec = pltpu.PrefetchScalarGridSpec(
        num_scalar_prefetch=1,
        grid=(count // group,),
        in_specs=[
            pl.BlockSpec(amplitudes.shape, fixed),
            pl.BlockSpec((group, 2, width, width), batch),
            pl.BlockSpec((group, channels - 2, width, width), batch),
            pl.BlockSpec((group, channels, width, width), batch),
            pl.BlockSpec((2, width, width), fixed),
            pl.BlockSpec((2, width, width), fixed),
            pl.BlockSpec(left_tables.shape, fixed),
            pl.BlockSpec(right_tables.shape, fixed),
        ],
        out_specs=pl.BlockSpec((group, channels, width, width), batch),
    )
    return pl.pallas_call(
        _backward_kernel,
        grid_spec=grid_spec,
        out_shape=jax.ShapeDtypeStruct((count, channels, width, width), jnp.bfloat16),
    )(target, amplitudes, far, incoming, windows, probe, kernel, left_tables, right_tables)


def per_device(object_init, probe, propagator_phase, measured, corners, owner_column):
    width = probe.shape[-1]
    field = object_init
    tile = field.shape[1]
    capacity = measured.shape[3]
    columns = lax.axis_size("ty")
    tops = corners[0, 0, :, 0]
    lefts = corners[0, 0, :, 1]
    owner = owner_column[0, 0, :, 0]
    slot = slot_table(owner)
    target = jnp.clip(owner * capacity + slot, 0, columns * capacity - 1)
    gathered = lax.all_to_all(measured[0, 0], "ty", split_axis=0, concat_axis=0, tiled=True)
    gathered = gathered.reshape(columns * capacity, width, width)
    offsets = jnp.arange(width)
    cells = jnp.arange(tile)
    row_pick = (cells[None, None, :] == (tops[:, None, None] + offsets[None, :, None])).astype(
        jnp.bfloat16
    )
    col_pick = (cells[None, :, None] == (lefts[:, None, None] + offsets[None, None, :])).astype(
        jnp.bfloat16
    )
    field_low = field.astype(jnp.bfloat16)
    rows = jnp.einsum(
        "kir,crs->kcis", row_pick, field_low, preferred_element_type=jnp.float32
    ).astype(jnp.bfloat16)
    windows = jnp.einsum(
        "kcis,ksj->kcij", rows, col_pick, preferred_element_type=jnp.float32
    ).astype(jnp.bfloat16)
    tables = block_tables(width)
    kernel = jnp.stack([jnp.cos(propagator_phase), jnp.sin(propagator_phase)])
    far, incoming = forward_waves(windows, probe, kernel, tables)
    grads = backward_gradients(target, gathered, far, incoming, windows, probe, kernel, tables)
    ends = jnp.stack([row_pick[:, :, 0], row_pick[:, :, -1]], axis=-1)
    edge_rows = jnp.einsum(
        "kie,kcij->kcej", ends, grads, preferred_element_type=jnp.float32
    ).astype(jnp.bfloat16)
    total_rows = jnp.einsum("kcej,ksj->ces", edge_rows, col_pick, preferred_element_type=jnp.float32)
    sides = jnp.stack([col_pick[:, 0, :], col_pick[:, -1, :]], axis=1)
    edge_cols = jnp.einsum(
        "kcij,kej->kcie", grads, sides, preferred_element_type=jnp.float32
    ).astype(jnp.bfloat16)
    total_cols = jnp.einsum("kir,kcie->cer", row_pick, edge_cols, preferred_element_type=jnp.float32)
    halos = exchange_edges(
        field[:, 0, :] - step_rate * total_rows[:, 0],
        field[:, -1, :] - step_rate * total_rows[:, 1],
        field[:, :, 0] - step_rate * total_cols[:, 0],
        field[:, :, -1] - step_rate * total_cols[:, 1],
    )
    placed_rows = jnp.einsum(
        "kir,kcij->kcrj", row_pick, grads, preferred_element_type=jnp.float32
    ).astype(jnp.bfloat16)
    total = jnp.einsum("kcrj,ksj->crs", placed_rows, col_pick, preferred_element_type=jnp.float32)
    updated = field - step_rate * total
    return smooth(updated, halos)


def solution(mesh):
    placed = (
        P(None, "tx", "ty"),
        P(),
        P(),
        P("tx", "ty", None, None, None, None),
        P("tx", "ty", None, None),
        P("tx", "ty", None, None),
    )
    return jax.shard_map(
        per_device, mesh=mesh, in_specs=placed, out_specs=P(None, "tx", "ty"), check_vma=False
    )
```

```python
import math

import jax
import numpy as np
import jax.numpy as jnp
from jax import lax
from jax.experimental import pallas as pl
from jax.experimental.pallas import tpu as pltpu
from jax.sharding import PartitionSpec as P

step_rate = 0.5
smooth_rate = 0.2


def slot_table(owner):
    order = jnp.arange(owner.shape[0])
    same = owner[:, None] == owner[None, :]
    earlier = order[None, :] < order[:, None]
    return jnp.sum(jnp.where(same & earlier, 1, 0), axis=1).astype(jnp.int32)


def exchange_edges(top, bottom, first, last):
    n_rows = lax.axis_size("tx")
    n_cols = lax.axis_size("ty")
    up_rows = [(i, i + 1) for i in range(n_rows - 1)]
    down_rows = [(i + 1, i) for i in range(n_rows - 1)]
    up_cols = [(i, i + 1) for i in range(n_cols - 1)]
    down_cols = [(i + 1, i) for i in range(n_cols - 1)]
    above = lax.ppermute(bottom, "tx", up_rows)
    below = lax.ppermute(top, "tx", down_rows)
    left = lax.ppermute(last, "ty", up_cols)
    right = lax.ppermute(first, "ty", down_cols)
    return above, below, left, right


def _smooth_kernel(field_ref, total_ref, above_ref, below_ref, left_ref, right_ref, out_ref):
    size = field_ref.shape[-1]
    rows = lax.broadcasted_iota(jnp.int32, (size, size), 0)
    cols = lax.broadcasted_iota(jnp.int32, (size, size), 1)

    def as_column(line):
        return jnp.sum(jnp.where(rows == cols, line, 0.0), axis=1, keepdims=True)

    centers, views = [], []
    for part in range(2):
        v = field_ref[part] - step_rate * total_ref[part]
        above = above_ref[0, part:part + 1, :]
        below = below_ref[0, part:part + 1, :]
        left = as_column(left_ref[0, part:part + 1, :])
        right = as_column(right_ref[0, part:part + 1, :])
        south = jnp.where(rows == size - 1, below, pltpu.roll(v, size - 1, 0))
        north = jnp.where(rows == 0, above, pltpu.roll(v, 1, 0))
        east = jnp.where(cols == size - 1, right, pltpu.roll(v, size - 1, 1))
        west = jnp.where(cols == 0, left, pltpu.roll(v, 1, 1))
        centers.append(v)
        views.append((south, north, east, west))
    total_r = jnp.zeros_like(centers[0])
    total_i = jnp.zeros_like(centers[1])
    for n in range(4):
        dr = views[0][n] - centers[0]
        di = views[1][n] - centers[1]
        weight = 1.0 / jnp.sqrt(1.0 + dr * dr + di * di)
        total_r = total_r + dr * weight
        total_i = total_i + di * weight
    out_ref[0] = centers[0] + smooth_rate * total_r
    out_ref[1] = centers[1] + smooth_rate * total_i


def smooth_update(field, total, above, below, left, right):
    channels, size, _ = field.shape
    slices = channels // 2
    plane = pl.BlockSpec((2, size, size), lambda s: (s, 0, 0))
    edge = pl.BlockSpec((1, 2, size), lambda s: (s, 0, 0))
    shaped = [x.reshape(slices, 2, size) for x in (above, below, left, right)]
    return pl.pallas_call(
        _smooth_kernel,
        grid=(slices,),
        in_specs=[plane, plane, edge, edge, edge, edge],
        out_specs=plane,
        out_shape=jax.ShapeDtypeStruct(field.shape, jnp.float32),
    )(field, total, *shaped)


def block_tables(width):
    index = np.arange(width)
    angles = (index[:, None] * index[None, :] % width) * (2.0 * math.pi / width)
    scale = 1.0 / math.sqrt(width)
    cosine, sine = np.cos(angles) * scale, np.sin(angles) * scale
    plus = np.block([[cosine, -sine], [sine, cosine]])
    minus = np.block([[cosine, sine], [-sine, cosine]])
    lefts, rights = [], []
    for table in (plus, minus):
        high = table.astype(jnp.bfloat16)
        low = (table - high.astype(np.float64)).astype(jnp.bfloat16)
        lefts.append(np.concatenate([high, low, high], axis=1))
        rights.append(np.concatenate([high, low, high], axis=0))
    return jnp.asarray(np.stack(lefts)), jnp.asarray(np.stack(rights))


def _split(x):
    high = x.astype(jnp.bfloat16)
    low = (x - high.astype(jnp.float32)).astype(jnp.bfloat16)
    return high, low


def _dot(a, b):
    return jnp.dot(a, b, preferred_element_type=jnp.float32)


def _times(a, b):
    return (a[0] * b[0] - a[1] * b[1], a[0] * b[1] + a[1] * b[0])


def _conj_times(a, b):
    return (a[0] * b[0] + a[1] * b[1], a[0] * b[1] - a[1] * b[0])


def _transformer(left_ref, right_ref, group, width):
    def transform(pair, sign):
        first, second = (1, 0) if sign < 0 else (0, 1)
        stacked = jnp.concatenate(
            [jnp.concatenate([pair[0][g], pair[1][g]], axis=0) for g in range(group)], axis=1
        )
        high, low = _split(stacked)
        rows = _dot(left_ref[first], jnp.concatenate([high, high, low], axis=0))
        joined = jnp.concatenate(
            [
                jnp.concatenate(
                    [rows[:width, g * width:(g + 1) * width], rows[width:, g * width:(g + 1) * width]],
                    axis=1,
                )
                for g in range(group)
            ],
            axis=0,
        )
        high, low = _split(joined)
        out = _dot(jnp.concatenate([high, high, low], axis=1), right_ref[second])
        return (
            out[:, :width].reshape(group, width, width),
            out[:, width:].reshape(group, width, width),
        )

    return transform


def _layers(win_ref):
    slices = win_ref.shape[1] // 2
    return [
        (win_ref[:, 2 * s].astype(jnp.float32), win_ref[:, 2 * s + 1].astype(jnp.float32))
        for s in range(slices)
    ]


def _forward_kernel(win_ref, probe_ref, prop_ref, left_ref, right_ref, far_ref, inc_ref):
    group, width = win_ref.shape[0], probe_ref.shape[-1]
    transform = _transformer(left_ref, right_ref, group, width)
    layers = _layers(win_ref)
    probe = (probe_ref[0][None], probe_ref[1][None])
    kernel = (prop_ref[0][None], prop_ref[1][None])
    wave = _times(probe, layers[0])
    for s in range(1, len(layers)):
        moved = transform(_times(kernel, transform(wave, -1)), 1)
        inc_ref[:, 2 * (s - 1)] = moved[0]
        inc_ref[:, 2 * (s - 1) + 1] = moved[1]
        wave = _times(layers[s], moved)
    far = transform(wave, -1)
    far_ref[:, 0] = far[0]
    far_ref[:, 1] = far[1]


def _backward_kernel(
    target_ref, amp_ref, far_ref, inc_ref, win_ref, probe_ref, prop_ref, left_ref, right_ref, out_ref
):
    group, width = win_ref.shape[0], probe_ref.shape[-1]
    step = pl.program_id(0)
    transform = _transformer(left_ref, right_ref, group, width)
    layers = _layers(win_ref)
    slices = len(layers)
    probe = (probe_ref[0][None], probe_ref[1][None])
    kernel_conj = (prop_ref[0][None], -prop_ref[1][None])
    amplitude = jnp.stack(
        [amp_ref[target_ref[step * group + g]].astype(jnp.float32) for g in range(group)]
    )
    far = (far_ref[:, 0], far_ref[:, 1])
    magnitude = jnp.sqrt(far[0] * far[0] + far[1] * far[1] + 1.0)
    factor = 1.0 - amplitude / magnitude
    back = transform((far[0] * factor, far[1] * factor), 1)
    grads = [None] * slices
    for s in range(slices - 1, 0, -1):
        grads[s] = _conj_times((inc_ref[:, 2 * (s - 1)], inc_ref[:, 2 * (s - 1) + 1]), back)
        back = transform(_times(kernel_conj, transform(_conj_times(layers[s], back), -1)), 1)
    grads[0] = _conj_times(probe, back)
    for s in range(slices):
        out_ref[:, 2 * s] = grads[s][0].astype(out_ref.dtype)
        out_ref[:, 2 * s + 1] = grads[s][1].astype(out_ref.dtype)


def forward_waves(windows, probe, kernel, tables, group=8):
    count, channels, width, _ = windows.shape
    group = math.gcd(count, group)
    left_tables, right_tables = tables
    fixed = lambda k: (0, 0, 0)
    return pl.pallas_call(
        _forward_kernel,
        grid=(count // group,),
        in_specs=[
            pl.BlockSpec((group, channels, width, width), lambda k: (k, 0, 0, 0)),
            pl.BlockSpec((2, width, width), fixed),
            pl.BlockSpec((2, width, width), fixed),
            pl.BlockSpec(left_tables.shape, fixed),
            pl.BlockSpec(right_tables.shape, fixed),
        ],
        out_specs=[
            pl.BlockSpec((group, 2, width, width), lambda k: (k, 0, 0, 0)),
            pl.BlockSpec((group, channels - 2, width, width), lambda k: (k, 0, 0, 0)),
        ],
        out_shape=[
            jax.ShapeDtypeStruct((count, 2, width, width), jnp.float32),
            jax.ShapeDtypeStruct((count, channels - 2, width, width), jnp.float32),
        ],
    )(windows, probe, kernel, left_tables, right_tables)


def backward_gradients(target, amplitudes, far, incoming, windows, probe, kernel, tables, group=8):
    count, channels, width, _ = windows.shape
    group = math.gcd(count, group)
    left_tables, right_tables = tables
    fixed = lambda k, t: (0, 0, 0)
    batch = lambda k, t: (k, 0, 0, 0)
    grid_spec = pltpu.PrefetchScalarGridSpec(
        num_scalar_prefetch=1,
        grid=(count // group,),
        in_specs=[
            pl.BlockSpec(amplitudes.shape, fixed),
            pl.BlockSpec((group, 2, width, width), batch),
            pl.BlockSpec((group, channels - 2, width, width), batch),
            pl.BlockSpec((group, channels, width, width), batch),
            pl.BlockSpec((2, width, width), fixed),
            pl.BlockSpec((2, width, width), fixed),
            pl.BlockSpec(left_tables.shape, fixed),
            pl.BlockSpec(right_tables.shape, fixed),
        ],
        out_specs=pl.BlockSpec((group, channels, width, width), batch),
    )
    return pl.pallas_call(
        _backward_kernel,
        grid_spec=grid_spec,
        out_shape=jax.ShapeDtypeStruct((count, channels, width, width), jnp.bfloat16),
    )(target, amplitudes, far, incoming, windows, probe, kernel, left_tables, right_tables)


def per_device(object_init, probe, propagator_phase, measured, corners, owner_column):
    width = probe.shape[-1]
    field = object_init
    tile = field.shape[1]
    capacity = measured.shape[3]
    columns = lax.axis_size("ty")
    tops = corners[0, 0, :, 0]
    lefts = corners[0, 0, :, 1]
    owner = owner_column[0, 0, :, 0]
    slot = slot_table(owner)
    target = jnp.clip(owner * capacity + slot, 0, columns * capacity - 1)
    gathered = lax.all_to_all(measured[0, 0], "ty", split_axis=0, concat_axis=0, tiled=True)
    gathered = gathered.reshape(columns * capacity, width, width)
    offsets = jnp.arange(width)
    cells = jnp.arange(tile)
    row_pick = (cells[None, None, :] == (tops[:, None, None] + offsets[None, :, None])).astype(
        jnp.bfloat16
    )
    col_pick = (cells[None, :, None] == (lefts[:, None, None] + offsets[None, None, :])).astype(
        jnp.bfloat16
    )
    field_low = field.astype(jnp.bfloat16)
    rows = jnp.einsum(
        "kir,crs->kcis", row_pick, field_low, preferred_element_type=jnp.float32
    ).astype(jnp.bfloat16)
    windows = jnp.einsum(
        "kcis,ksj->kcij", rows, col_pick, preferred_element_type=jnp.float32
    ).astype(jnp.bfloat16)
    tables = block_tables(width)
    kernel = jnp.stack([jnp.cos(propagator_phase), jnp.sin(propagator_phase)])
    far, incoming = forward_waves(windows, probe, kernel, tables)
    grads = backward_gradients(target, gathered, far, incoming, windows, probe, kernel, tables)
    placed_rows = jnp.einsum(
        "kir,kcij->kcrj", row_pick, grads, preferred_element_type=jnp.float32
    ).astype(jnp.bfloat16)
    total = jnp.einsum("kcrj,ksj->crs", placed_rows, col_pick, preferred_element_type=jnp.float32)
    halos = exchange_edges(
        field[:, 0, :] - step_rate * total[:, 0, :],
        field[:, -1, :] - step_rate * total[:, -1, :],
        field[:, :, 0] - step_rate * total[:, :, 0],
        field[:, :, -1] - step_rate * total[:, :, -1],
    )
    return smooth_update(field, total, *halos)


def solution(mesh):
    placed = (
        P(None, "tx", "ty"),
        P(),
        P(),
        P("tx", "ty", None, None, None, None),
        P("tx", "ty", None, None),
        P("tx", "ty", None, None),
    )
    return jax.shard_map(
        per_device, mesh=mesh, in_specs=placed, out_specs=P(None, "tx", "ty"), check_vma=False
    )
```

```python
import math

import jax
import numpy as np
import jax.numpy as jnp
from jax import lax
from jax.experimental import pallas as pl
from jax.experimental.pallas import tpu as pltpu
from jax.sharding import PartitionSpec as P

step_rate = 0.5
smooth_rate = 0.2


def slot_table(owner):
    order = jnp.arange(owner.shape[0])
    same = owner[:, None] == owner[None, :]
    earlier = order[None, :] < order[:, None]
    return jnp.sum(jnp.where(same & earlier, 1, 0), axis=1).astype(jnp.int32)


def exchange_edges(top, bottom, first, last):
    n_rows = lax.axis_size("tx")
    n_cols = lax.axis_size("ty")
    up_rows = [(i, i + 1) for i in range(n_rows - 1)]
    down_rows = [(i + 1, i) for i in range(n_rows - 1)]
    up_cols = [(i, i + 1) for i in range(n_cols - 1)]
    down_cols = [(i + 1, i) for i in range(n_cols - 1)]
    above = lax.ppermute(bottom, "tx", up_rows)
    below = lax.ppermute(top, "tx", down_rows)
    left = lax.ppermute(last, "ty", up_cols)
    right = lax.ppermute(first, "ty", down_cols)
    return above, below, left, right


def _smooth_kernel(field_ref, total_ref, above_ref, below_ref, left_ref, right_ref, out_ref):
    size = field_ref.shape[-1]
    rows = lax.broadcasted_iota(jnp.int32, (size, size), 0)
    cols = lax.broadcasted_iota(jnp.int32, (size, size), 1)

    def as_column(line):
        return jnp.sum(jnp.where(rows == cols, line, 0.0), axis=1, keepdims=True)

    centers, views = [], []
    for part in range(2):
        v = field_ref[part] - step_rate * total_ref[part]
        channel = 2 * pl.program_id(0) + part
        above = above_ref[pl.ds(channel, 1), :]
        below = below_ref[pl.ds(channel, 1), :]
        left = as_column(left_ref[pl.ds(channel, 1), :])
        right = as_column(right_ref[pl.ds(channel, 1), :])
        south = jnp.where(rows == size - 1, below, pltpu.roll(v, size - 1, 0))
        north = jnp.where(rows == 0, above, pltpu.roll(v, 1, 0))
        east = jnp.where(cols == size - 1, right, pltpu.roll(v, size - 1, 1))
        west = jnp.where(cols == 0, left, pltpu.roll(v, 1, 1))
        centers.append(v)
        views.append((south, north, east, west))
    total_r = jnp.zeros_like(centers[0])
    total_i = jnp.zeros_like(centers[1])
    for n in range(4):
        dr = views[0][n] - centers[0]
        di = views[1][n] - centers[1]
        weight = 1.0 / jnp.sqrt(1.0 + dr * dr + di * di)
        total_r = total_r + dr * weight
        total_i = total_i + di * weight
    out_ref[0] = centers[0] + smooth_rate * total_r
    out_ref[1] = centers[1] + smooth_rate * total_i


def smooth_update(field, total, above, below, left, right):
    channels, size, _ = field.shape
    slices = channels // 2
    plane = pl.BlockSpec((2, size, size), lambda s: (s, 0, 0))
    edge = pl.BlockSpec((channels, size), lambda s: (0, 0))
    return pl.pallas_call(
        _smooth_kernel,
        grid=(slices,),
        in_specs=[plane, plane, edge, edge, edge, edge],
        out_specs=plane,
        out_shape=jax.ShapeDtypeStruct(field.shape, jnp.float32),
    )(field, total, above, below, left, right)


def block_tables(width):
    index = np.arange(width)
    angles = (index[:, None] * index[None, :] % width) * (2.0 * math.pi / width)
    scale = 1.0 / math.sqrt(width)
    cosine, sine = np.cos(angles) * scale, np.sin(angles) * scale
    plus = np.block([[cosine, -sine], [sine, cosine]])
    minus = np.block([[cosine, sine], [-sine, cosine]])
    lefts, rights = [], []
    for table in (plus, minus):
        high = table.astype(jnp.bfloat16)
        low = (table - high.astype(np.float64)).astype(jnp.bfloat16)
        lefts.append(np.concatenate([high, low, high], axis=1))
        rights.append(np.concatenate([high, low, high], axis=0))
    return jnp.asarray(np.stack(lefts)), jnp.asarray(np.stack(rights))


def _split(x):
    high = x.astype(jnp.bfloat16)
    low = (x - high.astype(jnp.float32)).astype(jnp.bfloat16)
    return high, low


def _dot(a, b):
    return jnp.dot(a, b, preferred_element_type=jnp.float32)


def _times(a, b):
    return (a[0] * b[0] - a[1] * b[1], a[0] * b[1] + a[1] * b[0])


def _conj_times(a, b):
    return (a[0] * b[0] + a[1] * b[1], a[0] * b[1] - a[1] * b[0])


def _transformer(left_ref, right_ref, group, width):
    def transform(pair, sign):
        first, second = (1, 0) if sign < 0 else (0, 1)
        stacked = jnp.concatenate(
            [jnp.concatenate([pair[0][g], pair[1][g]], axis=0) for g in range(group)], axis=1
        )
        high, low = _split(stacked)
        rows = _dot(left_ref[first], jnp.concatenate([high, high, low], axis=0))
        joined = jnp.concatenate(
            [
                jnp.concatenate(
                    [rows[:width, g * width:(g + 1) * width], rows[width:, g * width:(g + 1) * width]],
                    axis=1,
                )
                for g in range(group)
            ],
            axis=0,
        )
        high, low = _split(joined)
        out = _dot(jnp.concatenate([high, high, low], axis=1), right_ref[second])
        return (
            out[:, :width].reshape(group, width, width),
            out[:, width:].reshape(group, width, width),
        )

    return transform


def _layers(win_ref):
    slices = win_ref.shape[1] // 2
    return [
        (win_ref[:, 2 * s].astype(jnp.float32), win_ref[:, 2 * s + 1].astype(jnp.float32))
        for s in range(slices)
    ]


def _forward_kernel(win_ref, probe_ref, prop_ref, left_ref, right_ref, far_ref, inc_ref):
    group, width = win_ref.shape[0], probe_ref.shape[-1]
    transform = _transformer(left_ref, right_ref, group, width)
    layers = _layers(win_ref)
    probe = (probe_ref[0][None], probe_ref[1][None])
    kernel = (prop_ref[0][None], prop_ref[1][None])
    wave = _times(probe, layers[0])
    for s in range(1, len(layers)):
        moved = transform(_times(kernel, transform(wave, -1)), 1)
        inc_ref[:, 2 * (s - 1)] = moved[0]
        inc_ref[:, 2 * (s - 1) + 1] = moved[1]
        wave = _times(layers[s], moved)
    far = transform(wave, -1)
    far_ref[:, 0] = far[0]
    far_ref[:, 1] = far[1]


def _backward_kernel(
    target_ref, amp_ref, far_ref, inc_ref, win_ref, probe_ref, prop_ref, left_ref, right_ref, out_ref
):
    group, width = win_ref.shape[0], probe_ref.shape[-1]
    step = pl.program_id(0)
    transform = _transformer(left_ref, right_ref, group, width)
    layers = _layers(win_ref)
    slices = len(layers)
    probe = (probe_ref[0][None], probe_ref[1][None])
    kernel_conj = (prop_ref[0][None], -prop_ref[1][None])
    amplitude = jnp.stack(
        [amp_ref[target_ref[step * group + g]].astype(jnp.float32) for g in range(group)]
    )
    far = (far_ref[:, 0], far_ref[:, 1])
    magnitude = jnp.sqrt(far[0] * far[0] + far[1] * far[1] + 1.0)
    factor = 1.0 - amplitude / magnitude
    back = transform((far[0] * factor, far[1] * factor), 1)
    grads = [None] * slices
    for s in range(slices - 1, 0, -1):
        grads[s] = _conj_times((inc_ref[:, 2 * (s - 1)], inc_ref[:, 2 * (s - 1) + 1]), back)
        back = transform(_times(kernel_conj, transform(_conj_times(layers[s], back), -1)), 1)
    grads[0] = _conj_times(probe, back)
    for s in range(slices):
        out_ref[:, 2 * s] = grads[s][0].astype(out_ref.dtype)
        out_ref[:, 2 * s + 1] = grads[s][1].astype(out_ref.dtype)


def forward_waves(windows, probe, kernel, tables, group=8):
    count, channels, width, _ = windows.shape
    group = math.gcd(count, group)
    left_tables, right_tables = tables
    fixed = lambda k: (0, 0, 0)
    return pl.pallas_call(
        _forward_kernel,
        grid=(count // group,),
        in_specs=[
            pl.BlockSpec((group, channels, width, width), lambda k: (k, 0, 0, 0)),
            pl.BlockSpec((2, width, width), fixed),
            pl.BlockSpec((2, width, width), fixed),
            pl.BlockSpec(left_tables.shape, fixed),
            pl.BlockSpec(right_tables.shape, fixed),
        ],
        out_specs=[
            pl.BlockSpec((group, 2, width, width), lambda k: (k, 0, 0, 0)),
            pl.BlockSpec((group, channels - 2, width, width), lambda k: (k, 0, 0, 0)),
        ],
        out_shape=[
            jax.ShapeDtypeStruct((count, 2, width, width), jnp.float32),
            jax.ShapeDtypeStruct((count, channels - 2, width, width), jnp.float32),
        ],
    )(windows, probe, kernel, left_tables, right_tables)


def backward_gradients(target, amplitudes, far, incoming, windows, probe, kernel, tables, group=8):
    count, channels, width, _ = windows.shape
    group = math.gcd(count, group)
    left_tables, right_tables = tables
    fixed = lambda k, t: (0, 0, 0)
    batch = lambda k, t: (k, 0, 0, 0)
    grid_spec = pltpu.PrefetchScalarGridSpec(
        num_scalar_prefetch=1,
        grid=(count // group,),
        in_specs=[
            pl.BlockSpec(amplitudes.shape, fixed),
            pl.BlockSpec((group, 2, width, width), batch),
            pl.BlockSpec((group, channels - 2, width, width), batch),
            pl.BlockSpec((group, channels, width, width), batch),
            pl.BlockSpec((2, width, width), fixed),
            pl.BlockSpec((2, width, width), fixed),
            pl.BlockSpec(left_tables.shape, fixed),
            pl.BlockSpec(right_tables.shape, fixed),
        ],
        out_specs=pl.BlockSpec((group, channels, width, width), batch),
    )
    return pl.pallas_call(
        _backward_kernel,
        grid_spec=grid_spec,
        out_shape=jax.ShapeDtypeStruct((count, channels, width, width), jnp.bfloat16),
    )(target, amplitudes, far, incoming, windows, probe, kernel, left_tables, right_tables)


def per_device(object_init, probe, propagator_phase, measured, corners, owner_column):
    width = probe.shape[-1]
    field = object_init
    tile = field.shape[1]
    capacity = measured.shape[3]
    columns = lax.axis_size("ty")
    tops = corners[0, 0, :, 0]
    lefts = corners[0, 0, :, 1]
    owner = owner_column[0, 0, :, 0]
    slot = slot_table(owner)
    target = jnp.clip(owner * capacity + slot, 0, columns * capacity - 1)
    gathered = lax.all_to_all(measured[0, 0], "ty", split_axis=0, concat_axis=0, tiled=True)
    gathered = gathered.reshape(columns * capacity, width, width)
    offsets = jnp.arange(width)
    cells = jnp.arange(tile)
    row_pick = (cells[None, None, :] == (tops[:, None, None] + offsets[None, :, None])).astype(
        jnp.bfloat16
    )
    col_pick = (cells[None, :, None] == (lefts[:, None, None] + offsets[None, None, :])).astype(
        jnp.bfloat16
    )
    field_low = field.astype(jnp.bfloat16)
    rows = jnp.einsum(
        "kir,crs->kcis", row_pick, field_low, preferred_element_type=jnp.float32
    ).astype(jnp.bfloat16)
    windows = jnp.einsum(
        "kcis,ksj->kcij", rows, col_pick, preferred_element_type=jnp.float32
    ).astype(jnp.bfloat16)
    tables = block_tables(width)
    kernel = jnp.stack([jnp.cos(propagator_phase), jnp.sin(propagator_phase)])
    far, incoming = forward_waves(windows, probe, kernel, tables)
    grads = backward_gradients(target, gathered, far, incoming, windows, probe, kernel, tables)
    placed_rows = jnp.einsum(
        "kir,kcij->kcrj", row_pick, grads, preferred_element_type=jnp.float32
    ).astype(jnp.bfloat16)
    total = jnp.einsum("kcrj,ksj->crs", placed_rows, col_pick, preferred_element_type=jnp.float32)
    halos = exchange_edges(
        field[:, 0, :] - step_rate * total[:, 0, :],
        field[:, -1, :] - step_rate * total[:, -1, :],
        field[:, :, 0] - step_rate * total[:, :, 0],
        field[:, :, -1] - step_rate * total[:, :, -1],
    )
    return smooth_update(field, total, *halos)


def solution(mesh):
    placed = (
        P(None, "tx", "ty"),
        P(),
        P(),
        P("tx", "ty", None, None, None, None),
        P("tx", "ty", None, None),
        P("tx", "ty", None, None),
    )
    return jax.shard_map(
        per_device, mesh=mesh, in_specs=placed, out_specs=P(None, "tx", "ty"), check_vma=False
    )
```

```python
import math

import jax
import numpy as np
import jax.numpy as jnp
from jax import lax
from jax.experimental import pallas as pl
from jax.experimental.pallas import tpu as pltpu
from jax.sharding import PartitionSpec as P

step_rate = 0.5
smooth_rate = 0.2


def slot_table(owner):
    order = jnp.arange(owner.shape[0])
    same = owner[:, None] == owner[None, :]
    earlier = order[None, :] < order[:, None]
    return jnp.sum(jnp.where(same & earlier, 1, 0), axis=1).astype(jnp.int32)


def exchange_edges(top, bottom, first, last):
    n_rows = lax.axis_size("tx")
    n_cols = lax.axis_size("ty")
    up_rows = [(i, i + 1) for i in range(n_rows - 1)]
    down_rows = [(i + 1, i) for i in range(n_rows - 1)]
    up_cols = [(i, i + 1) for i in range(n_cols - 1)]
    down_cols = [(i + 1, i) for i in range(n_cols - 1)]
    above = lax.ppermute(bottom, "tx", up_rows)
    below = lax.ppermute(top, "tx", down_rows)
    left = lax.ppermute(last, "ty", up_cols)
    right = lax.ppermute(first, "ty", down_cols)
    return above, below, left, right


def _bend(real, imag):
    weight = 1.0 / jnp.sqrt(1.0 + real * real + imag * imag)
    return real * weight, imag * weight


def _inner_kernel(field_ref, total_ref, out_ref):
    size = field_ref.shape[-1]
    rows = lax.broadcasted_iota(jnp.int32, (size, size), 0)
    cols = lax.broadcasted_iota(jnp.int32, (size, size), 1)
    centers = [field_ref[p] - step_rate * total_ref[p] for p in range(2)]
    views = []
    for v in centers:
        views.append((
            jnp.where(rows == size - 1, v, pltpu.roll(v, size - 1, 0)),
            jnp.where(rows == 0, v, pltpu.roll(v, 1, 0)),
            jnp.where(cols == size - 1, v, pltpu.roll(v, size - 1, 1)),
            jnp.where(cols == 0, v, pltpu.roll(v, 1, 1)),
        ))
    total_r = jnp.zeros_like(centers[0])
    total_i = jnp.zeros_like(centers[1])
    for n in range(4):
        bent = _bend(views[0][n] - centers[0], views[1][n] - centers[1])
        total_r = total_r + bent[0]
        total_i = total_i + bent[1]
    out_ref[0] = centers[0] + smooth_rate * total_r
    out_ref[1] = centers[1] + smooth_rate * total_i


def _edge_kernel(inner_ref, top_ref, bottom_ref, first_ref, last_ref,
                 above_ref, below_ref, left_ref, right_ref, out_ref):
    size, lanes = inner_ref.shape[1], inner_ref.shape[2]
    block = pl.program_id(0)
    rows = lax.broadcasted_iota(jnp.int32, (size, lanes), 0)
    cols = lax.broadcasted_iota(jnp.int32, (size, lanes), 1)
    square = lax.broadcasted_iota(jnp.int32, (size, size), 0) == lax.broadcasted_iota(
        jnp.int32, (size, size), 1)

    def as_column(line):
        return jnp.sum(jnp.where(square, line, 0.0), axis=1, keepdims=True)

    edge_col = jnp.where(block == 0, 0, lanes - 1)
    for s in range(inner_ref.shape[0] // 2):
        c0, c1 = 2 * s, 2 * s + 1
        north = _bend(above_ref[c0:c0 + 1] - top_ref[c0:c0 + 1], above_ref[c1:c1 + 1] - top_ref[c1:c1 + 1])
        south = _bend(below_ref[c0:c0 + 1] - bottom_ref[c0:c0 + 1],
                      below_ref[c1:c1 + 1] - bottom_ref[c1:c1 + 1])
        west = _bend(left_ref[c0:c0 + 1] - first_ref[c0:c0 + 1], left_ref[c1:c1 + 1] - first_ref[c1:c1 + 1])
        east = _bend(right_ref[c0:c0 + 1] - last_ref[c0:c0 + 1], right_ref[c1:c1 + 1] - last_ref[c1:c1 + 1])
        for part, c in ((0, c0), (1, c1)):
            side = as_column(jnp.where(block == 0, west[part], east[part]))
            extra = (
                jnp.where(rows == 0, north[part], 0.0)
                + jnp.where(rows == size - 1, south[part], 0.0)
                + jnp.where(cols == edge_col, side, 0.0)
            )
            out_ref[c] = inner_ref[c] + smooth_rate * extra


def smooth_update(field, total, edges, halos):
    channels, size, _ = field.shape
    plane = pl.BlockSpec((2, size, size), lambda s: (s, 0, 0))
    inner = pl.pallas_call(
        _inner_kernel,
        grid=(channels // 2,),
        in_specs=[plane, plane],
        out_specs=plane,
        out_shape=jax.ShapeDtypeStruct(field.shape, jnp.float32),
    )(field, total)
    lanes = 128
    half = pl.BlockSpec((channels, size, lanes), lambda b: (0, 0, b))
    row_part = pl.BlockSpec((channels, lanes), lambda b: (0, b))
    whole = pl.BlockSpec((channels, size), lambda b: (0, 0))
    return pl.pallas_call(
        _edge_kernel,
        grid=(size // lanes,),
        in_specs=[half, row_part, row_part, whole, whole, row_part, row_part, whole, whole],
        out_specs=half,
        out_shape=jax.ShapeDtypeStruct(field.shape, jnp.float32),
        input_output_aliases={0: 0},
    )(inner, *edges, *halos)


def block_tables(width):
    index = np.arange(width)
    angles = (index[:, None] * index[None, :] % width) * (2.0 * math.pi / width)
    scale = 1.0 / math.sqrt(width)
    cosine, sine = np.cos(angles) * scale, np.sin(angles) * scale
    plus = np.block([[cosine, -sine], [sine, cosine]])
    minus = np.block([[cosine, sine], [-sine, cosine]])
    lefts, rights = [], []
    for table in (plus, minus):
        high = table.astype(jnp.bfloat16)
        low = (table - high.astype(np.float64)).astype(jnp.bfloat16)
        lefts.append(np.concatenate([high, low, high], axis=1))
        rights.append(np.concatenate([high, low, high], axis=0))
    return jnp.asarray(np.stack(lefts)), jnp.asarray(np.stack(rights))


def _split(x):
    high = x.astype(jnp.bfloat16)
    low = (x - high.astype(jnp.float32)).astype(jnp.bfloat16)
    return high, low


def _dot(a, b):
    return jnp.dot(a, b, preferred_element_type=jnp.float32)


def _times(a, b):
    return (a[0] * b[0] - a[1] * b[1], a[0] * b[1] + a[1] * b[0])


def _conj_times(a, b):
    return (a[0] * b[0] + a[1] * b[1], a[0] * b[1] - a[1] * b[0])


def _transformer(left_ref, right_ref, group, width):
    def transform(pair, sign):
        first, second = (1, 0) if sign < 0 else (0, 1)
        stacked = jnp.concatenate(
            [jnp.concatenate([pair[0][g], pair[1][g]], axis=0) for g in range(group)], axis=1
        )
        high, low = _split(stacked)
        rows = _dot(left_ref[first], jnp.concatenate([high, high, low], axis=0))
        joined = jnp.concatenate(
            [
                jnp.concatenate(
                    [rows[:width, g * width:(g + 1) * width], rows[width:, g * width:(g + 1) * width]],
                    axis=1,
                )
                for g in range(group)
            ],
            axis=0,
        )
        high, low = _split(joined)
        out = _dot(jnp.concatenate([high, high, low], axis=1), right_ref[second])
        return (
            out[:, :width].reshape(group, width, width),
            out[:, width:].reshape(group, width, width),
        )

    return transform


def _layers(win_ref):
    slices = win_ref.shape[1] // 2
    return [
        (win_ref[:, 2 * s].astype(jnp.float32), win_ref[:, 2 * s + 1].astype(jnp.float32))
        for s in range(slices)
    ]


def _forward_kernel(win_ref, probe_ref, prop_ref, left_ref, right_ref, far_ref, inc_ref):
    group, width = win_ref.shape[0], probe_ref.shape[-1]
    transform = _transformer(left_ref, right_ref, group, width)
    layers = _layers(win_ref)
    probe = (probe_ref[0][None], probe_ref[1][None])
    kernel = (prop_ref[0][None], prop_ref[1][None])
    wave = _times(probe, layers[0])
    for s in range(1, len(layers)):
        moved = transform(_times(kernel, transform(wave, -1)), 1)
        inc_ref[:, 2 * (s - 1)] = moved[0]
        inc_ref[:, 2 * (s - 1) + 1] = moved[1]
        wave = _times(layers[s], moved)
    far = transform(wave, -1)
    far_ref[:, 0] = far[0]
    far_ref[:, 1] = far[1]


def _backward_kernel(
    target_ref, amp_ref, far_ref, inc_ref, win_ref, probe_ref, prop_ref, left_ref, right_ref, out_ref
):
    group, width = win_ref.shape[0], probe_ref.shape[-1]
    step = pl.program_id(0)
    transform = _transformer(left_ref, right_ref, group, width)
    layers = _layers(win_ref)
    slices = len(layers)
    probe = (probe_ref[0][None], probe_ref[1][None])
    kernel_conj = (prop_ref[0][None], -prop_ref[1][None])
    amplitude = jnp.stack(
        [amp_ref[target_ref[step * group + g]].astype(jnp.float32) for g in range(group)]
    )
    far = (far_ref[:, 0], far_ref[:, 1])
    magnitude = jnp.sqrt(far[0] * far[0] + far[1] * far[1] + 1.0)
    factor = 1.0 - amplitude / magnitude
    back = transform((far[0] * factor, far[1] * factor), 1)
    grads = [None] * slices
    for s in range(slices - 1, 0, -1):
        grads[s] = _conj_times((inc_ref[:, 2 * (s - 1)], inc_ref[:, 2 * (s - 1) + 1]), back)
        back = transform(_times(kernel_conj, transform(_conj_times(layers[s], back), -1)), 1)
    grads[0] = _conj_times(probe, back)
    for s in range(slices):
        out_ref[:, 2 * s] = grads[s][0].astype(out_ref.dtype)
        out_ref[:, 2 * s + 1] = grads[s][1].astype(out_ref.dtype)


def forward_waves(windows, probe, kernel, tables, group=8):
    count, channels, width, _ = windows.shape
    group = math.gcd(count, group)
    left_tables, right_tables = tables
    fixed = lambda k: (0, 0, 0)
    return pl.pallas_call(
        _forward_kernel,
        grid=(count // group,),
        in_specs=[
            pl.BlockSpec((group, channels, width, width), lambda k: (k, 0, 0, 0)),
            pl.BlockSpec((2, width, width), fixed),
            pl.BlockSpec((2, width, width), fixed),
            pl.BlockSpec(left_tables.shape, fixed),
            pl.BlockSpec(right_tables.shape, fixed),
        ],
        out_specs=[
            pl.BlockSpec((group, 2, width, width), lambda k: (k, 0, 0, 0)),
            pl.BlockSpec((group, channels - 2, width, width), lambda k: (k, 0, 0, 0)),
        ],
        out_shape=[
            jax.ShapeDtypeStruct((count, 2, width, width), jnp.float32),
            jax.ShapeDtypeStruct((count, channels - 2, width, width), jnp.float32),
        ],
    )(windows, probe, kernel, left_tables, right_tables)


def backward_gradients(target, amplitudes, far, incoming, windows, probe, kernel, tables, group=8):
    count, channels, width, _ = windows.shape
    group = math.gcd(count, group)
    left_tables, right_tables = tables
    fixed = lambda k, t: (0, 0, 0)
    batch = lambda k, t: (k, 0, 0, 0)
    grid_spec = pltpu.PrefetchScalarGridSpec(
        num_scalar_prefetch=1,
        grid=(count // group,),
        in_specs=[
            pl.BlockSpec(amplitudes.shape, fixed),
            pl.BlockSpec((group, 2, width, width), batch),
            pl.BlockSpec((group, channels - 2, width, width), batch),
            pl.BlockSpec((group, channels, width, width), batch),
            pl.BlockSpec((2, width, width), fixed),
            pl.BlockSpec((2, width, width), fixed),
            pl.BlockSpec(left_tables.shape, fixed),
            pl.BlockSpec(right_tables.shape, fixed),
        ],
        out_specs=pl.BlockSpec((group, channels, width, width), batch),
    )
    return pl.pallas_call(
        _backward_kernel,
        grid_spec=grid_spec,
        out_shape=jax.ShapeDtypeStruct((count, channels, width, width), jnp.bfloat16),
    )(target, amplitudes, far, incoming, windows, probe, kernel, left_tables, right_tables)


def per_device(object_init, probe, propagator_phase, measured, corners, owner_column):
    width = probe.shape[-1]
    field = object_init
    tile = field.shape[1]
    capacity = measured.shape[3]
    columns = lax.axis_size("ty")
    tops = corners[0, 0, :, 0]
    lefts = corners[0, 0, :, 1]
    owner = owner_column[0, 0, :, 0]
    slot = slot_table(owner)
    target = jnp.clip(owner * capacity + slot, 0, columns * capacity - 1)
    gathered = lax.all_to_all(measured[0, 0], "ty", split_axis=0, concat_axis=0, tiled=True)
    gathered = gathered.reshape(columns * capacity, width, width)
    offsets = jnp.arange(width)
    cells = jnp.arange(tile)
    row_pick = (cells[None, None, :] == (tops[:, None, None] + offsets[None, :, None])).astype(
        jnp.bfloat16
    )
    col_pick = (cells[None, :, None] == (lefts[:, None, None] + offsets[None, None, :])).astype(
        jnp.bfloat16
    )
    field_low = field.astype(jnp.bfloat16)
    rows = jnp.einsum(
        "kir,crs->kcis", row_pick, field_low, preferred_element_type=jnp.float32
    ).astype(jnp.bfloat16)
    windows = jnp.einsum(
        "kcis,ksj->kcij", rows, col_pick, preferred_element_type=jnp.float32
    ).astype(jnp.bfloat16)
    tables = block_tables(width)
    kernel = jnp.stack([jnp.cos(propagator_phase), jnp.sin(propagator_phase)])
    far, incoming = forward_waves(windows, probe, kernel, tables)
    grads = backward_gradients(target, gathered, far, incoming, windows, probe, kernel, tables)
    placed_rows = jnp.einsum(
        "kir,kcij->kcrj", row_pick, grads, preferred_element_type=jnp.float32
    ).astype(jnp.bfloat16)
    total = jnp.einsum("kcrj,ksj->crs", placed_rows, col_pick, preferred_element_type=jnp.float32)
    edges = (
        field[:, 0, :] - step_rate * total[:, 0, :],
        field[:, -1, :] - step_rate * total[:, -1, :],
        field[:, :, 0] - step_rate * total[:, :, 0],
        field[:, :, -1] - step_rate * total[:, :, -1],
    )
    halos = exchange_edges(*edges)
    return smooth_update(field, total, edges, halos)


def solution(mesh):
    placed = (
        P(None, "tx", "ty"),
        P(),
        P(),
        P("tx", "ty", None, None, None, None),
        P("tx", "ty", None, None),
        P("tx", "ty", None, None),
    )
    return jax.shard_map(
        per_device, mesh=mesh, in_specs=placed, out_specs=P(None, "tx", "ty"), check_vma=False
    )
```

```python
import math

import jax
import numpy as np
import jax.numpy as jnp
from jax import lax
from jax.experimental import pallas as pl
from jax.experimental.pallas import tpu as pltpu
from jax.sharding import PartitionSpec as P

step_rate = 0.5
smooth_rate = 0.2


def slot_table(owner):
    order = jnp.arange(owner.shape[0])
    same = owner[:, None] == owner[None, :]
    earlier = order[None, :] < order[:, None]
    return jnp.sum(jnp.where(same & earlier, 1, 0), axis=1).astype(jnp.int32)


def exchange_edges(top, bottom, first, last):
    n_rows = lax.axis_size("tx")
    n_cols = lax.axis_size("ty")
    up_rows = [(i, i + 1) for i in range(n_rows - 1)]
    down_rows = [(i + 1, i) for i in range(n_rows - 1)]
    up_cols = [(i, i + 1) for i in range(n_cols - 1)]
    down_cols = [(i + 1, i) for i in range(n_cols - 1)]
    above = lax.ppermute(bottom, "tx", up_rows)
    below = lax.ppermute(top, "tx", down_rows)
    left = lax.ppermute(last, "ty", up_cols)
    right = lax.ppermute(first, "ty", down_cols)
    return above, below, left, right


def _bend(real, imag):
    weight = 1.0 / jnp.sqrt(1.0 + real * real + imag * imag)
    return real * weight, imag * weight


def _inner_kernel(field_ref, total_ref, out_ref):
    size = field_ref.shape[-1]
    rows = lax.broadcasted_iota(jnp.int32, (size, size), 0)
    cols = lax.broadcasted_iota(jnp.int32, (size, size), 1)
    centers = [field_ref[p] - step_rate * total_ref[p] for p in range(2)]
    views = []
    for v in centers:
        views.append((
            jnp.where(rows == size - 1, v, pltpu.roll(v, size - 1, 0)),
            jnp.where(rows == 0, v, pltpu.roll(v, 1, 0)),
            jnp.where(cols == size - 1, v, pltpu.roll(v, size - 1, 1)),
            jnp.where(cols == 0, v, pltpu.roll(v, 1, 1)),
        ))
    total_r = jnp.zeros_like(centers[0])
    total_i = jnp.zeros_like(centers[1])
    for n in range(4):
        bent = _bend(views[0][n] - centers[0], views[1][n] - centers[1])
        total_r = total_r + bent[0]
        total_i = total_i + bent[1]
    out_ref[0] = centers[0] + smooth_rate * total_r
    out_ref[1] = centers[1] + smooth_rate * total_i


def _edge_kernel(inner_ref, top_ref, bottom_ref, first_ref, last_ref,
                 above_ref, below_ref, left_ref, right_ref, out_ref):
    size, lanes = inner_ref.shape[1], inner_ref.shape[2]
    block = pl.program_id(0)
    rows = lax.broadcasted_iota(jnp.int32, (size, lanes), 0)
    cols = lax.broadcasted_iota(jnp.int32, (size, lanes), 1)
    square = lax.broadcasted_iota(jnp.int32, (size, size), 0) == lax.broadcasted_iota(
        jnp.int32, (size, size), 1)

    def as_column(line):
        return jnp.sum(jnp.where(square, line, 0.0), axis=1, keepdims=True)

    edge_col = jnp.where(block == 0, 0, lanes - 1)
    for s in range(inner_ref.shape[0] // 2):
        c0, c1 = 2 * s, 2 * s + 1
        north = _bend(above_ref[c0:c0 + 1] - top_ref[c0:c0 + 1], above_ref[c1:c1 + 1] - top_ref[c1:c1 + 1])
        south = _bend(below_ref[c0:c0 + 1] - bottom_ref[c0:c0 + 1],
                      below_ref[c1:c1 + 1] - bottom_ref[c1:c1 + 1])
        west = _bend(left_ref[c0:c0 + 1] - first_ref[c0:c0 + 1], left_ref[c1:c1 + 1] - first_ref[c1:c1 + 1])
        east = _bend(right_ref[c0:c0 + 1] - last_ref[c0:c0 + 1], right_ref[c1:c1 + 1] - last_ref[c1:c1 + 1])
        for part, c in ((0, c0), (1, c1)):
            side = as_column(jnp.where(block == 0, west[part], east[part]))
            extra = (
                jnp.where(rows == 0, north[part], 0.0)
                + jnp.where(rows == size - 1, south[part], 0.0)
                + jnp.where(cols == edge_col, side, 0.0)
            )
            out_ref[c] = inner_ref[c] + smooth_rate * extra


def smooth_update(field, total, edges, halos):
    channels, size, _ = field.shape
    plane = pl.BlockSpec((2, size, size), lambda s: (s, 0, 0))
    inner = pl.pallas_call(
        _inner_kernel,
        grid=(channels // 2,),
        in_specs=[plane, plane],
        out_specs=plane,
        out_shape=jax.ShapeDtypeStruct(field.shape, jnp.float32),
    )(field, total)
    lanes = 128
    half = pl.BlockSpec((channels, size, lanes), lambda b: (0, 0, b))
    row_part = pl.BlockSpec((channels, lanes), lambda b: (0, b))
    whole = pl.BlockSpec((channels, size), lambda b: (0, 0))
    return pl.pallas_call(
        _edge_kernel,
        grid=(size // lanes,),
        in_specs=[half, row_part, row_part, whole, whole, row_part, row_part, whole, whole],
        out_specs=half,
        out_shape=jax.ShapeDtypeStruct(field.shape, jnp.float32),
        input_output_aliases={0: 0},
    )(inner, *edges, *halos)


def block_tables(width):
    index = np.arange(width)
    angles = (index[:, None] * index[None, :] % width) * (2.0 * math.pi / width)
    scale = 1.0 / math.sqrt(width)
    cosine, sine = np.cos(angles) * scale, np.sin(angles) * scale
    plus = np.block([[cosine, -sine], [sine, cosine]])
    minus = np.block([[cosine, sine], [-sine, cosine]])
    lefts, rights = [], []
    for table in (plus, minus):
        high = table.astype(jnp.bfloat16)
        low = (table - high.astype(np.float64)).astype(jnp.bfloat16)
        lefts.append(np.concatenate([high, low, high], axis=1))
        rights.append(np.concatenate([high, low, high], axis=0))
    return jnp.asarray(np.stack(lefts)), jnp.asarray(np.stack(rights))


def _split(x):
    high = x.astype(jnp.bfloat16)
    low = (x - high.astype(jnp.float32)).astype(jnp.bfloat16)
    return high, low


def _dot(a, b):
    return jnp.dot(a, b, preferred_element_type=jnp.float32)


def _times(a, b):
    return (a[0] * b[0] - a[1] * b[1], a[0] * b[1] + a[1] * b[0])


def _conj_times(a, b):
    return (a[0] * b[0] + a[1] * b[1], a[0] * b[1] - a[1] * b[0])


def _transformer(left_ref, right_ref, group, width):
    def transform(pair, sign):
        first, second = (1, 0) if sign < 0 else (0, 1)
        stacked = jnp.concatenate(
            [jnp.concatenate([pair[0][g], pair[1][g]], axis=0) for g in range(group)], axis=1
        )
        high, low = _split(stacked)
        rows = _dot(left_ref[first], jnp.concatenate([high, high, low], axis=0))
        joined = jnp.concatenate(
            [
                jnp.concatenate(
                    [rows[:width, g * width:(g + 1) * width], rows[width:, g * width:(g + 1) * width]],
                    axis=1,
                )
                for g in range(group)
            ],
            axis=0,
        )
        high, low = _split(joined)
        out = _dot(jnp.concatenate([high, high, low], axis=1), right_ref[second])
        return (
            out[:, :width].reshape(group, width, width),
            out[:, width:].reshape(group, width, width),
        )

    return transform


def _layers(win_ref):
    slices = win_ref.shape[1] // 2
    return [
        (win_ref[:, 2 * s].astype(jnp.float32), win_ref[:, 2 * s + 1].astype(jnp.float32))
        for s in range(slices)
    ]


def _forward_kernel(win_ref, probe_ref, prop_ref, left_ref, right_ref, far_ref, inc_ref):
    group, width = win_ref.shape[0], probe_ref.shape[-1]
    transform = _transformer(left_ref, right_ref, group, width)
    layers = _layers(win_ref)
    probe = (probe_ref[0][None], probe_ref[1][None])
    kernel = (prop_ref[0][None], prop_ref[1][None])
    wave = _times(probe, layers[0])
    for s in range(1, len(layers)):
        moved = transform(_times(kernel, transform(wave, -1)), 1)
        inc_ref[:, 2 * (s - 1)] = moved[0]
        inc_ref[:, 2 * (s - 1) + 1] = moved[1]
        wave = _times(layers[s], moved)
    far = transform(wave, -1)
    far_ref[:, 0] = far[0]
    far_ref[:, 1] = far[1]


def _backward_kernel(
    target_ref, tops_ref, lefts_ref, amp_ref, far_ref, inc_ref, win_ref, probe_ref, prop_ref,
    left_ref, right_ref, out_ref
):
    group, width = win_ref.shape[0], probe_ref.shape[-1]
    step = pl.program_id(0)
    transform = _transformer(left_ref, right_ref, group, width)
    layers = _layers(win_ref)
    slices = len(layers)
    probe = (probe_ref[0][None], probe_ref[1][None])
    kernel_conj = (prop_ref[0][None], -prop_ref[1][None])
    amplitude = jnp.stack(
        [amp_ref[target_ref[step * group + g]].astype(jnp.float32) for g in range(group)]
    )
    far = (far_ref[:, 0], far_ref[:, 1])
    magnitude = jnp.sqrt(far[0] * far[0] + far[1] * far[1] + 1.0)
    factor = 1.0 - amplitude / magnitude
    back = transform((far[0] * factor, far[1] * factor), 1)
    grads = [None] * slices
    for s in range(slices - 1, 0, -1):
        grads[s] = _conj_times((inc_ref[:, 2 * (s - 1)], inc_ref[:, 2 * (s - 1) + 1]), back)
        back = transform(_times(kernel_conj, transform(_conj_times(layers[s], back), -1)), 1)
    grads[0] = _conj_times(probe, back)
    planes = [part.astype(jnp.bfloat16) for pair in grads for part in pair]
    channels, tile = out_ref.shape[0], out_ref.shape[-1]
    down = lax.broadcasted_iota(jnp.int32, (tile, width), 0) - lax.broadcasted_iota(
        jnp.int32, (tile, width), 1)
    across = lax.broadcasted_iota(jnp.int32, (width, tile), 1) - lax.broadcasted_iota(
        jnp.int32, (width, tile), 0)
    placed, col_picks = [], []
    for g in range(group):
        top = tops_ref[step * group + g]
        left = lefts_ref[step * group + g]
        row_pick = (down == top).astype(jnp.bfloat16)
        col_picks.append((across == left).astype(jnp.bfloat16))
        stacked = jnp.concatenate([plane[g] for plane in planes], axis=1)
        placed.append(_dot(row_pick, stacked).astype(jnp.bfloat16))
    spread = jnp.concatenate(
        [
            jnp.concatenate([rows[:, c * width:(c + 1) * width] for rows in placed], axis=1)
            for c in range(channels)
        ],
        axis=0,
    )
    contribution = _dot(spread, jnp.concatenate(col_picks, axis=0)).reshape(channels, tile, tile)

    @pl.when(step == 0)
    def _():
        out_ref[...] = jnp.zeros_like(out_ref)

    out_ref[...] += contribution


def forward_waves(windows, probe, kernel, tables, group=8):
    count, channels, width, _ = windows.shape
    group = math.gcd(count, group)
    left_tables, right_tables = tables
    fixed = lambda k: (0, 0, 0)
    return pl.pallas_call(
        _forward_kernel,
        grid=(count // group,),
        in_specs=[
            pl.BlockSpec((group, channels, width, width), lambda k: (k, 0, 0, 0)),
            pl.BlockSpec((2, width, width), fixed),
            pl.BlockSpec((2, width, width), fixed),
            pl.BlockSpec(left_tables.shape, fixed),
            pl.BlockSpec(right_tables.shape, fixed),
        ],
        out_specs=[
            pl.BlockSpec((group, 2, width, width), lambda k: (k, 0, 0, 0)),
            pl.BlockSpec((group, channels - 2, width, width), lambda k: (k, 0, 0, 0)),
        ],
        out_shape=[
            jax.ShapeDtypeStruct((count, 2, width, width), jnp.float32),
            jax.ShapeDtypeStruct((count, channels - 2, width, width), jnp.float32),
        ],
    )(windows, probe, kernel, left_tables, right_tables)


def backward_gradients(target, tops, lefts, amplitudes, far, incoming, windows, probe, kernel,
                       tables, tile, group=8):
    count, channels, width, _ = windows.shape
    group = math.gcd(count, group)
    left_tables, right_tables = tables
    fixed = lambda k, *_: (0, 0, 0)
    batch = lambda k, *_: (k, 0, 0, 0)
    grid_spec = pltpu.PrefetchScalarGridSpec(
        num_scalar_prefetch=3,
        grid=(count // group,),
        in_specs=[
            pl.BlockSpec(amplitudes.shape, fixed),
            pl.BlockSpec((group, 2, width, width), batch),
            pl.BlockSpec((group, channels - 2, width, width), batch),
            pl.BlockSpec((group, channels, width, width), batch),
            pl.BlockSpec((2, width, width), fixed),
            pl.BlockSpec((2, width, width), fixed),
            pl.BlockSpec(left_tables.shape, fixed),
            pl.BlockSpec(right_tables.shape, fixed),
        ],
        out_specs=pl.BlockSpec((channels, tile, tile), fixed),
    )
    return pl.pallas_call(
        _backward_kernel,
        grid_spec=grid_spec,
        out_shape=jax.ShapeDtypeStruct((channels, tile, tile), jnp.float32),
    )(target, tops, lefts, amplitudes, far, incoming, windows, probe, kernel, left_tables,
      right_tables)


def per_device(object_init, probe, propagator_phase, measured, corners, owner_column):
    width = probe.shape[-1]
    field = object_init
    tile = field.shape[1]
    capacity = measured.shape[3]
    columns = lax.axis_size("ty")
    tops = corners[0, 0, :, 0]
    lefts = corners[0, 0, :, 1]
    owner = owner_column[0, 0, :, 0]
    slot = slot_table(owner)
    target = jnp.clip(owner * capacity + slot, 0, columns * capacity - 1)
    gathered = lax.all_to_all(measured[0, 0], "ty", split_axis=0, concat_axis=0, tiled=True)
    gathered = gathered.reshape(columns * capacity, width, width)
    offsets = jnp.arange(width)
    cells = jnp.arange(tile)
    row_pick = (cells[None, None, :] == (tops[:, None, None] + offsets[None, :, None])).astype(
        jnp.bfloat16
    )
    col_pick = (cells[None, :, None] == (lefts[:, None, None] + offsets[None, None, :])).astype(
        jnp.bfloat16
    )
    field_low = field.astype(jnp.bfloat16)
    rows = jnp.einsum(
        "kir,crs->kcis", row_pick, field_low, preferred_element_type=jnp.float32
    ).astype(jnp.bfloat16)
    windows = jnp.einsum(
        "kcis,ksj->kcij", rows, col_pick, preferred_element_type=jnp.float32
    ).astype(jnp.bfloat16)
    tables = block_tables(width)
    kernel = jnp.stack([jnp.cos(propagator_phase), jnp.sin(propagator_phase)])
    far, incoming = forward_waves(windows, probe, kernel, tables)
    total = backward_gradients(
        target, tops, lefts, gathered, far, incoming, windows, probe, kernel, tables, tile
    )
    edges = (
        field[:, 0, :] - step_rate * total[:, 0, :],
        field[:, -1, :] - step_rate * total[:, -1, :],
        field[:, :, 0] - step_rate * total[:, :, 0],
        field[:, :, -1] - step_rate * total[:, :, -1],
    )
    halos = exchange_edges(*edges)
    return smooth_update(field, total, edges, halos)


def solution(mesh):
    placed = (
        P(None, "tx", "ty"),
        P(),
        P(),
        P("tx", "ty", None, None, None, None),
        P("tx", "ty", None, None),
        P("tx", "ty", None, None),
    )
    return jax.shard_map(
        per_device, mesh=mesh, in_specs=placed, out_specs=P(None, "tx", "ty"), check_vma=False
    )
```

```python
import math

import jax
import numpy as np
import jax.numpy as jnp
from jax import lax
from jax.experimental import pallas as pl
from jax.experimental.pallas import tpu as pltpu
from jax.sharding import PartitionSpec as P

step_rate = 0.5
smooth_rate = 0.2


def slot_table(owner):
    order = jnp.arange(owner.shape[0])
    same = owner[:, None] == owner[None, :]
    earlier = order[None, :] < order[:, None]
    return jnp.sum(jnp.where(same & earlier, 1, 0), axis=1).astype(jnp.int32)


def exchange_edges(top, bottom, first, last):
    n_rows = lax.axis_size("tx")
    n_cols = lax.axis_size("ty")
    up_rows = [(i, i + 1) for i in range(n_rows - 1)]
    down_rows = [(i + 1, i) for i in range(n_rows - 1)]
    up_cols = [(i, i + 1) for i in range(n_cols - 1)]
    down_cols = [(i + 1, i) for i in range(n_cols - 1)]
    above = lax.ppermute(bottom, "tx", up_rows)
    below = lax.ppermute(top, "tx", down_rows)
    left = lax.ppermute(last, "ty", up_cols)
    right = lax.ppermute(first, "ty", down_cols)
    return above, below, left, right


def _bend(real, imag):
    weight = 1.0 / jnp.sqrt(1.0 + real * real + imag * imag)
    return real * weight, imag * weight


def _inner_kernel(field_ref, total_ref, out_ref):
    size = field_ref.shape[-1]
    rows = lax.broadcasted_iota(jnp.int32, (size, size), 0)
    cols = lax.broadcasted_iota(jnp.int32, (size, size), 1)
    centers = [field_ref[p] - step_rate * total_ref[p] for p in range(2)]
    views = []
    for v in centers:
        views.append((
            jnp.where(rows == size - 1, v, pltpu.roll(v, size - 1, 0)),
            jnp.where(rows == 0, v, pltpu.roll(v, 1, 0)),
            jnp.where(cols == size - 1, v, pltpu.roll(v, size - 1, 1)),
            jnp.where(cols == 0, v, pltpu.roll(v, 1, 1)),
        ))
    total_r = jnp.zeros_like(centers[0])
    total_i = jnp.zeros_like(centers[1])
    for n in range(4):
        bent = _bend(views[0][n] - centers[0], views[1][n] - centers[1])
        total_r = total_r + bent[0]
        total_i = total_i + bent[1]
    out_ref[0] = centers[0] + smooth_rate * total_r
    out_ref[1] = centers[1] + smooth_rate * total_i


def _edge_kernel(inner_ref, top_ref, bottom_ref, first_ref, last_ref,
                 above_ref, below_ref, left_ref, right_ref, out_ref):
    size, lanes = inner_ref.shape[1], inner_ref.shape[2]
    block = pl.program_id(0)
    rows = lax.broadcasted_iota(jnp.int32, (size, lanes), 0)
    cols = lax.broadcasted_iota(jnp.int32, (size, lanes), 1)
    square = lax.broadcasted_iota(jnp.int32, (lanes, lanes), 0) == lax.broadcasted_iota(
        jnp.int32, (lanes, lanes), 1)

    def as_column(line):
        return jnp.concatenate(
            [
                jnp.sum(jnp.where(square, line[:, h * lanes:(h + 1) * lanes], 0.0), axis=1,
                        keepdims=True)
                for h in range(size // lanes)
            ],
            axis=0,
        )

    edge_col = jnp.where(block == 0, 0, lanes - 1)
    for s in range(inner_ref.shape[0] // 2):
        c0, c1 = 2 * s, 2 * s + 1
        north = _bend(above_ref[c0:c0 + 1] - top_ref[c0:c0 + 1], above_ref[c1:c1 + 1] - top_ref[c1:c1 + 1])
        south = _bend(below_ref[c0:c0 + 1] - bottom_ref[c0:c0 + 1],
                      below_ref[c1:c1 + 1] - bottom_ref[c1:c1 + 1])
        west = _bend(left_ref[c0:c0 + 1] - first_ref[c0:c0 + 1], left_ref[c1:c1 + 1] - first_ref[c1:c1 + 1])
        east = _bend(right_ref[c0:c0 + 1] - last_ref[c0:c0 + 1], right_ref[c1:c1 + 1] - last_ref[c1:c1 + 1])
        for part, c in ((0, c0), (1, c1)):
            side = as_column(jnp.where(block == 0, west[part], east[part]))
            extra = (
                jnp.where(rows == 0, north[part], 0.0)
                + jnp.where(rows == size - 1, south[part], 0.0)
                + jnp.where(cols == edge_col, side, 0.0)
            )
            out_ref[c] = inner_ref[c] + smooth_rate * extra


def smooth_update(field, total, edges, halos):
    channels, size, _ = field.shape
    plane = pl.BlockSpec((2, size, size), lambda s: (s, 0, 0))
    inner = pl.pallas_call(
        _inner_kernel,
        grid=(channels // 2,),
        in_specs=[plane, plane],
        out_specs=plane,
        out_shape=jax.ShapeDtypeStruct(field.shape, jnp.float32),
    )(field, total)
    lanes = 128
    half = pl.BlockSpec((channels, size, lanes), lambda b: (0, 0, b))
    row_part = pl.BlockSpec((channels, lanes), lambda b: (0, b))
    whole = pl.BlockSpec((channels, size), lambda b: (0, 0))
    return pl.pallas_call(
        _edge_kernel,
        grid=(size // lanes,),
        in_specs=[half, row_part, row_part, whole, whole, row_part, row_part, whole, whole],
        out_specs=half,
        out_shape=jax.ShapeDtypeStruct(field.shape, jnp.float32),
        input_output_aliases={0: 0},
    )(inner, *edges, *halos)


def block_tables(width):
    index = np.arange(width)
    angles = (index[:, None] * index[None, :] % width) * (2.0 * math.pi / width)
    scale = 1.0 / math.sqrt(width)
    cosine, sine = np.cos(angles) * scale, np.sin(angles) * scale
    plus = np.block([[cosine, -sine], [sine, cosine]])
    minus = np.block([[cosine, sine], [-sine, cosine]])
    lefts, rights = [], []
    for table in (plus, minus):
        high = table.astype(jnp.bfloat16)
        low = (table - high.astype(np.float64)).astype(jnp.bfloat16)
        lefts.append(np.concatenate([high, low, high], axis=1))
        rights.append(np.concatenate([high, low, high], axis=0))
    return jnp.asarray(np.stack(lefts)), jnp.asarray(np.stack(rights))


def _split(x):
    high = x.astype(jnp.bfloat16)
    low = (x - high.astype(jnp.float32)).astype(jnp.bfloat16)
    return high, low


def _dot(a, b):
    return jnp.dot(a, b, preferred_element_type=jnp.float32)


def _times(a, b):
    return (a[0] * b[0] - a[1] * b[1], a[0] * b[1] + a[1] * b[0])


def _conj_times(a, b):
    return (a[0] * b[0] + a[1] * b[1], a[0] * b[1] - a[1] * b[0])


def _transformer(left_ref, right_ref, group, width):
    def transform(pair, sign):
        first, second = (1, 0) if sign < 0 else (0, 1)
        stacked = jnp.concatenate(
            [jnp.concatenate([pair[0][g], pair[1][g]], axis=0) for g in range(group)], axis=1
        )
        high, low = _split(stacked)
        rows = _dot(left_ref[first], jnp.concatenate([high, high, low], axis=0))
        joined = jnp.concatenate(
            [
                jnp.concatenate(
                    [rows[:width, g * width:(g + 1) * width], rows[width:, g * width:(g + 1) * width]],
                    axis=1,
                )
                for g in range(group)
            ],
            axis=0,
        )
        high, low = _split(joined)
        out = _dot(jnp.concatenate([high, high, low], axis=1), right_ref[second])
        return (
            out[:, :width].reshape(group, width, width),
            out[:, width:].reshape(group, width, width),
        )

    return transform


def _layers(win_ref):
    slices = win_ref.shape[1] // 2
    return [
        (win_ref[:, 2 * s].astype(jnp.float32), win_ref[:, 2 * s + 1].astype(jnp.float32))
        for s in range(slices)
    ]


def _forward_kernel(win_ref, probe_ref, prop_ref, left_ref, right_ref, far_ref, inc_ref):
    group, width = win_ref.shape[0], probe_ref.shape[-1]
    transform = _transformer(left_ref, right_ref, group, width)
    layers = _layers(win_ref)
    probe = (probe_ref[0][None], probe_ref[1][None])
    kernel = (prop_ref[0][None], prop_ref[1][None])
    wave = _times(probe, layers[0])
    for s in range(1, len(layers)):
        moved = transform(_times(kernel, transform(wave, -1)), 1)
        inc_ref[:, 2 * (s - 1)] = moved[0]
        inc_ref[:, 2 * (s - 1) + 1] = moved[1]
        wave = _times(layers[s], moved)
    far = transform(wave, -1)
    far_ref[:, 0] = far[0]
    far_ref[:, 1] = far[1]


def _backward_kernel(
    target_ref, tops_ref, lefts_ref, amp_ref, far_ref, inc_ref, win_ref, probe_ref, prop_ref,
    left_ref, right_ref, out_ref, edges_ref
):
    group, width = win_ref.shape[0], probe_ref.shape[-1]
    step = pl.program_id(0)
    transform = _transformer(left_ref, right_ref, group, width)
    layers = _layers(win_ref)
    slices = len(layers)
    probe = (probe_ref[0][None], probe_ref[1][None])
    kernel_conj = (prop_ref[0][None], -prop_ref[1][None])
    amplitude = jnp.stack(
        [amp_ref[target_ref[step * group + g]].astype(jnp.float32) for g in range(group)]
    )
    far = (far_ref[:, 0], far_ref[:, 1])
    magnitude = jnp.sqrt(far[0] * far[0] + far[1] * far[1] + 1.0)
    factor = 1.0 - amplitude / magnitude
    back = transform((far[0] * factor, far[1] * factor), 1)
    grads = [None] * slices
    for s in range(slices - 1, 0, -1):
        grads[s] = _conj_times((inc_ref[:, 2 * (s - 1)], inc_ref[:, 2 * (s - 1) + 1]), back)
        back = transform(_times(kernel_conj, transform(_conj_times(layers[s], back), -1)), 1)
    grads[0] = _conj_times(probe, back)
    planes = [part.astype(jnp.bfloat16) for pair in grads for part in pair]
    channels, tile = out_ref.shape[0], out_ref.shape[-1]
    down = lax.broadcasted_iota(jnp.int32, (tile, width), 0) - lax.broadcasted_iota(
        jnp.int32, (tile, width), 1)
    across = lax.broadcasted_iota(jnp.int32, (width, tile), 1) - lax.broadcasted_iota(
        jnp.int32, (width, tile), 0)
    placed, col_picks = [], []
    for g in range(group):
        top = tops_ref[step * group + g]
        left = lefts_ref[step * group + g]
        row_pick = (down == top).astype(jnp.bfloat16)
        col_picks.append((across == left).astype(jnp.bfloat16))
        stacked = jnp.concatenate([plane[g] for plane in planes], axis=1)
        placed.append(_dot(row_pick, stacked).astype(jnp.bfloat16))
    spread = jnp.concatenate(
        [
            jnp.concatenate([rows[:, c * width:(c + 1) * width] for rows in placed], axis=1)
            for c in range(channels)
        ],
        axis=0,
    )
    contribution = _dot(spread, jnp.concatenate(col_picks, axis=0)).reshape(channels, tile, tile)

    @pl.when(step == 0)
    def _():
        out_ref[...] = jnp.zeros_like(out_ref)

    out_ref[...] += contribution

    @pl.when(step == pl.num_programs(0) - 1)
    def _():
        lanes = lax.broadcasted_iota(jnp.int32, (8, tile), 1)
        which = jnp.where(lax.broadcasted_iota(jnp.int32, (8, tile), 0) == 0, 0, tile - 1)
        pick = (lanes == which).astype(jnp.bfloat16)
        for c in range(channels):
            plane = out_ref[c]
            edges_ref[0, c:c + 1, :] = plane[0:1, :]
            edges_ref[1, c:c + 1, :] = plane[tile - 1:tile, :]
            high = plane.astype(jnp.bfloat16)
            rest = plane - high.astype(jnp.float32)
            middle = rest.astype(jnp.bfloat16)
            low = (rest - middle.astype(jnp.float32)).astype(jnp.bfloat16)
            cols = None
            for part in (high, middle, low):
                term = lax.dot_general(
                    pick, part, (((1,), (1,)), ((), ())), preferred_element_type=jnp.float32
                )
                cols = term if cols is None else cols + term
            edges_ref[2, c:c + 1, :] = cols[0:1]
            edges_ref[3, c:c + 1, :] = cols[1:2]


def forward_waves(windows, probe, kernel, tables, group=8):
    count, channels, width, _ = windows.shape
    group = math.gcd(count, group)
    left_tables, right_tables = tables
    fixed = lambda k: (0, 0, 0)
    return pl.pallas_call(
        _forward_kernel,
        grid=(count // group,),
        in_specs=[
            pl.BlockSpec((group, channels, width, width), lambda k: (k, 0, 0, 0)),
            pl.BlockSpec((2, width, width), fixed),
            pl.BlockSpec((2, width, width), fixed),
            pl.BlockSpec(left_tables.shape, fixed),
            pl.BlockSpec(right_tables.shape, fixed),
        ],
        out_specs=[
            pl.BlockSpec((group, 2, width, width), lambda k: (k, 0, 0, 0)),
            pl.BlockSpec((group, channels - 2, width, width), lambda k: (k, 0, 0, 0)),
        ],
        out_shape=[
            jax.ShapeDtypeStruct((count, 2, width, width), jnp.float32),
            jax.ShapeDtypeStruct((count, channels - 2, width, width), jnp.float32),
        ],
    )(windows, probe, kernel, left_tables, right_tables)


def backward_gradients(target, tops, lefts, amplitudes, far, incoming, windows, probe, kernel,
                       tables, tile, group=8):
    count, channels, width, _ = windows.shape
    group = math.gcd(count, group)
    left_tables, right_tables = tables
    fixed = lambda k, *_: (0, 0, 0)
    batch = lambda k, *_: (k, 0, 0, 0)
    grid_spec = pltpu.PrefetchScalarGridSpec(
        num_scalar_prefetch=3,
        grid=(count // group,),
        in_specs=[
            pl.BlockSpec(amplitudes.shape, fixed),
            pl.BlockSpec((group, 2, width, width), batch),
            pl.BlockSpec((group, channels - 2, width, width), batch),
            pl.BlockSpec((group, channels, width, width), batch),
            pl.BlockSpec((2, width, width), fixed),
            pl.BlockSpec((2, width, width), fixed),
            pl.BlockSpec(left_tables.shape, fixed),
            pl.BlockSpec(right_tables.shape, fixed),
        ],
        out_specs=[
            pl.BlockSpec((channels, tile, tile), fixed),
            pl.BlockSpec((4, channels, tile), fixed),
        ],
    )
    return pl.pallas_call(
        _backward_kernel,
        grid_spec=grid_spec,
        out_shape=[
            jax.ShapeDtypeStruct((channels, tile, tile), jnp.float32),
            jax.ShapeDtypeStruct((4, channels, tile), jnp.float32),
        ],
    )(target, tops, lefts, amplitudes, far, incoming, windows, probe, kernel, left_tables,
      right_tables)


def per_device(object_init, probe, propagator_phase, measured, corners, owner_column):
    width = probe.shape[-1]
    field = object_init
    tile = field.shape[1]
    capacity = measured.shape[3]
    columns = lax.axis_size("ty")
    tops = corners[0, 0, :, 0]
    lefts = corners[0, 0, :, 1]
    owner = owner_column[0, 0, :, 0]
    slot = slot_table(owner)
    target = jnp.clip(owner * capacity + slot, 0, columns * capacity - 1)
    gathered = lax.all_to_all(measured[0, 0], "ty", split_axis=0, concat_axis=0, tiled=True)
    gathered = gathered.reshape(columns * capacity, width, width)
    offsets = jnp.arange(width)
    cells = jnp.arange(tile)
    row_pick = (cells[None, None, :] == (tops[:, None, None] + offsets[None, :, None])).astype(
        jnp.bfloat16
    )
    col_pick = (cells[None, :, None] == (lefts[:, None, None] + offsets[None, None, :])).astype(
        jnp.bfloat16
    )
    field_low = field.astype(jnp.bfloat16)
    rows = jnp.einsum(
        "kir,crs->kcis", row_pick, field_low, preferred_element_type=jnp.float32
    ).astype(jnp.bfloat16)
    windows = jnp.einsum(
        "kcis,ksj->kcij", rows, col_pick, preferred_element_type=jnp.float32
    ).astype(jnp.bfloat16)
    tables = block_tables(width)
    kernel = jnp.stack([jnp.cos(propagator_phase), jnp.sin(propagator_phase)])
    far, incoming = forward_waves(windows, probe, kernel, tables)
    total, total_edges = backward_gradients(
        target, tops, lefts, gathered, far, incoming, windows, probe, kernel, tables, tile
    )
    edges = (
        field[:, 0, :] - step_rate * total_edges[0],
        field[:, -1, :] - step_rate * total_edges[1],
        field[:, :, 0] - step_rate * total_edges[2],
        field[:, :, -1] - step_rate * total_edges[3],
    )
    halos = exchange_edges(*edges)
    return smooth_update(field, total, edges, halos)


def solution(mesh):
    placed = (
        P(None, "tx", "ty"),
        P(),
        P(),
        P("tx", "ty", None, None, None, None),
        P("tx", "ty", None, None),
        P("tx", "ty", None, None),
    )
    return jax.shard_map(
        per_device, mesh=mesh, in_specs=placed, out_specs=P(None, "tx", "ty"), check_vma=False
    )
```

```python
import math

import jax
import numpy as np
import jax.numpy as jnp
from jax import lax
from jax.experimental import pallas as pl
from jax.experimental.pallas import tpu as pltpu
from jax.sharding import PartitionSpec as P

step_rate = 0.5
smooth_rate = 0.2


def slot_table(owner):
    order = jnp.arange(owner.shape[0])
    same = owner[:, None] == owner[None, :]
    earlier = order[None, :] < order[:, None]
    return jnp.sum(jnp.where(same & earlier, 1, 0), axis=1).astype(jnp.int32)


def exchange_edges(top, bottom, first, last):
    n_rows = lax.axis_size("tx")
    n_cols = lax.axis_size("ty")
    up_rows = [(i, i + 1) for i in range(n_rows - 1)]
    down_rows = [(i + 1, i) for i in range(n_rows - 1)]
    up_cols = [(i, i + 1) for i in range(n_cols - 1)]
    down_cols = [(i + 1, i) for i in range(n_cols - 1)]
    above = lax.ppermute(bottom, "tx", up_rows)
    below = lax.ppermute(top, "tx", down_rows)
    left = lax.ppermute(last, "ty", up_cols)
    right = lax.ppermute(first, "ty", down_cols)
    return above, below, left, right


def _bend(real, imag):
    weight = 1.0 / jnp.sqrt(1.0 + real * real + imag * imag)
    return real * weight, imag * weight


def _inner_kernel(field_ref, total_ref, out_ref):
    size = field_ref.shape[-1]
    rows = lax.broadcasted_iota(jnp.int32, (size, size), 0)
    cols = lax.broadcasted_iota(jnp.int32, (size, size), 1)
    centers = [field_ref[p] - step_rate * total_ref[p] for p in range(2)]
    views = []
    for v in centers:
        views.append((
            jnp.where(rows == size - 1, v, pltpu.roll(v, size - 1, 0)),
            jnp.where(rows == 0, v, pltpu.roll(v, 1, 0)),
            jnp.where(cols == size - 1, v, pltpu.roll(v, size - 1, 1)),
            jnp.where(cols == 0, v, pltpu.roll(v, 1, 1)),
        ))
    total_r = jnp.zeros_like(centers[0])
    total_i = jnp.zeros_like(centers[1])
    for n in range(4):
        bent = _bend(views[0][n] - centers[0], views[1][n] - centers[1])
        total_r = total_r + bent[0]
        total_i = total_i + bent[1]
    out_ref[0] = centers[0] + smooth_rate * total_r
    out_ref[1] = centers[1] + smooth_rate * total_i


def _edge_kernel(inner_ref, top_ref, bottom_ref, first_ref, last_ref,
                 above_ref, below_ref, left_ref, right_ref, out_ref):
    size, lanes = inner_ref.shape[1], inner_ref.shape[2]
    block = pl.program_id(0)
    rows = lax.broadcasted_iota(jnp.int32, (size, lanes), 0)
    cols = lax.broadcasted_iota(jnp.int32, (size, lanes), 1)
    square = lax.broadcasted_iota(jnp.int32, (lanes, lanes), 0) == lax.broadcasted_iota(
        jnp.int32, (lanes, lanes), 1)

    def as_column(line):
        return jnp.concatenate(
            [
                jnp.sum(jnp.where(square, line[:, h * lanes:(h + 1) * lanes], 0.0), axis=1,
                        keepdims=True)
                for h in range(size // lanes)
            ],
            axis=0,
        )

    edge_col = jnp.where(block == 0, 0, lanes - 1)
    for s in range(inner_ref.shape[0] // 2):
        c0, c1 = 2 * s, 2 * s + 1
        north = _bend(above_ref[c0:c0 + 1] - top_ref[c0:c0 + 1], above_ref[c1:c1 + 1] - top_ref[c1:c1 + 1])
        south = _bend(below_ref[c0:c0 + 1] - bottom_ref[c0:c0 + 1],
                      below_ref[c1:c1 + 1] - bottom_ref[c1:c1 + 1])
        west = _bend(left_ref[c0:c0 + 1] - first_ref[c0:c0 + 1], left_ref[c1:c1 + 1] - first_ref[c1:c1 + 1])
        east = _bend(right_ref[c0:c0 + 1] - last_ref[c0:c0 + 1], right_ref[c1:c1 + 1] - last_ref[c1:c1 + 1])
        for part, c in ((0, c0), (1, c1)):
            side = as_column(jnp.where(block == 0, west[part], east[part]))
            extra = (
                jnp.where(rows == 0, north[part], 0.0)
                + jnp.where(rows == size - 1, south[part], 0.0)
                + jnp.where(cols == edge_col, side, 0.0)
            )
            out_ref[c] = inner_ref[c] + smooth_rate * extra


def smooth_update(field, total, edges, halos):
    channels, size, _ = field.shape
    plane = pl.BlockSpec((2, size, size), lambda s: (s, 0, 0))
    inner = pl.pallas_call(
        _inner_kernel,
        grid=(channels // 2,),
        in_specs=[plane, plane],
        out_specs=plane,
        out_shape=jax.ShapeDtypeStruct(field.shape, jnp.float32),
    )(field, total)
    lanes = 128
    half = pl.BlockSpec((channels, size, lanes), lambda b: (0, 0, b))
    row_part = pl.BlockSpec((channels, lanes), lambda b: (0, b))
    whole = pl.BlockSpec((channels, size), lambda b: (0, 0))
    return pl.pallas_call(
        _edge_kernel,
        grid=(size // lanes,),
        in_specs=[half, row_part, row_part, whole, whole, row_part, row_part, whole, whole],
        out_specs=half,
        out_shape=jax.ShapeDtypeStruct(field.shape, jnp.float32),
        input_output_aliases={0: 0},
    )(inner, *edges, *halos)


def block_tables(width):
    index = np.arange(width)
    angles = (index[:, None] * index[None, :] % width) * (2.0 * math.pi / width)
    scale = 1.0 / math.sqrt(width)
    cosine, sine = np.cos(angles) * scale, np.sin(angles) * scale
    plus = np.block([[cosine, -sine], [sine, cosine]])
    minus = np.block([[cosine, sine], [-sine, cosine]])
    lefts, rights = [], []
    for table in (plus, minus):
        high = table.astype(jnp.bfloat16)
        low = (table - high.astype(np.float64)).astype(jnp.bfloat16)
        lefts.append(np.concatenate([high, low, high], axis=1))
        rights.append(np.concatenate([high, low, high], axis=0))
    return jnp.asarray(np.stack(lefts)), jnp.asarray(np.stack(rights))


def _split(x):
    high = x.astype(jnp.bfloat16)
    low = (x - high.astype(jnp.float32)).astype(jnp.bfloat16)
    return high, low


def _dot(a, b):
    return jnp.dot(a, b, preferred_element_type=jnp.float32)


def _times(a, b):
    return (a[0] * b[0] - a[1] * b[1], a[0] * b[1] + a[1] * b[0])


def _conj_times(a, b):
    return (a[0] * b[0] + a[1] * b[1], a[0] * b[1] - a[1] * b[0])


def _transformer(left_ref, right_ref, group, width):
    def transform(pair, sign):
        first, second = (1, 0) if sign < 0 else (0, 1)
        stacked = jnp.concatenate(
            [jnp.concatenate([pair[0][g], pair[1][g]], axis=0) for g in range(group)], axis=1
        )
        high, low = _split(stacked)
        rows = _dot(left_ref[first], jnp.concatenate([high, high, low], axis=0))
        joined = jnp.concatenate(
            [
                jnp.concatenate(
                    [rows[:width, g * width:(g + 1) * width], rows[width:, g * width:(g + 1) * width]],
                    axis=1,
                )
                for g in range(group)
            ],
            axis=0,
        )
        high, low = _split(joined)
        out = _dot(jnp.concatenate([high, high, low], axis=1), right_ref[second])
        return (
            out[:, :width].reshape(group, width, width),
            out[:, width:].reshape(group, width, width),
        )

    return transform


def _layers(win_ref):
    slices = win_ref.shape[1] // 2
    return [
        (win_ref[:, 2 * s].astype(jnp.float32), win_ref[:, 2 * s + 1].astype(jnp.float32))
        for s in range(slices)
    ]


def _forward_kernel(win_ref, probe_ref, prop_ref, left_ref, right_ref, far_ref, inc_ref):
    group, width = win_ref.shape[0], probe_ref.shape[-1]
    transform = _transformer(left_ref, right_ref, group, width)
    layers = _layers(win_ref)
    probe = (probe_ref[0][None], probe_ref[1][None])
    kernel = (prop_ref[0][None], prop_ref[1][None])
    wave = _times(probe, layers[0])
    for s in range(1, len(layers)):
        moved = transform(_times(kernel, transform(wave, -1)), 1)
        inc_ref[:, 2 * (s - 1)] = moved[0]
        inc_ref[:, 2 * (s - 1) + 1] = moved[1]
        wave = _times(layers[s], moved)
    far = transform(wave, -1)
    far_ref[:, 0] = far[0]
    far_ref[:, 1] = far[1]


def _backward_kernel(
    target_ref, tops_ref, lefts_ref, amp_ref, far_ref, inc_ref, win_ref, probe_ref, prop_ref,
    left_ref, right_ref, border_ref, out_ref, edges_ref
):
    group, width = win_ref.shape[0], probe_ref.shape[-1]
    step = pl.program_id(0)
    transform = _transformer(left_ref, right_ref, group, width)
    layers = _layers(win_ref)
    slices = len(layers)
    probe = (probe_ref[0][None], probe_ref[1][None])
    kernel_conj = (prop_ref[0][None], -prop_ref[1][None])
    amplitude = jnp.stack(
        [amp_ref[target_ref[step * group + g]].astype(jnp.float32) for g in range(group)]
    )
    far = (far_ref[:, 0], far_ref[:, 1])
    magnitude = jnp.sqrt(far[0] * far[0] + far[1] * far[1] + 1.0)
    factor = 1.0 - amplitude / magnitude
    back = transform((far[0] * factor, far[1] * factor), 1)
    grads = [None] * slices
    for s in range(slices - 1, 0, -1):
        grads[s] = _conj_times((inc_ref[:, 2 * (s - 1)], inc_ref[:, 2 * (s - 1) + 1]), back)
        back = transform(_times(kernel_conj, transform(_conj_times(layers[s], back), -1)), 1)
    grads[0] = _conj_times(probe, back)
    planes = [part.astype(jnp.bfloat16) for pair in grads for part in pair]
    channels, tile = out_ref.shape[0], out_ref.shape[-1]
    down = lax.broadcasted_iota(jnp.int32, (tile, width), 0) - lax.broadcasted_iota(
        jnp.int32, (tile, width), 1)
    across = lax.broadcasted_iota(jnp.int32, (width, tile), 1) - lax.broadcasted_iota(
        jnp.int32, (width, tile), 0)
    placed, col_picks = [], []
    for g in range(group):
        top = tops_ref[step * group + g]
        left = lefts_ref[step * group + g]
        row_pick = (down == top).astype(jnp.bfloat16)
        col_picks.append((across == left).astype(jnp.bfloat16))
        stacked = jnp.concatenate([plane[g] for plane in planes], axis=1)
        placed.append(_dot(row_pick, stacked).astype(jnp.bfloat16))
    spread = jnp.concatenate(
        [
            jnp.concatenate([rows[:, c * width:(c + 1) * width] for rows in placed], axis=1)
            for c in range(channels)
        ],
        axis=0,
    )
    contribution = _dot(spread, jnp.concatenate(col_picks, axis=0)).reshape(channels, tile, tile)

    @pl.when(step == 0)
    def _():
        out_ref[...] = jnp.zeros_like(out_ref)

    out_ref[...] += contribution

    @pl.when(step == pl.num_programs(0) - 1)
    def _():
        lanes = lax.broadcasted_iota(jnp.int32, (8, tile), 1)
        which = jnp.where(lax.broadcasted_iota(jnp.int32, (8, tile), 0) == 0, 0, tile - 1)
        pick = (lanes == which).astype(jnp.bfloat16)
        for c in range(channels):
            plane = out_ref[c]
            edges_ref[0, c:c + 1, :] = border_ref[0, c:c + 1, :] - step_rate * plane[0:1, :]
            edges_ref[1, c:c + 1, :] = border_ref[1, c:c + 1, :] - step_rate * plane[tile - 1:tile, :]
            high = plane.astype(jnp.bfloat16)
            rest = plane - high.astype(jnp.float32)
            middle = rest.astype(jnp.bfloat16)
            low = (rest - middle.astype(jnp.float32)).astype(jnp.bfloat16)
            cols = None
            for part in (high, middle, low):
                term = lax.dot_general(
                    pick, part, (((1,), (1,)), ((), ())), preferred_element_type=jnp.float32
                )
                cols = term if cols is None else cols + term
            edges_ref[2, c:c + 1, :] = border_ref[2, c:c + 1, :] - step_rate * cols[0:1]
            edges_ref[3, c:c + 1, :] = border_ref[3, c:c + 1, :] - step_rate * cols[1:2]


def forward_waves(windows, probe, kernel, tables, group=8):
    count, channels, width, _ = windows.shape
    group = math.gcd(count, group)
    left_tables, right_tables = tables
    fixed = lambda k: (0, 0, 0)
    return pl.pallas_call(
        _forward_kernel,
        grid=(count // group,),
        in_specs=[
            pl.BlockSpec((group, channels, width, width), lambda k: (k, 0, 0, 0)),
            pl.BlockSpec((2, width, width), fixed),
            pl.BlockSpec((2, width, width), fixed),
            pl.BlockSpec(left_tables.shape, fixed),
            pl.BlockSpec(right_tables.shape, fixed),
        ],
        out_specs=[
            pl.BlockSpec((group, 2, width, width), lambda k: (k, 0, 0, 0)),
            pl.BlockSpec((group, channels - 2, width, width), lambda k: (k, 0, 0, 0)),
        ],
        out_shape=[
            jax.ShapeDtypeStruct((count, 2, width, width), jnp.float32),
            jax.ShapeDtypeStruct((count, channels - 2, width, width), jnp.float32),
        ],
    )(windows, probe, kernel, left_tables, right_tables)


def backward_gradients(target, tops, lefts, amplitudes, far, incoming, windows, probe, kernel,
                       tables, border, group=8):
    tile = border.shape[-1]
    count, channels, width, _ = windows.shape
    group = math.gcd(count, group)
    left_tables, right_tables = tables
    fixed = lambda k, *_: (0, 0, 0)
    batch = lambda k, *_: (k, 0, 0, 0)
    grid_spec = pltpu.PrefetchScalarGridSpec(
        num_scalar_prefetch=3,
        grid=(count // group,),
        in_specs=[
            pl.BlockSpec(memory_space=pltpu.VMEM),
            pl.BlockSpec((group, 2, width, width), batch),
            pl.BlockSpec((group, channels - 2, width, width), batch),
            pl.BlockSpec((group, channels, width, width), batch),
            pl.BlockSpec((2, width, width), fixed),
            pl.BlockSpec((2, width, width), fixed),
            pl.BlockSpec(left_tables.shape, fixed),
            pl.BlockSpec(right_tables.shape, fixed),
            pl.BlockSpec(border.shape, fixed),
        ],
        out_specs=[
            pl.BlockSpec((channels, tile, tile), fixed),
            pl.BlockSpec((4, channels, tile), fixed),
        ],
    )
    return pl.pallas_call(
        _backward_kernel,
        grid_spec=grid_spec,
        out_shape=[
            jax.ShapeDtypeStruct((channels, tile, tile), jnp.float32),
            jax.ShapeDtypeStruct((4, channels, tile), jnp.float32),
        ],
    )(target, tops, lefts, amplitudes, far, incoming, windows, probe, kernel, left_tables,
      right_tables, border)


def per_device(object_init, probe, propagator_phase, measured, corners, owner_column):
    width = probe.shape[-1]
    field = object_init
    tile = field.shape[1]
    capacity = measured.shape[3]
    columns = lax.axis_size("ty")
    tops = corners[0, 0, :, 0]
    lefts = corners[0, 0, :, 1]
    owner = owner_column[0, 0, :, 0]
    slot = slot_table(owner)
    target = jnp.clip(owner * capacity + slot, 0, columns * capacity - 1)
    gathered = lax.all_to_all(measured[0, 0], "ty", split_axis=0, concat_axis=0, tiled=True)
    gathered = gathered.reshape(columns * capacity, width, width)
    offsets = jnp.arange(width)
    cells = jnp.arange(tile)
    row_pick = (cells[None, None, :] == (tops[:, None, None] + offsets[None, :, None])).astype(
        jnp.bfloat16
    )
    col_pick = (cells[None, :, None] == (lefts[:, None, None] + offsets[None, None, :])).astype(
        jnp.bfloat16
    )
    field_low = field.astype(jnp.bfloat16)
    rows = jnp.einsum(
        "kir,crs->kcis", row_pick, field_low, preferred_element_type=jnp.float32
    ).astype(jnp.bfloat16)
    windows = jnp.einsum(
        "kcis,ksj->kcij", rows, col_pick, preferred_element_type=jnp.float32
    ).astype(jnp.bfloat16)
    tables = block_tables(width)
    kernel = jnp.stack([jnp.cos(propagator_phase), jnp.sin(propagator_phase)])
    far, incoming = forward_waves(windows, probe, kernel, tables)
    border = jnp.stack([field[:, 0, :], field[:, -1, :], field[:, :, 0], field[:, :, -1]])
    total, updated_edges = backward_gradients(
        target, tops, lefts, gathered, far, incoming, windows, probe, kernel, tables, border
    )
    edges = tuple(updated_edges[k] for k in range(4))
    halos = exchange_edges(*edges)
    return smooth_update(field, total, edges, halos)


def solution(mesh):
    placed = (
        P(None, "tx", "ty"),
        P(),
        P(),
        P("tx", "ty", None, None, None, None),
        P("tx", "ty", None, None),
        P("tx", "ty", None, None),
    )
    return jax.shard_map(
        per_device, mesh=mesh, in_specs=placed, out_specs=P(None, "tx", "ty"), check_vma=False
    )
```

```python
import math

import jax
import numpy as np
import jax.numpy as jnp
from jax import lax
from jax.experimental import pallas as pl
from jax.experimental.pallas import tpu as pltpu
from jax.sharding import PartitionSpec as P

step_rate = 0.5
smooth_rate = 0.2


def slot_table(owner):
    order = jnp.arange(owner.shape[0])
    same = owner[:, None] == owner[None, :]
    earlier = order[None, :] < order[:, None]
    return jnp.sum(jnp.where(same & earlier, 1, 0), axis=1).astype(jnp.int32)


def _swap_pairs(axis, first, last):
    size = lax.axis_size(axis)
    parity = lax.axis_index(axis) % 2
    even = [(i, i + 1) for i in range(0, size - 1, 2)] + [(i + 1, i) for i in range(0, size - 1, 2)]
    odd = [(i, i + 1) for i in range(1, size - 1, 2)] + [(i + 1, i) for i in range(1, size - 1, 2)]
    from_even = lax.ppermute(jnp.where(parity == 0, last, first), axis, even)
    from_odd = lax.ppermute(jnp.where(parity == 1, last, first), axis, odd)
    before = jnp.where(parity == 1, from_even, from_odd)
    after = jnp.where(parity == 0, from_even, from_odd)
    return before, after


def exchange_edges(top, bottom, first, last):
    above, below = _swap_pairs("tx", top, bottom)
    left, right = _swap_pairs("ty", first, last)
    return above, below, left, right


def _bend(real, imag):
    weight = 1.0 / jnp.sqrt(1.0 + real * real + imag * imag)
    return real * weight, imag * weight


def _inner_kernel(field_ref, total_ref, out_ref):
    size = field_ref.shape[-1]
    rows = lax.broadcasted_iota(jnp.int32, (size, size), 0)
    cols = lax.broadcasted_iota(jnp.int32, (size, size), 1)
    centers = [field_ref[p] - step_rate * total_ref[p] for p in range(2)]
    views = []
    for v in centers:
        views.append((
            jnp.where(rows == size - 1, v, pltpu.roll(v, size - 1, 0)),
            jnp.where(rows == 0, v, pltpu.roll(v, 1, 0)),
            jnp.where(cols == size - 1, v, pltpu.roll(v, size - 1, 1)),
            jnp.where(cols == 0, v, pltpu.roll(v, 1, 1)),
        ))
    total_r = jnp.zeros_like(centers[0])
    total_i = jnp.zeros_like(centers[1])
    for n in range(4):
        bent = _bend(views[0][n] - centers[0], views[1][n] - centers[1])
        total_r = total_r + bent[0]
        total_i = total_i + bent[1]
    out_ref[0] = centers[0] + smooth_rate * total_r
    out_ref[1] = centers[1] + smooth_rate * total_i


def _edge_kernel(inner_ref, top_ref, bottom_ref, first_ref, last_ref,
                 above_ref, below_ref, left_ref, right_ref, out_ref):
    size, lanes = inner_ref.shape[1], inner_ref.shape[2]
    block = pl.program_id(0)
    rows = lax.broadcasted_iota(jnp.int32, (size, lanes), 0)
    cols = lax.broadcasted_iota(jnp.int32, (size, lanes), 1)
    square = lax.broadcasted_iota(jnp.int32, (lanes, lanes), 0) == lax.broadcasted_iota(
        jnp.int32, (lanes, lanes), 1)

    def as_column(line):
        return jnp.concatenate(
            [
                jnp.sum(jnp.where(square, line[:, h * lanes:(h + 1) * lanes], 0.0), axis=1,
                        keepdims=True)
                for h in range(size // lanes)
            ],
            axis=0,
        )

    edge_col = jnp.where(block == 0, 0, lanes - 1)
    for s in range(inner_ref.shape[0] // 2):
        c0, c1 = 2 * s, 2 * s + 1
        north = _bend(above_ref[c0:c0 + 1] - top_ref[c0:c0 + 1], above_ref[c1:c1 + 1] - top_ref[c1:c1 + 1])
        south = _bend(below_ref[c0:c0 + 1] - bottom_ref[c0:c0 + 1],
                      below_ref[c1:c1 + 1] - bottom_ref[c1:c1 + 1])
        west = _bend(left_ref[c0:c0 + 1] - first_ref[c0:c0 + 1], left_ref[c1:c1 + 1] - first_ref[c1:c1 + 1])
        east = _bend(right_ref[c0:c0 + 1] - last_ref[c0:c0 + 1], right_ref[c1:c1 + 1] - last_ref[c1:c1 + 1])
        for part, c in ((0, c0), (1, c1)):
            side = as_column(jnp.where(block == 0, west[part], east[part]))
            extra = (
                jnp.where(rows == 0, north[part], 0.0)
                + jnp.where(rows == size - 1, south[part], 0.0)
                + jnp.where(cols == edge_col, side, 0.0)
            )
            out_ref[c] = inner_ref[c] + smooth_rate * extra


def smooth_update(field, total, edges, halos):
    channels, size, _ = field.shape
    plane = pl.BlockSpec((2, size, size), lambda s: (s, 0, 0))
    inner = pl.pallas_call(
        _inner_kernel,
        grid=(channels // 2,),
        in_specs=[plane, plane],
        out_specs=plane,
        out_shape=jax.ShapeDtypeStruct(field.shape, jnp.float32),
    )(field, total)
    lanes = 128
    half = pl.BlockSpec((channels, size, lanes), lambda b: (0, 0, b))
    row_part = pl.BlockSpec((channels, lanes), lambda b: (0, b))
    whole = pl.BlockSpec((channels, size), lambda b: (0, 0))
    return pl.pallas_call(
        _edge_kernel,
        grid=(size // lanes,),
        in_specs=[half, row_part, row_part, whole, whole, row_part, row_part, whole, whole],
        out_specs=half,
        out_shape=jax.ShapeDtypeStruct(field.shape, jnp.float32),
        input_output_aliases={0: 0},
    )(inner, *edges, *halos)


def block_tables(width):
    index = np.arange(width)
    angles = (index[:, None] * index[None, :] % width) * (2.0 * math.pi / width)
    scale = 1.0 / math.sqrt(width)
    cosine, sine = np.cos(angles) * scale, np.sin(angles) * scale
    plus = np.block([[cosine, -sine], [sine, cosine]])
    minus = np.block([[cosine, sine], [-sine, cosine]])
    lefts, rights = [], []
    for table in (plus, minus):
        high = table.astype(jnp.bfloat16)
        low = (table - high.astype(np.float64)).astype(jnp.bfloat16)
        lefts.append(np.concatenate([high, low, high], axis=1))
        rights.append(np.concatenate([high, low, high], axis=0))
    return jnp.asarray(np.stack(lefts)), jnp.asarray(np.stack(rights))


def _split(x):
    high = x.astype(jnp.bfloat16)
    low = (x - high.astype(jnp.float32)).astype(jnp.bfloat16)
    return high, low


def _dot(a, b):
    return jnp.dot(a, b, preferred_element_type=jnp.float32)


def _times(a, b):
    return (a[0] * b[0] - a[1] * b[1], a[0] * b[1] + a[1] * b[0])


def _conj_times(a, b):
    return (a[0] * b[0] + a[1] * b[1], a[0] * b[1] - a[1] * b[0])


def _transformer(left_ref, right_ref, group, width):
    def transform(pair, sign):
        first, second = (1, 0) if sign < 0 else (0, 1)
        stacked = jnp.concatenate(
            [jnp.concatenate([pair[0][g], pair[1][g]], axis=0) for g in range(group)], axis=1
        )
        high, low = _split(stacked)
        rows = _dot(left_ref[first], jnp.concatenate([high, high, low], axis=0))
        joined = jnp.concatenate(
            [
                jnp.concatenate(
                    [rows[:width, g * width:(g + 1) * width], rows[width:, g * width:(g + 1) * width]],
                    axis=1,
                )
                for g in range(group)
            ],
            axis=0,
        )
        high, low = _split(joined)
        out = _dot(jnp.concatenate([high, high, low], axis=1), right_ref[second])
        return (
            out[:, :width].reshape(group, width, width),
            out[:, width:].reshape(group, width, width),
        )

    return transform


def _layers(win_ref):
    slices = win_ref.shape[1] // 2
    return [
        (win_ref[:, 2 * s].astype(jnp.float32), win_ref[:, 2 * s + 1].astype(jnp.float32))
        for s in range(slices)
    ]


def _forward_kernel(win_ref, probe_ref, prop_ref, left_ref, right_ref, far_ref, inc_ref):
    group, width = win_ref.shape[0], probe_ref.shape[-1]
    transform = _transformer(left_ref, right_ref, group, width)
    layers = _layers(win_ref)
    probe = (probe_ref[0][None], probe_ref[1][None])
    kernel = (prop_ref[0][None], prop_ref[1][None])
    wave = _times(probe, layers[0])
    for s in range(1, len(layers)):
        moved = transform(_times(kernel, transform(wave, -1)), 1)
        inc_ref[:, 2 * (s - 1)] = moved[0]
        inc_ref[:, 2 * (s - 1) + 1] = moved[1]
        wave = _times(layers[s], moved)
    far = transform(wave, -1)
    far_ref[:, 0] = far[0]
    far_ref[:, 1] = far[1]


def _backward_kernel(
    target_ref, tops_ref, lefts_ref, amp_ref, far_ref, inc_ref, win_ref, probe_ref, prop_ref,
    left_ref, right_ref, out_ref, edges_ref
):
    group, width = win_ref.shape[0], probe_ref.shape[-1]
    step = pl.program_id(0)
    transform = _transformer(left_ref, right_ref, group, width)
    layers = _layers(win_ref)
    slices = len(layers)
    probe = (probe_ref[0][None], probe_ref[1][None])
    kernel_conj = (prop_ref[0][None], -prop_ref[1][None])
    amplitude = jnp.stack(
        [amp_ref[target_ref[step * group + g]].astype(jnp.float32) for g in range(group)]
    )
    far = (far_ref[:, 0], far_ref[:, 1])
    magnitude = jnp.sqrt(far[0] * far[0] + far[1] * far[1] + 1.0)
    factor = 1.0 - amplitude / magnitude
    back = transform((far[0] * factor, far[1] * factor), 1)
    grads = [None] * slices
    for s in range(slices - 1, 0, -1):
        grads[s] = _conj_times((inc_ref[:, 2 * (s - 1)], inc_ref[:, 2 * (s - 1) + 1]), back)
        back = transform(_times(kernel_conj, transform(_conj_times(layers[s], back), -1)), 1)
    grads[0] = _conj_times(probe, back)
    planes = [part.astype(jnp.bfloat16) for pair in grads for part in pair]
    channels, tile = out_ref.shape[0], out_ref.shape[-1]
    down = lax.broadcasted_iota(jnp.int32, (tile, width), 0) - lax.broadcasted_iota(
        jnp.int32, (tile, width), 1)
    across = lax.broadcasted_iota(jnp.int32, (width, tile), 1) - lax.broadcasted_iota(
        jnp.int32, (width, tile), 0)
    placed, col_picks = [], []
    for g in range(group):
        top = tops_ref[step * group + g]
        left = lefts_ref[step * group + g]
        row_pick = (down == top).astype(jnp.bfloat16)
        col_picks.append((across == left).astype(jnp.bfloat16))
        stacked = jnp.concatenate([plane[g] for plane in planes], axis=1)
        placed.append(_dot(row_pick, stacked).astype(jnp.bfloat16))
    spread = jnp.concatenate(
        [
            jnp.concatenate([rows[:, c * width:(c + 1) * width] for rows in placed], axis=1)
            for c in range(channels)
        ],
        axis=0,
    )
    contribution = _dot(spread, jnp.concatenate(col_picks, axis=0)).reshape(channels, tile, tile)

    @pl.when(step == 0)
    def _():
        out_ref[...] = jnp.zeros_like(out_ref)

    out_ref[...] += contribution

    @pl.when(step == pl.num_programs(0) - 1)
    def _():
        lanes = lax.broadcasted_iota(jnp.int32, (8, tile), 1)
        which = jnp.where(lax.broadcasted_iota(jnp.int32, (8, tile), 0) == 0, 0, tile - 1)
        pick = (lanes == which).astype(jnp.bfloat16)
        for c in range(channels):
            plane = out_ref[c]
            edges_ref[0, c:c + 1, :] = plane[0:1, :]
            edges_ref[1, c:c + 1, :] = plane[tile - 1:tile, :]
            high = plane.astype(jnp.bfloat16)
            rest = plane - high.astype(jnp.float32)
            middle = rest.astype(jnp.bfloat16)
            low = (rest - middle.astype(jnp.float32)).astype(jnp.bfloat16)
            cols = None
            for part in (high, middle, low):
                term = lax.dot_general(
                    pick, part, (((1,), (1,)), ((), ())), preferred_element_type=jnp.float32
                )
                cols = term if cols is None else cols + term
            edges_ref[2, c:c + 1, :] = cols[0:1]
            edges_ref[3, c:c + 1, :] = cols[1:2]


def forward_waves(windows, probe, kernel, tables, group=8):
    count, channels, width, _ = windows.shape
    group = math.gcd(count, group)
    left_tables, right_tables = tables
    fixed = lambda k: (0, 0, 0)
    return pl.pallas_call(
        _forward_kernel,
        grid=(count // group,),
        in_specs=[
            pl.BlockSpec((group, channels, width, width), lambda k: (k, 0, 0, 0)),
            pl.BlockSpec((2, width, width), fixed),
            pl.BlockSpec((2, width, width), fixed),
            pl.BlockSpec(left_tables.shape, fixed),
            pl.BlockSpec(right_tables.shape, fixed),
        ],
        out_specs=[
            pl.BlockSpec((group, 2, width, width), lambda k: (k, 0, 0, 0)),
            pl.BlockSpec((group, channels - 2, width, width), lambda k: (k, 0, 0, 0)),
        ],
        out_shape=[
            jax.ShapeDtypeStruct((count, 2, width, width), jnp.float32),
            jax.ShapeDtypeStruct((count, channels - 2, width, width), jnp.float32),
        ],
    )(windows, probe, kernel, left_tables, right_tables)


def backward_gradients(target, tops, lefts, amplitudes, far, incoming, windows, probe, kernel,
                       tables, tile, group=8):
    count, channels, width, _ = windows.shape
    group = math.gcd(count, group)
    left_tables, right_tables = tables
    fixed = lambda k, *_: (0, 0, 0)
    batch = lambda k, *_: (k, 0, 0, 0)
    grid_spec = pltpu.PrefetchScalarGridSpec(
        num_scalar_prefetch=3,
        grid=(count // group,),
        in_specs=[
            pl.BlockSpec(amplitudes.shape, fixed),
            pl.BlockSpec((group, 2, width, width), batch),
            pl.BlockSpec((group, channels - 2, width, width), batch),
            pl.BlockSpec((group, channels, width, width), batch),
            pl.BlockSpec((2, width, width), fixed),
            pl.BlockSpec((2, width, width), fixed),
            pl.BlockSpec(left_tables.shape, fixed),
            pl.BlockSpec(right_tables.shape, fixed),
        ],
        out_specs=[
            pl.BlockSpec((channels, tile, tile), fixed),
            pl.BlockSpec((4, channels, tile), fixed),
        ],
    )
    return pl.pallas_call(
        _backward_kernel,
        grid_spec=grid_spec,
        out_shape=[
            jax.ShapeDtypeStruct((channels, tile, tile), jnp.float32),
            jax.ShapeDtypeStruct((4, channels, tile), jnp.float32),
        ],
    )(target, tops, lefts, amplitudes, far, incoming, windows, probe, kernel, left_tables,
      right_tables)


def per_device(object_init, probe, propagator_phase, measured, corners, owner_column):
    width = probe.shape[-1]
    field = object_init
    tile = field.shape[1]
    capacity = measured.shape[3]
    columns = lax.axis_size("ty")
    tops = corners[0, 0, :, 0]
    lefts = corners[0, 0, :, 1]
    owner = owner_column[0, 0, :, 0]
    slot = slot_table(owner)
    target = jnp.clip(owner * capacity + slot, 0, columns * capacity - 1)
    gathered = lax.all_to_all(measured[0, 0], "ty", split_axis=0, concat_axis=0, tiled=True)
    gathered = gathered.reshape(columns * capacity, width, width)
    offsets = jnp.arange(width)
    cells = jnp.arange(tile)
    row_pick = (cells[None, None, :] == (tops[:, None, None] + offsets[None, :, None])).astype(
        jnp.bfloat16
    )
    col_pick = (cells[None, :, None] == (lefts[:, None, None] + offsets[None, None, :])).astype(
        jnp.bfloat16
    )
    field_low = field.astype(jnp.bfloat16)
    rows = jnp.einsum(
        "kir,crs->kcis", row_pick, field_low, preferred_element_type=jnp.float32
    ).astype(jnp.bfloat16)
    windows = jnp.einsum(
        "kcis,ksj->kcij", rows, col_pick, preferred_element_type=jnp.float32
    ).astype(jnp.bfloat16)
    tables = block_tables(width)
    kernel = jnp.stack([jnp.cos(propagator_phase), jnp.sin(propagator_phase)])
    far, incoming = forward_waves(windows, probe, kernel, tables)
    total, total_edges = backward_gradients(
        target, tops, lefts, gathered, far, incoming, windows, probe, kernel, tables, tile
    )
    edges = (
        field[:, 0, :] - step_rate * total_edges[0],
        field[:, -1, :] - step_rate * total_edges[1],
        field[:, :, 0] - step_rate * total_edges[2],
        field[:, :, -1] - step_rate * total_edges[3],
    )
    halos = exchange_edges(*edges)
    return smooth_update(field, total, edges, halos)


def solution(mesh):
    placed = (
        P(None, "tx", "ty"),
        P(),
        P(),
        P("tx", "ty", None, None, None, None),
        P("tx", "ty", None, None),
        P("tx", "ty", None, None),
    )
    return jax.shard_map(
        per_device, mesh=mesh, in_specs=placed, out_specs=P(None, "tx", "ty"), check_vma=False
    )
```

```python
import math

import jax
import numpy as np
import jax.numpy as jnp
from jax import lax
from jax.experimental import pallas as pl
from jax.experimental.pallas import tpu as pltpu
from jax.sharding import PartitionSpec as P

step_rate = 0.5
smooth_rate = 0.2


def slot_table(owner):
    order = jnp.arange(owner.shape[0])
    same = owner[:, None] == owner[None, :]
    earlier = order[None, :] < order[:, None]
    return jnp.sum(jnp.where(same & earlier, 1, 0), axis=1).astype(jnp.int32)


def _swap(axis, even_payload, odd_payload):
    size = lax.axis_size(axis)
    even = [(i, i + 1) for i in range(0, size - 1, 2)] + [(i + 1, i) for i in range(0, size - 1, 2)]
    odd = [(i, i + 1) for i in range(1, size - 1, 2)] + [(i + 1, i) for i in range(1, size - 1, 2)]
    return lax.ppermute(even_payload, axis, even), lax.ppermute(odd_payload, axis, odd)


def _bend(real, imag):
    weight = 1.0 / jnp.sqrt(1.0 + real * real + imag * imag)
    return real * weight, imag * weight


def _inner_kernel(field_ref, total_ref, out_ref):
    size = field_ref.shape[-1]
    rows = lax.broadcasted_iota(jnp.int32, (size, size), 0)
    cols = lax.broadcasted_iota(jnp.int32, (size, size), 1)
    centers = [field_ref[p] - step_rate * total_ref[p] for p in range(2)]
    views = []
    for v in centers:
        views.append((
            jnp.where(rows == size - 1, v, pltpu.roll(v, size - 1, 0)),
            jnp.where(rows == 0, v, pltpu.roll(v, 1, 0)),
            jnp.where(cols == size - 1, v, pltpu.roll(v, size - 1, 1)),
            jnp.where(cols == 0, v, pltpu.roll(v, 1, 1)),
        ))
    total_r = jnp.zeros_like(centers[0])
    total_i = jnp.zeros_like(centers[1])
    for n in range(4):
        bent = _bend(views[0][n] - centers[0], views[1][n] - centers[1])
        total_r = total_r + bent[0]
        total_i = total_i + bent[1]
    out_ref[0] = centers[0] + smooth_rate * total_r
    out_ref[1] = centers[1] + smooth_rate * total_i


def _edge_kernel(parity_ref, inner_ref, row_even_ref, row_odd_ref, col_even_ref, col_odd_ref,
                 got_row_even_ref, got_row_odd_ref, got_col_even_ref, got_col_odd_ref, out_ref):
    size, lanes = inner_ref.shape[1], inner_ref.shape[2]
    block = pl.program_id(0)
    row_parity = parity_ref[0]
    col_parity = parity_ref[1]
    row_even, row_odd = row_even_ref[...], row_odd_ref[...]
    col_even, col_odd = col_even_ref[...], col_odd_ref[...]
    got_row_even, got_row_odd = got_row_even_ref[...], got_row_odd_ref[...]
    got_col_even, got_col_odd = got_col_even_ref[...], got_col_odd_ref[...]
    top = jnp.where(row_parity == 0, row_odd, row_even)
    bottom = jnp.where(row_parity == 0, row_even, row_odd)
    first = jnp.where(col_parity == 0, col_odd, col_even)
    last = jnp.where(col_parity == 0, col_even, col_odd)
    above = jnp.where(row_parity == 1, got_row_even, got_row_odd)
    below = jnp.where(row_parity == 0, got_row_even, got_row_odd)
    left = jnp.where(col_parity == 1, got_col_even, got_col_odd)
    right = jnp.where(col_parity == 0, got_col_even, got_col_odd)
    rows = lax.broadcasted_iota(jnp.int32, (size, lanes), 0)
    cols = lax.broadcasted_iota(jnp.int32, (size, lanes), 1)
    square = lax.broadcasted_iota(jnp.int32, (lanes, lanes), 0) == lax.broadcasted_iota(
        jnp.int32, (lanes, lanes), 1)

    def as_column(line):
        return jnp.concatenate(
            [
                jnp.sum(jnp.where(square, line[:, h * lanes:(h + 1) * lanes], 0.0), axis=1,
                        keepdims=True)
                for h in range(size // lanes)
            ],
            axis=0,
        )

    edge_col = jnp.where(block == 0, 0, lanes - 1)
    for s in range(inner_ref.shape[0] // 2):
        c0, c1 = 2 * s, 2 * s + 1
        north = _bend(above[c0:c0 + 1] - top[c0:c0 + 1], above[c1:c1 + 1] - top[c1:c1 + 1])
        south = _bend(below[c0:c0 + 1] - bottom[c0:c0 + 1],
                      below[c1:c1 + 1] - bottom[c1:c1 + 1])
        west = _bend(left[c0:c0 + 1] - first[c0:c0 + 1], left[c1:c1 + 1] - first[c1:c1 + 1])
        east = _bend(right[c0:c0 + 1] - last[c0:c0 + 1], right[c1:c1 + 1] - last[c1:c1 + 1])
        for part, c in ((0, c0), (1, c1)):
            side = as_column(jnp.where(block == 0, west[part], east[part]))
            extra = (
                jnp.where(rows == 0, north[part], 0.0)
                + jnp.where(rows == size - 1, south[part], 0.0)
                + jnp.where(cols == edge_col, side, 0.0)
            )
            out_ref[c] = inner_ref[c] + smooth_rate * extra


def smooth_update(field, total, parity, payloads, received):
    channels, size, _ = field.shape
    plane = pl.BlockSpec((2, size, size), lambda s: (s, 0, 0))
    inner = pl.pallas_call(
        _inner_kernel,
        grid=(channels // 2,),
        in_specs=[plane, plane],
        out_specs=plane,
        out_shape=jax.ShapeDtypeStruct(field.shape, jnp.float32),
    )(field, total)
    lanes = 128
    half = pl.BlockSpec((channels, size, lanes), lambda b: (0, 0, b))
    row_part = pl.BlockSpec((channels, lanes), lambda b: (0, b))
    whole = pl.BlockSpec((channels, size), lambda b: (0, 0))
    scalars = pl.BlockSpec(memory_space=pltpu.SMEM)
    return pl.pallas_call(
        _edge_kernel,
        grid=(size // lanes,),
        in_specs=[scalars, half, row_part, row_part, whole, whole, row_part, row_part, whole, whole],
        out_specs=half,
        out_shape=jax.ShapeDtypeStruct(field.shape, jnp.float32),
        input_output_aliases={1: 0},
    )(parity, inner, *payloads, *received)


def block_tables(width):
    index = np.arange(width)
    angles = (index[:, None] * index[None, :] % width) * (2.0 * math.pi / width)
    scale = 1.0 / math.sqrt(width)
    cosine, sine = np.cos(angles) * scale, np.sin(angles) * scale
    plus = np.block([[cosine, -sine], [sine, cosine]])
    minus = np.block([[cosine, sine], [-sine, cosine]])
    lefts, rights = [], []
    for table in (plus, minus):
        high = table.astype(jnp.bfloat16)
        low = (table - high.astype(np.float64)).astype(jnp.bfloat16)
        lefts.append(np.concatenate([high, low, high], axis=1))
        rights.append(np.concatenate([high, low, high], axis=0))
    return jnp.asarray(np.stack(lefts)), jnp.asarray(np.stack(rights))


def _split(x):
    high = x.astype(jnp.bfloat16)
    low = (x - high.astype(jnp.float32)).astype(jnp.bfloat16)
    return high, low


def _dot(a, b):
    return jnp.dot(a, b, preferred_element_type=jnp.float32)


def _times(a, b):
    return (a[0] * b[0] - a[1] * b[1], a[0] * b[1] + a[1] * b[0])


def _conj_times(a, b):
    return (a[0] * b[0] + a[1] * b[1], a[0] * b[1] - a[1] * b[0])


def _transformer(left_ref, right_ref, group, width):
    def transform(pair, sign):
        first, second = (1, 0) if sign < 0 else (0, 1)
        stacked = jnp.concatenate(
            [jnp.concatenate([pair[0][g], pair[1][g]], axis=0) for g in range(group)], axis=1
        )
        high, low = _split(stacked)
        rows = _dot(left_ref[first], jnp.concatenate([high, high, low], axis=0))
        joined = jnp.concatenate(
            [
                jnp.concatenate(
                    [rows[:width, g * width:(g + 1) * width], rows[width:, g * width:(g + 1) * width]],
                    axis=1,
                )
                for g in range(group)
            ],
            axis=0,
        )
        high, low = _split(joined)
        out = _dot(jnp.concatenate([high, high, low], axis=1), right_ref[second])
        return (
            out[:, :width].reshape(group, width, width),
            out[:, width:].reshape(group, width, width),
        )

    return transform


def _layers(win_ref):
    slices = win_ref.shape[1] // 2
    return [
        (win_ref[:, 2 * s].astype(jnp.float32), win_ref[:, 2 * s + 1].astype(jnp.float32))
        for s in range(slices)
    ]


def _forward_kernel(win_ref, probe_ref, prop_ref, left_ref, right_ref, far_ref, inc_ref):
    group, width = win_ref.shape[0], probe_ref.shape[-1]
    transform = _transformer(left_ref, right_ref, group, width)
    layers = _layers(win_ref)
    probe = (probe_ref[0][None], probe_ref[1][None])
    kernel = (prop_ref[0][None], prop_ref[1][None])
    wave = _times(probe, layers[0])
    for s in range(1, len(layers)):
        moved = transform(_times(kernel, transform(wave, -1)), 1)
        inc_ref[:, 2 * (s - 1)] = moved[0]
        inc_ref[:, 2 * (s - 1) + 1] = moved[1]
        wave = _times(layers[s], moved)
    far = transform(wave, -1)
    far_ref[:, 0] = far[0]
    far_ref[:, 1] = far[1]


def _backward_kernel(
    target_ref, tops_ref, lefts_ref, parity_ref, amp_ref, far_ref, inc_ref, win_ref, probe_ref,
    prop_ref, left_ref, right_ref, border_ref, out_ref, row_even_ref, row_odd_ref, col_even_ref,
    col_odd_ref
):
    group, width = win_ref.shape[0], probe_ref.shape[-1]
    step = pl.program_id(0)
    transform = _transformer(left_ref, right_ref, group, width)
    layers = _layers(win_ref)
    slices = len(layers)
    probe = (probe_ref[0][None], probe_ref[1][None])
    kernel_conj = (prop_ref[0][None], -prop_ref[1][None])
    amplitude = jnp.stack(
        [amp_ref[target_ref[step * group + g]].astype(jnp.float32) for g in range(group)]
    )
    far = (far_ref[:, 0], far_ref[:, 1])
    magnitude = jnp.sqrt(far[0] * far[0] + far[1] * far[1] + 1.0)
    factor = 1.0 - amplitude / magnitude
    back = transform((far[0] * factor, far[1] * factor), 1)
    grads = [None] * slices
    for s in range(slices - 1, 0, -1):
        grads[s] = _conj_times((inc_ref[:, 2 * (s - 1)], inc_ref[:, 2 * (s - 1) + 1]), back)
        back = transform(_times(kernel_conj, transform(_conj_times(layers[s], back), -1)), 1)
    grads[0] = _conj_times(probe, back)
    planes = [part.astype(jnp.bfloat16) for pair in grads for part in pair]
    channels, tile = out_ref.shape[0], out_ref.shape[-1]
    down = lax.broadcasted_iota(jnp.int32, (tile, width), 0) - lax.broadcasted_iota(
        jnp.int32, (tile, width), 1)
    across = lax.broadcasted_iota(jnp.int32, (width, tile), 1) - lax.broadcasted_iota(
        jnp.int32, (width, tile), 0)
    placed, col_picks = [], []
    for g in range(group):
        top = tops_ref[step * group + g]
        left = lefts_ref[step * group + g]
        row_pick = (down == top).astype(jnp.bfloat16)
        col_picks.append((across == left).astype(jnp.bfloat16))
        stacked = jnp.concatenate([plane[g] for plane in planes], axis=1)
        placed.append(_dot(row_pick, stacked).astype(jnp.bfloat16))
    spread = jnp.concatenate(
        [
            jnp.concatenate([rows[:, c * width:(c + 1) * width] for rows in placed], axis=1)
            for c in range(channels)
        ],
        axis=0,
    )
    contribution = _dot(spread, jnp.concatenate(col_picks, axis=0)).reshape(channels, tile, tile)

    @pl.when(step == 0)
    def _():
        out_ref[...] = jnp.zeros_like(out_ref)

    out_ref[...] += contribution

    @pl.when(step == pl.num_programs(0) - 1)
    def _():
        lanes = lax.broadcasted_iota(jnp.int32, (8, tile), 1)
        which = jnp.where(lax.broadcasted_iota(jnp.int32, (8, tile), 0) == 0, 0, tile - 1)
        pick = (lanes == which).astype(jnp.bfloat16)
        row_parity = parity_ref[0]
        col_parity = parity_ref[1]
        for c in range(channels):
            plane = out_ref[c]
            top = border_ref[0, c:c + 1, :] - step_rate * plane[0:1, :]
            bottom = border_ref[1, c:c + 1, :] - step_rate * plane[tile - 1:tile, :]
            row_even_ref[c:c + 1, :] = jnp.where(row_parity == 0, bottom, top)
            row_odd_ref[c:c + 1, :] = jnp.where(row_parity == 1, bottom, top)
            high = plane.astype(jnp.bfloat16)
            rest = plane - high.astype(jnp.float32)
            middle = rest.astype(jnp.bfloat16)
            low = (rest - middle.astype(jnp.float32)).astype(jnp.bfloat16)
            cols = None
            for part in (high, middle, low):
                term = lax.dot_general(
                    pick, part, (((1,), (1,)), ((), ())), preferred_element_type=jnp.float32
                )
                cols = term if cols is None else cols + term
            first = border_ref[2, c:c + 1, :] - step_rate * cols[0:1]
            last = border_ref[3, c:c + 1, :] - step_rate * cols[1:2]
            col_even_ref[c:c + 1, :] = jnp.where(col_parity == 0, last, first)
            col_odd_ref[c:c + 1, :] = jnp.where(col_parity == 1, last, first)


def forward_waves(windows, probe, kernel, tables, group=8):
    count, channels, width, _ = windows.shape
    group = math.gcd(count, group)
    left_tables, right_tables = tables
    fixed = lambda k: (0, 0, 0)
    return pl.pallas_call(
        _forward_kernel,
        grid=(count // group,),
        in_specs=[
            pl.BlockSpec((group, channels, width, width), lambda k: (k, 0, 0, 0)),
            pl.BlockSpec((2, width, width), fixed),
            pl.BlockSpec((2, width, width), fixed),
            pl.BlockSpec(left_tables.shape, fixed),
            pl.BlockSpec(right_tables.shape, fixed),
        ],
        out_specs=[
            pl.BlockSpec((group, 2, width, width), lambda k: (k, 0, 0, 0)),
            pl.BlockSpec((group, channels - 2, width, width), lambda k: (k, 0, 0, 0)),
        ],
        out_shape=[
            jax.ShapeDtypeStruct((count, 2, width, width), jnp.float32),
            jax.ShapeDtypeStruct((count, channels - 2, width, width), jnp.float32),
        ],
    )(windows, probe, kernel, left_tables, right_tables)


def backward_gradients(target, tops, lefts, parity, amplitudes, far, incoming, windows, probe,
                       kernel, tables, border, group=8):
    count, channels, width, _ = windows.shape
    tile = border.shape[-1]
    group = math.gcd(count, group)
    left_tables, right_tables = tables
    fixed = lambda k, *_: (0, 0, 0)
    batch = lambda k, *_: (k, 0, 0, 0)
    line = pl.BlockSpec((channels, tile), lambda k, *_: (0, 0))
    grid_spec = pltpu.PrefetchScalarGridSpec(
        num_scalar_prefetch=4,
        grid=(count // group,),
        in_specs=[
            pl.BlockSpec(amplitudes.shape, fixed),
            pl.BlockSpec((group, 2, width, width), batch),
            pl.BlockSpec((group, channels - 2, width, width), batch),
            pl.BlockSpec((group, channels, width, width), batch),
            pl.BlockSpec((2, width, width), fixed),
            pl.BlockSpec((2, width, width), fixed),
            pl.BlockSpec(left_tables.shape, fixed),
            pl.BlockSpec(right_tables.shape, fixed),
            pl.BlockSpec(border.shape, fixed),
        ],
        out_specs=[pl.BlockSpec((channels, tile, tile), fixed), line, line, line, line],
    )
    edge = jax.ShapeDtypeStruct((channels, tile), jnp.float32)
    return pl.pallas_call(
        _backward_kernel,
        grid_spec=grid_spec,
        out_shape=[jax.ShapeDtypeStruct((channels, tile, tile), jnp.float32), edge, edge, edge, edge],
    )(target, tops, lefts, parity, amplitudes, far, incoming, windows, probe, kernel, left_tables,
      right_tables, border)


def per_device(object_init, probe, propagator_phase, measured, corners, owner_column):
    width = probe.shape[-1]
    field = object_init
    tile = field.shape[1]
    capacity = measured.shape[3]
    columns = lax.axis_size("ty")
    tops = corners[0, 0, :, 0]
    lefts = corners[0, 0, :, 1]
    owner = owner_column[0, 0, :, 0]
    slot = slot_table(owner)
    target = jnp.clip(owner * capacity + slot, 0, columns * capacity - 1)
    gathered = lax.all_to_all(measured[0, 0], "ty", split_axis=0, concat_axis=0, tiled=True)
    gathered = gathered.reshape(columns * capacity, width, width)
    offsets = jnp.arange(width)
    cells = jnp.arange(tile)
    row_pick = (cells[None, None, :] == (tops[:, None, None] + offsets[None, :, None])).astype(
        jnp.bfloat16
    )
    col_pick = (cells[None, :, None] == (lefts[:, None, None] + offsets[None, None, :])).astype(
        jnp.bfloat16
    )
    field_low = field.astype(jnp.bfloat16)
    rows = jnp.einsum(
        "kir,crs->kcis", row_pick, field_low, preferred_element_type=jnp.float32
    ).astype(jnp.bfloat16)
    windows = jnp.einsum(
        "kcis,ksj->kcij", rows, col_pick, preferred_element_type=jnp.float32
    ).astype(jnp.bfloat16)
    tables = block_tables(width)
    kernel = jnp.stack([jnp.cos(propagator_phase), jnp.sin(propagator_phase)])
    far, incoming = forward_waves(windows, probe, kernel, tables)
    parity = jnp.stack([lax.axis_index("tx") % 2, lax.axis_index("ty") % 2]).astype(jnp.int32)
    border = jnp.stack([field[:, 0, :], field[:, -1, :], field[:, :, 0], field[:, :, -1]])
    total, *payloads = backward_gradients(
        target, tops, lefts, parity, gathered, far, incoming, windows, probe, kernel, tables, border
    )
    received = _swap("tx", payloads[0], payloads[1]) + _swap("ty", payloads[2], payloads[3])
    return smooth_update(field, total, parity, payloads, received)


def solution(mesh):
    placed = (
        P(None, "tx", "ty"),
        P(),
        P(),
        P("tx", "ty", None, None, None, None),
        P("tx", "ty", None, None),
        P("tx", "ty", None, None),
    )
    return jax.shard_map(
        per_device, mesh=mesh, in_specs=placed, out_specs=P(None, "tx", "ty"), check_vma=False
    )
```

```python
import math

import jax
import numpy as np
import jax.numpy as jnp
from jax import lax
from jax.experimental import pallas as pl
from jax.experimental.pallas import tpu as pltpu
from jax.sharding import PartitionSpec as P

step_rate = 0.5
smooth_rate = 0.2


def slot_table(owner):
    order = jnp.arange(owner.shape[0])
    same = owner[:, None] == owner[None, :]
    earlier = order[None, :] < order[:, None]
    return jnp.sum(jnp.where(same & earlier, 1, 0), axis=1).astype(jnp.int32)


def _swap(axis, even_payload, odd_payload):
    size = lax.axis_size(axis)
    even = [(i, i + 1) for i in range(0, size - 1, 2)] + [(i + 1, i) for i in range(0, size - 1, 2)]
    odd = [(i, i + 1) for i in range(1, size - 1, 2)] + [(i + 1, i) for i in range(1, size - 1, 2)]
    return lax.ppermute(even_payload, axis, even), lax.ppermute(odd_payload, axis, odd)


def _bend(real, imag):
    weight = 1.0 / jnp.sqrt(1.0 + real * real + imag * imag)
    return real * weight, imag * weight


def _inner_kernel(field_ref, total_ref, out_ref):
    size = field_ref.shape[-1]
    rows = lax.broadcasted_iota(jnp.int32, (size, size), 0)
    cols = lax.broadcasted_iota(jnp.int32, (size, size), 1)
    centers = [field_ref[p] - step_rate * total_ref[p] for p in range(2)]
    views = []
    for v in centers:
        views.append((
            jnp.where(rows == size - 1, v, pltpu.roll(v, size - 1, 0)),
            jnp.where(rows == 0, v, pltpu.roll(v, 1, 0)),
            jnp.where(cols == size - 1, v, pltpu.roll(v, size - 1, 1)),
            jnp.where(cols == 0, v, pltpu.roll(v, 1, 1)),
        ))
    total_r = jnp.zeros_like(centers[0])
    total_i = jnp.zeros_like(centers[1])
    for n in range(4):
        bent = _bend(views[0][n] - centers[0], views[1][n] - centers[1])
        total_r = total_r + bent[0]
        total_i = total_i + bent[1]
    out_ref[0] = centers[0] + smooth_rate * total_r
    out_ref[1] = centers[1] + smooth_rate * total_i


def _edge_kernel(parity_ref, inner_ref, row_even_ref, row_odd_ref, col_even_ref, col_odd_ref,
                 got_row_even_ref, got_row_odd_ref, got_col_even_ref, got_col_odd_ref, out_ref):
    size, lanes = inner_ref.shape[1], inner_ref.shape[2]
    block = pl.program_id(0)
    row_parity = parity_ref[parity_ref.shape[0] - 2]
    col_parity = parity_ref[parity_ref.shape[0] - 1]
    row_even, row_odd = row_even_ref[...], row_odd_ref[...]
    col_even, col_odd = col_even_ref[...], col_odd_ref[...]
    got_row_even, got_row_odd = got_row_even_ref[...], got_row_odd_ref[...]
    got_col_even, got_col_odd = got_col_even_ref[...], got_col_odd_ref[...]
    top = jnp.where(row_parity == 0, row_odd, row_even)
    bottom = jnp.where(row_parity == 0, row_even, row_odd)
    first = jnp.where(col_parity == 0, col_odd, col_even)
    last = jnp.where(col_parity == 0, col_even, col_odd)
    above = jnp.where(row_parity == 1, got_row_even, got_row_odd)
    below = jnp.where(row_parity == 0, got_row_even, got_row_odd)
    left = jnp.where(col_parity == 1, got_col_even, got_col_odd)
    right = jnp.where(col_parity == 0, got_col_even, got_col_odd)
    rows = lax.broadcasted_iota(jnp.int32, (size, lanes), 0)
    cols = lax.broadcasted_iota(jnp.int32, (size, lanes), 1)
    square = lax.broadcasted_iota(jnp.int32, (lanes, lanes), 0) == lax.broadcasted_iota(
        jnp.int32, (lanes, lanes), 1)

    def as_column(line):
        return jnp.concatenate(
            [
                jnp.sum(jnp.where(square, line[:, h * lanes:(h + 1) * lanes], 0.0), axis=1,
                        keepdims=True)
                for h in range(size // lanes)
            ],
            axis=0,
        )

    edge_col = jnp.where(block == 0, 0, lanes - 1)
    for s in range(inner_ref.shape[0] // 2):
        c0, c1 = 2 * s, 2 * s + 1
        north = _bend(above[c0:c0 + 1] - top[c0:c0 + 1], above[c1:c1 + 1] - top[c1:c1 + 1])
        south = _bend(below[c0:c0 + 1] - bottom[c0:c0 + 1],
                      below[c1:c1 + 1] - bottom[c1:c1 + 1])
        west = _bend(left[c0:c0 + 1] - first[c0:c0 + 1], left[c1:c1 + 1] - first[c1:c1 + 1])
        east = _bend(right[c0:c0 + 1] - last[c0:c0 + 1], right[c1:c1 + 1] - last[c1:c1 + 1])
        for part, c in ((0, c0), (1, c1)):
            side = as_column(jnp.where(block == 0, west[part], east[part]))
            extra = (
                jnp.where(rows == 0, north[part], 0.0)
                + jnp.where(rows == size - 1, south[part], 0.0)
                + jnp.where(cols == edge_col, side, 0.0)
            )
            out_ref[c] = inner_ref[c] + smooth_rate * extra


def smooth_update(field, total, parity, payloads, received):
    channels, size, _ = field.shape
    plane = pl.BlockSpec((2, size, size), lambda s: (s, 0, 0))
    inner = pl.pallas_call(
        _inner_kernel,
        grid=(channels // 2,),
        in_specs=[plane, plane],
        out_specs=plane,
        out_shape=jax.ShapeDtypeStruct(field.shape, jnp.float32),
    )(field, total)
    lanes = 128
    half = pl.BlockSpec((channels, size, lanes), lambda b: (0, 0, b))
    row_part = pl.BlockSpec((channels, lanes), lambda b: (0, b))
    whole = pl.BlockSpec((channels, size), lambda b: (0, 0))
    scalars = pl.BlockSpec(memory_space=pltpu.SMEM)
    return pl.pallas_call(
        _edge_kernel,
        grid=(size // lanes,),
        in_specs=[scalars, half, row_part, row_part, whole, whole, row_part, row_part, whole, whole],
        out_specs=half,
        out_shape=jax.ShapeDtypeStruct(field.shape, jnp.float32),
        input_output_aliases={1: 0},
    )(parity, inner, *payloads, *received)


def block_tables(width):
    index = np.arange(width)
    angles = (index[:, None] * index[None, :] % width) * (2.0 * math.pi / width)
    scale = 1.0 / math.sqrt(width)
    cosine, sine = np.cos(angles) * scale, np.sin(angles) * scale
    plus = np.block([[cosine, -sine], [sine, cosine]])
    minus = np.block([[cosine, sine], [-sine, cosine]])
    lefts, rights = [], []
    for table in (plus, minus):
        high = table.astype(jnp.bfloat16)
        low = (table - high.astype(np.float64)).astype(jnp.bfloat16)
        lefts.append(np.concatenate([high, low, high], axis=1))
        rights.append(np.concatenate([high, low, high], axis=0))
    return jnp.asarray(np.stack(lefts)), jnp.asarray(np.stack(rights))


def _split(x):
    high = x.astype(jnp.bfloat16)
    low = (x - high.astype(jnp.float32)).astype(jnp.bfloat16)
    return high, low


def _dot(a, b):
    return jnp.dot(a, b, preferred_element_type=jnp.float32)


def _times(a, b):
    return (a[0] * b[0] - a[1] * b[1], a[0] * b[1] + a[1] * b[0])


def _conj_times(a, b):
    return (a[0] * b[0] + a[1] * b[1], a[0] * b[1] - a[1] * b[0])


def _transformer(left_ref, right_ref, group, width):
    def transform(pair, sign):
        first, second = (1, 0) if sign < 0 else (0, 1)
        stacked = jnp.concatenate(
            [jnp.concatenate([pair[0][g], pair[1][g]], axis=0) for g in range(group)], axis=1
        )
        high, low = _split(stacked)
        rows = _dot(left_ref[first], jnp.concatenate([high, high, low], axis=0))
        joined = jnp.concatenate(
            [
                jnp.concatenate(
                    [rows[:width, g * width:(g + 1) * width], rows[width:, g * width:(g + 1) * width]],
                    axis=1,
                )
                for g in range(group)
            ],
            axis=0,
        )
        high, low = _split(joined)
        out = _dot(jnp.concatenate([high, high, low], axis=1), right_ref[second])
        return (
            out[:, :width].reshape(group, width, width),
            out[:, width:].reshape(group, width, width),
        )

    return transform


def _layers(win_ref):
    slices = win_ref.shape[1] // 2
    return [
        (win_ref[:, 2 * s].astype(jnp.float32), win_ref[:, 2 * s + 1].astype(jnp.float32))
        for s in range(slices)
    ]


def _forward_kernel(win_ref, probe_ref, prop_ref, left_ref, right_ref, far_ref, inc_ref):
    group, width = win_ref.shape[0], probe_ref.shape[-1]
    transform = _transformer(left_ref, right_ref, group, width)
    layers = _layers(win_ref)
    probe = (probe_ref[0][None], probe_ref[1][None])
    kernel = (prop_ref[0][None], prop_ref[1][None])
    wave = _times(probe, layers[0])
    for s in range(1, len(layers)):
        moved = transform(_times(kernel, transform(wave, -1)), 1)
        inc_ref[:, 2 * (s - 1)] = moved[0]
        inc_ref[:, 2 * (s - 1) + 1] = moved[1]
        wave = _times(layers[s], moved)
    far = transform(wave, -1)
    far_ref[:, 0] = far[0]
    far_ref[:, 1] = far[1]


def _backward_kernel(
    scalar_ref, amp_ref, far_ref, inc_ref, win_ref, probe_ref,
    prop_ref, left_ref, right_ref, border_ref, out_ref, row_even_ref, row_odd_ref, col_even_ref,
    col_odd_ref
):
    group, width = win_ref.shape[0], probe_ref.shape[-1]
    step = pl.program_id(0)
    count = group * pl.num_programs(0)
    transform = _transformer(left_ref, right_ref, group, width)
    layers = _layers(win_ref)
    slices = len(layers)
    probe = (probe_ref[0][None], probe_ref[1][None])
    kernel_conj = (prop_ref[0][None], -prop_ref[1][None])
    amplitude = jnp.stack(
        [amp_ref[scalar_ref[step * group + g]].astype(jnp.float32) for g in range(group)]
    )
    far = (far_ref[:, 0], far_ref[:, 1])
    magnitude = jnp.sqrt(far[0] * far[0] + far[1] * far[1] + 1.0)
    factor = 1.0 - amplitude / magnitude
    back = transform((far[0] * factor, far[1] * factor), 1)
    grads = [None] * slices
    for s in range(slices - 1, 0, -1):
        grads[s] = _conj_times((inc_ref[:, 2 * (s - 1)], inc_ref[:, 2 * (s - 1) + 1]), back)
        back = transform(_times(kernel_conj, transform(_conj_times(layers[s], back), -1)), 1)
    grads[0] = _conj_times(probe, back)
    planes = [part.astype(jnp.bfloat16) for pair in grads for part in pair]
    channels, tile = out_ref.shape[0], out_ref.shape[-1]
    down = lax.broadcasted_iota(jnp.int32, (tile, width), 0) - lax.broadcasted_iota(
        jnp.int32, (tile, width), 1)
    across = lax.broadcasted_iota(jnp.int32, (width, tile), 1) - lax.broadcasted_iota(
        jnp.int32, (width, tile), 0)
    placed, col_picks = [], []
    for g in range(group):
        top = scalar_ref[count + step * group + g]
        left = scalar_ref[2 * count + step * group + g]
        row_pick = (down == top).astype(jnp.bfloat16)
        col_picks.append((across == left).astype(jnp.bfloat16))
        stacked = jnp.concatenate([plane[g] for plane in planes], axis=1)
        placed.append(_dot(row_pick, stacked).astype(jnp.bfloat16))
    spread = jnp.concatenate(
        [
            jnp.concatenate([rows[:, c * width:(c + 1) * width] for rows in placed], axis=1)
            for c in range(channels)
        ],
        axis=0,
    )
    contribution = _dot(spread, jnp.concatenate(col_picks, axis=0)).reshape(channels, tile, tile)

    @pl.when(step == 0)
    def _():
        out_ref[...] = jnp.zeros_like(out_ref)

    out_ref[...] += contribution

    @pl.when(step == pl.num_programs(0) - 1)
    def _():
        lanes = lax.broadcasted_iota(jnp.int32, (8, tile), 1)
        which = jnp.where(lax.broadcasted_iota(jnp.int32, (8, tile), 0) == 0, 0, tile - 1)
        pick = (lanes == which).astype(jnp.bfloat16)
        row_parity = scalar_ref[3 * count]
        col_parity = scalar_ref[3 * count + 1]
        for c in range(channels):
            plane = out_ref[c]
            top = border_ref[0, c:c + 1, :] - step_rate * plane[0:1, :]
            bottom = border_ref[1, c:c + 1, :] - step_rate * plane[tile - 1:tile, :]
            row_even_ref[c:c + 1, :] = jnp.where(row_parity == 0, bottom, top)
            row_odd_ref[c:c + 1, :] = jnp.where(row_parity == 1, bottom, top)
            high = plane.astype(jnp.bfloat16)
            rest = plane - high.astype(jnp.float32)
            middle = rest.astype(jnp.bfloat16)
            low = (rest - middle.astype(jnp.float32)).astype(jnp.bfloat16)
            cols = None
            for part in (high, middle, low):
                term = lax.dot_general(
                    pick, part, (((1,), (1,)), ((), ())), preferred_element_type=jnp.float32
                )
                cols = term if cols is None else cols + term
            first = border_ref[2, c:c + 1, :] - step_rate * cols[0:1]
            last = border_ref[3, c:c + 1, :] - step_rate * cols[1:2]
            col_even_ref[c:c + 1, :] = jnp.where(col_parity == 0, last, first)
            col_odd_ref[c:c + 1, :] = jnp.where(col_parity == 1, last, first)


def forward_waves(windows, probe, kernel, tables, group=8):
    count, channels, width, _ = windows.shape
    group = math.gcd(count, group)
    left_tables, right_tables = tables
    fixed = lambda k: (0, 0, 0)
    return pl.pallas_call(
        _forward_kernel,
        grid=(count // group,),
        in_specs=[
            pl.BlockSpec((group, channels, width, width), lambda k: (k, 0, 0, 0)),
            pl.BlockSpec((2, width, width), fixed),
            pl.BlockSpec((2, width, width), fixed),
            pl.BlockSpec(left_tables.shape, fixed),
            pl.BlockSpec(right_tables.shape, fixed),
        ],
        out_specs=[
            pl.BlockSpec((group, 2, width, width), lambda k: (k, 0, 0, 0)),
            pl.BlockSpec((group, channels - 2, width, width), lambda k: (k, 0, 0, 0)),
        ],
        out_shape=[
            jax.ShapeDtypeStruct((count, 2, width, width), jnp.float32),
            jax.ShapeDtypeStruct((count, channels - 2, width, width), jnp.float32),
        ],
    )(windows, probe, kernel, left_tables, right_tables)


def backward_gradients(scalars, amplitudes, far, incoming, windows, probe, kernel, tables, border,
                       group=8):
    count, channels, width, _ = windows.shape
    tile = border.shape[-1]
    group = math.gcd(count, group)
    left_tables, right_tables = tables
    fixed = lambda k, *_: (0, 0, 0)
    batch = lambda k, *_: (k, 0, 0, 0)
    line = pl.BlockSpec((channels, tile), lambda k, *_: (0, 0))
    grid_spec = pltpu.PrefetchScalarGridSpec(
        num_scalar_prefetch=1,
        grid=(count // group,),
        in_specs=[
            pl.BlockSpec(amplitudes.shape, fixed),
            pl.BlockSpec((group, 2, width, width), batch),
            pl.BlockSpec((group, channels - 2, width, width), batch),
            pl.BlockSpec((group, channels, width, width), batch),
            pl.BlockSpec((2, width, width), fixed),
            pl.BlockSpec((2, width, width), fixed),
            pl.BlockSpec(left_tables.shape, fixed),
            pl.BlockSpec(right_tables.shape, fixed),
            pl.BlockSpec(border.shape, fixed),
        ],
        out_specs=[pl.BlockSpec((channels, tile, tile), fixed), line, line, line, line],
    )
    edge = jax.ShapeDtypeStruct((channels, tile), jnp.float32)
    return pl.pallas_call(
        _backward_kernel,
        grid_spec=grid_spec,
        out_shape=[jax.ShapeDtypeStruct((channels, tile, tile), jnp.float32), edge, edge, edge, edge],
    )(scalars, amplitudes, far, incoming, windows, probe, kernel, left_tables, right_tables, border)


def per_device(object_init, probe, propagator_phase, measured, corners, owner_column):
    width = probe.shape[-1]
    field = object_init
    tile = field.shape[1]
    capacity = measured.shape[3]
    columns = lax.axis_size("ty")
    tops = corners[0, 0, :, 0]
    lefts = corners[0, 0, :, 1]
    owner = owner_column[0, 0, :, 0]
    slot = slot_table(owner)
    target = jnp.clip(owner * capacity + slot, 0, columns * capacity - 1)
    gathered = lax.all_to_all(measured[0, 0], "ty", split_axis=0, concat_axis=0, tiled=True)
    gathered = gathered.reshape(columns * capacity, width, width)
    offsets = jnp.arange(width)
    cells = jnp.arange(tile)
    row_pick = (cells[None, None, :] == (tops[:, None, None] + offsets[None, :, None])).astype(
        jnp.bfloat16
    )
    col_pick = (cells[None, :, None] == (lefts[:, None, None] + offsets[None, None, :])).astype(
        jnp.bfloat16
    )
    field_low = field.astype(jnp.bfloat16)
    rows = jnp.einsum(
        "kir,crs->kcis", row_pick, field_low, preferred_element_type=jnp.float32
    ).astype(jnp.bfloat16)
    windows = jnp.einsum(
        "kcis,ksj->kcij", rows, col_pick, preferred_element_type=jnp.float32
    ).astype(jnp.bfloat16)
    tables = block_tables(width)
    kernel = jnp.stack([jnp.cos(propagator_phase), jnp.sin(propagator_phase)])
    far, incoming = forward_waves(windows, probe, kernel, tables)
    parity = jnp.stack([lax.axis_index("tx") % 2, lax.axis_index("ty") % 2])
    scalars = jnp.concatenate([target, tops, lefts, parity]).astype(jnp.int32)
    border = jnp.stack([field[:, 0, :], field[:, -1, :], field[:, :, 0], field[:, :, -1]])
    total, *payloads = backward_gradients(
        scalars, gathered, far, incoming, windows, probe, kernel, tables, border
    )
    received = _swap("tx", payloads[0], payloads[1]) + _swap("ty", payloads[2], payloads[3])
    return smooth_update(field, total, scalars, payloads, received)


def solution(mesh):
    placed = (
        P(None, "tx", "ty"),
        P(),
        P(),
        P("tx", "ty", None, None, None, None),
        P("tx", "ty", None, None),
        P("tx", "ty", None, None),
    )
    return jax.shard_map(
        per_device, mesh=mesh, in_specs=placed, out_specs=P(None, "tx", "ty"), check_vma=False
    )
```

```python
import math

import jax
import numpy as np
import jax.numpy as jnp
from jax import lax
from jax.experimental import pallas as pl
from jax.experimental.pallas import tpu as pltpu
from jax.sharding import PartitionSpec as P

step_rate = 0.5
smooth_rate = 0.2


def slot_table(owner):
    order = jnp.arange(owner.shape[0])
    same = owner[:, None] == owner[None, :]
    earlier = order[None, :] < order[:, None]
    return jnp.sum(jnp.where(same & earlier, 1, 0), axis=1).astype(jnp.int32)


def _swap(axis, even_payload, odd_payload):
    size = lax.axis_size(axis)
    even = [(i, i + 1) for i in range(0, size - 1, 2)] + [(i + 1, i) for i in range(0, size - 1, 2)]
    odd = [(i, i + 1) for i in range(1, size - 1, 2)] + [(i + 1, i) for i in range(1, size - 1, 2)]
    return lax.ppermute(even_payload, axis, even), lax.ppermute(odd_payload, axis, odd)


def _bend(real, imag):
    weight = 1.0 / jnp.sqrt(1.0 + real * real + imag * imag)
    return real * weight, imag * weight


def _inner_kernel(field_ref, total_ref, out_ref):
    size = field_ref.shape[-1]
    rows = lax.broadcasted_iota(jnp.int32, (size, size), 0)
    cols = lax.broadcasted_iota(jnp.int32, (size, size), 1)
    centers = [field_ref[p] - step_rate * total_ref[p] for p in range(2)]
    views = []
    for v in centers:
        views.append((
            jnp.where(rows == size - 1, v, pltpu.roll(v, size - 1, 0)),
            jnp.where(rows == 0, v, pltpu.roll(v, 1, 0)),
            jnp.where(cols == size - 1, v, pltpu.roll(v, size - 1, 1)),
            jnp.where(cols == 0, v, pltpu.roll(v, 1, 1)),
        ))
    total_r = jnp.zeros_like(centers[0])
    total_i = jnp.zeros_like(centers[1])
    for n in range(4):
        bent = _bend(views[0][n] - centers[0], views[1][n] - centers[1])
        total_r = total_r + bent[0]
        total_i = total_i + bent[1]
    out_ref[0] = centers[0] + smooth_rate * total_r
    out_ref[1] = centers[1] + smooth_rate * total_i


def _edge_kernel(parity_ref, inner_ref, row_even_ref, row_odd_ref, col_even_ref, col_odd_ref,
                 got_row_even_ref, got_row_odd_ref, got_col_even_ref, got_col_odd_ref, out_ref):
    size, lanes = inner_ref.shape[1], inner_ref.shape[2]
    block = pl.program_id(0)
    row_parity = parity_ref[parity_ref.shape[0] - 2]
    col_parity = parity_ref[parity_ref.shape[0] - 1]
    row_even, row_odd = row_even_ref[...], row_odd_ref[...]
    col_even, col_odd = col_even_ref[...], col_odd_ref[...]
    got_row_even, got_row_odd = got_row_even_ref[...], got_row_odd_ref[...]
    got_col_even, got_col_odd = got_col_even_ref[...], got_col_odd_ref[...]
    top = jnp.where(row_parity == 0, row_odd, row_even)
    bottom = jnp.where(row_parity == 0, row_even, row_odd)
    first = jnp.where(col_parity == 0, col_odd, col_even)
    last = jnp.where(col_parity == 0, col_even, col_odd)
    above = jnp.where(row_parity == 1, got_row_even, got_row_odd)
    below = jnp.where(row_parity == 0, got_row_even, got_row_odd)
    left = jnp.where(col_parity == 1, got_col_even, got_col_odd)
    right = jnp.where(col_parity == 0, got_col_even, got_col_odd)
    rows = lax.broadcasted_iota(jnp.int32, (size, lanes), 0)
    cols = lax.broadcasted_iota(jnp.int32, (size, lanes), 1)
    eye = (lax.broadcasted_iota(jnp.int32, (lanes, lanes), 0) == lax.broadcasted_iota(
        jnp.int32, (lanes, lanes), 1)).astype(jnp.bfloat16)

    def as_column(line):
        high = line.astype(jnp.bfloat16)
        rest = line - high.astype(jnp.float32)
        middle = rest.astype(jnp.bfloat16)
        low = (rest - middle.astype(jnp.float32)).astype(jnp.bfloat16)
        chunks = []
        for h in range(size // lanes):
            spread = None
            for part in (high, middle, low):
                rows_of = jnp.broadcast_to(part[:, h * lanes:(h + 1) * lanes], (lanes, lanes))
                term = lax.dot_general(
                    eye, rows_of, (((1,), (1,)), ((), ())), preferred_element_type=jnp.float32
                )
                spread = term if spread is None else spread + term
            chunks.append(spread)
        return jnp.concatenate(chunks, axis=0)

    edge_col = jnp.where(block == 0, 0, lanes - 1)
    for s in range(inner_ref.shape[0] // 2):
        c0, c1 = 2 * s, 2 * s + 1
        north = _bend(above[c0:c0 + 1] - top[c0:c0 + 1], above[c1:c1 + 1] - top[c1:c1 + 1])
        south = _bend(below[c0:c0 + 1] - bottom[c0:c0 + 1],
                      below[c1:c1 + 1] - bottom[c1:c1 + 1])
        west = _bend(left[c0:c0 + 1] - first[c0:c0 + 1], left[c1:c1 + 1] - first[c1:c1 + 1])
        east = _bend(right[c0:c0 + 1] - last[c0:c0 + 1], right[c1:c1 + 1] - last[c1:c1 + 1])
        for part, c in ((0, c0), (1, c1)):
            side = as_column(jnp.where(block == 0, west[part], east[part]))
            extra = (
                jnp.where(rows == 0, north[part], 0.0)
                + jnp.where(rows == size - 1, south[part], 0.0)
                + jnp.where(cols == edge_col, side, 0.0)
            )
            out_ref[c] = inner_ref[c] + smooth_rate * extra


def smooth_update(field, total, parity, payloads, received):
    channels, size, _ = field.shape
    plane = pl.BlockSpec((2, size, size), lambda s: (s, 0, 0))
    inner = pl.pallas_call(
        _inner_kernel,
        grid=(channels // 2,),
        in_specs=[plane, plane],
        out_specs=plane,
        out_shape=jax.ShapeDtypeStruct(field.shape, jnp.float32),
    )(field, total)
    lanes = 128
    half = pl.BlockSpec((channels, size, lanes), lambda b: (0, 0, b))
    row_part = pl.BlockSpec((channels, lanes), lambda b: (0, b))
    whole = pl.BlockSpec((channels, size), lambda b: (0, 0))
    scalars = pl.BlockSpec(memory_space=pltpu.SMEM)
    return pl.pallas_call(
        _edge_kernel,
        grid=(size // lanes,),
        in_specs=[scalars, half, row_part, row_part, whole, whole, row_part, row_part, whole, whole],
        out_specs=half,
        out_shape=jax.ShapeDtypeStruct(field.shape, jnp.float32),
        input_output_aliases={1: 0},
    )(parity, inner, *payloads, *received)


def block_tables(width):
    index = np.arange(width)
    angles = (index[:, None] * index[None, :] % width) * (2.0 * math.pi / width)
    scale = 1.0 / math.sqrt(width)
    cosine, sine = np.cos(angles) * scale, np.sin(angles) * scale
    plus = np.block([[cosine, -sine], [sine, cosine]])
    minus = np.block([[cosine, sine], [-sine, cosine]])
    lefts, rights = [], []
    for table in (plus, minus):
        high = table.astype(jnp.bfloat16)
        low = (table - high.astype(np.float64)).astype(jnp.bfloat16)
        lefts.append(np.concatenate([high, low, high], axis=1))
        rights.append(np.concatenate([high, low, high], axis=0))
    return jnp.asarray(np.stack(lefts)), jnp.asarray(np.stack(rights))


def _split(x):
    high = x.astype(jnp.bfloat16)
    low = (x - high.astype(jnp.float32)).astype(jnp.bfloat16)
    return high, low


def _dot(a, b):
    return jnp.dot(a, b, preferred_element_type=jnp.float32)


def _times(a, b):
    return (a[0] * b[0] - a[1] * b[1], a[0] * b[1] + a[1] * b[0])


def _conj_times(a, b):
    return (a[0] * b[0] + a[1] * b[1], a[0] * b[1] - a[1] * b[0])


def _transformer(left_ref, right_ref, group, width):
    def transform(pair, sign):
        first, second = (1, 0) if sign < 0 else (0, 1)
        stacked = jnp.concatenate(
            [jnp.concatenate([pair[0][g], pair[1][g]], axis=0) for g in range(group)], axis=1
        )
        high, low = _split(stacked)
        rows = _dot(left_ref[first], jnp.concatenate([high, high, low], axis=0))
        joined = jnp.concatenate(
            [
                jnp.concatenate(
                    [rows[:width, g * width:(g + 1) * width], rows[width:, g * width:(g + 1) * width]],
                    axis=1,
                )
                for g in range(group)
            ],
            axis=0,
        )
        high, low = _split(joined)
        out = _dot(jnp.concatenate([high, high, low], axis=1), right_ref[second])
        return (
            out[:, :width].reshape(group, width, width),
            out[:, width:].reshape(group, width, width),
        )

    return transform


def _layers(win_ref):
    slices = win_ref.shape[1] // 2
    return [
        (win_ref[:, 2 * s].astype(jnp.float32), win_ref[:, 2 * s + 1].astype(jnp.float32))
        for s in range(slices)
    ]


def _forward_kernel(win_ref, probe_ref, prop_ref, left_ref, right_ref, far_ref, inc_ref):
    group, width = win_ref.shape[0], probe_ref.shape[-1]
    transform = _transformer(left_ref, right_ref, group, width)
    layers = _layers(win_ref)
    probe = (probe_ref[0][None], probe_ref[1][None])
    kernel = (prop_ref[0][None], prop_ref[1][None])
    wave = _times(probe, layers[0])
    for s in range(1, len(layers)):
        moved = transform(_times(kernel, transform(wave, -1)), 1)
        inc_ref[:, 2 * (s - 1)] = moved[0]
        inc_ref[:, 2 * (s - 1) + 1] = moved[1]
        wave = _times(layers[s], moved)
    far = transform(wave, -1)
    far_ref[:, 0] = far[0]
    far_ref[:, 1] = far[1]


def _backward_kernel(
    scalar_ref, amp_ref, far_ref, inc_ref, win_ref, probe_ref,
    prop_ref, left_ref, right_ref, border_ref, out_ref, row_even_ref, row_odd_ref, col_even_ref,
    col_odd_ref
):
    group, width = win_ref.shape[0], probe_ref.shape[-1]
    step = pl.program_id(0)
    count = group * pl.num_programs(0)
    transform = _transformer(left_ref, right_ref, group, width)
    layers = _layers(win_ref)
    slices = len(layers)
    probe = (probe_ref[0][None], probe_ref[1][None])
    kernel_conj = (prop_ref[0][None], -prop_ref[1][None])
    amplitude = jnp.stack(
        [amp_ref[scalar_ref[step * group + g]].astype(jnp.float32) for g in range(group)]
    )
    far = (far_ref[:, 0], far_ref[:, 1])
    magnitude = jnp.sqrt(far[0] * far[0] + far[1] * far[1] + 1.0)
    factor = 1.0 - amplitude / magnitude
    back = transform((far[0] * factor, far[1] * factor), 1)
    grads = [None] * slices
    for s in range(slices - 1, 0, -1):
        grads[s] = _conj_times((inc_ref[:, 2 * (s - 1)], inc_ref[:, 2 * (s - 1) + 1]), back)
        back = transform(_times(kernel_conj, transform(_conj_times(layers[s], back), -1)), 1)
    grads[0] = _conj_times(probe, back)
    planes = [part.astype(jnp.bfloat16) for pair in grads for part in pair]
    channels, tile = out_ref.shape[0], out_ref.shape[-1]
    down = lax.broadcasted_iota(jnp.int32, (tile, width), 0) - lax.broadcasted_iota(
        jnp.int32, (tile, width), 1)
    across = lax.broadcasted_iota(jnp.int32, (width, tile), 1) - lax.broadcasted_iota(
        jnp.int32, (width, tile), 0)
    placed, col_picks = [], []
    for g in range(group):
        top = scalar_ref[count + step * group + g]
        left = scalar_ref[2 * count + step * group + g]
        row_pick = (down == top).astype(jnp.bfloat16)
        col_picks.append((across == left).astype(jnp.bfloat16))
        stacked = jnp.concatenate([plane[g] for plane in planes], axis=1)
        placed.append(_dot(row_pick, stacked).astype(jnp.bfloat16))
    spread = jnp.concatenate(
        [
            jnp.concatenate([rows[:, c * width:(c + 1) * width] for rows in placed], axis=1)
            for c in range(channels)
        ],
        axis=0,
    )
    contribution = _dot(spread, jnp.concatenate(col_picks, axis=0)).reshape(channels, tile, tile)

    @pl.when(step == 0)
    def _():
        out_ref[...] = jnp.zeros_like(out_ref)

    out_ref[...] += contribution

    @pl.when(step == pl.num_programs(0) - 1)
    def _():
        lanes = lax.broadcasted_iota(jnp.int32, (8, tile), 1)
        which = jnp.where(lax.broadcasted_iota(jnp.int32, (8, tile), 0) == 0, 0, tile - 1)
        pick = (lanes == which).astype(jnp.bfloat16)
        row_parity = scalar_ref[3 * count]
        col_parity = scalar_ref[3 * count + 1]
        for c in range(channels):
            plane = out_ref[c]
            top = border_ref[0, c:c + 1, :] - step_rate * plane[0:1, :]
            bottom = border_ref[1, c:c + 1, :] - step_rate * plane[tile - 1:tile, :]
            row_even_ref[c:c + 1, :] = jnp.where(row_parity == 0, bottom, top)
            row_odd_ref[c:c + 1, :] = jnp.where(row_parity == 1, bottom, top)
            high = plane.astype(jnp.bfloat16)
            rest = plane - high.astype(jnp.float32)
            middle = rest.astype(jnp.bfloat16)
            low = (rest - middle.astype(jnp.float32)).astype(jnp.bfloat16)
            cols = None
            for part in (high, middle, low):
                term = lax.dot_general(
                    pick, part, (((1,), (1,)), ((), ())), preferred_element_type=jnp.float32
                )
                cols = term if cols is None else cols + term
            first = border_ref[2, c:c + 1, :] - step_rate * cols[0:1]
            last = border_ref[3, c:c + 1, :] - step_rate * cols[1:2]
            col_even_ref[c:c + 1, :] = jnp.where(col_parity == 0, last, first)
            col_odd_ref[c:c + 1, :] = jnp.where(col_parity == 1, last, first)


def forward_waves(windows, probe, kernel, tables, group=8):
    count, channels, width, _ = windows.shape
    group = math.gcd(count, group)
    left_tables, right_tables = tables
    fixed = lambda k: (0, 0, 0)
    return pl.pallas_call(
        _forward_kernel,
        grid=(count // group,),
        in_specs=[
            pl.BlockSpec((group, channels, width, width), lambda k: (k, 0, 0, 0)),
            pl.BlockSpec((2, width, width), fixed),
            pl.BlockSpec((2, width, width), fixed),
            pl.BlockSpec(left_tables.shape, fixed),
            pl.BlockSpec(right_tables.shape, fixed),
        ],
        out_specs=[
            pl.BlockSpec((group, 2, width, width), lambda k: (k, 0, 0, 0)),
            pl.BlockSpec((group, channels - 2, width, width), lambda k: (k, 0, 0, 0)),
        ],
        out_shape=[
            jax.ShapeDtypeStruct((count, 2, width, width), jnp.float32),
            jax.ShapeDtypeStruct((count, channels - 2, width, width), jnp.float32),
        ],
    )(windows, probe, kernel, left_tables, right_tables)


def backward_gradients(scalars, amplitudes, far, incoming, windows, probe, kernel, tables, border,
                       group=8):
    count, channels, width, _ = windows.shape
    tile = border.shape[-1]
    group = math.gcd(count, group)
    left_tables, right_tables = tables
    fixed = lambda k, *_: (0, 0, 0)
    batch = lambda k, *_: (k, 0, 0, 0)
    line = pl.BlockSpec((channels, tile), lambda k, *_: (0, 0))
    grid_spec = pltpu.PrefetchScalarGridSpec(
        num_scalar_prefetch=1,
        grid=(count // group,),
        in_specs=[
            pl.BlockSpec(amplitudes.shape, fixed),
            pl.BlockSpec((group, 2, width, width), batch),
            pl.BlockSpec((group, channels - 2, width, width), batch),
            pl.BlockSpec((group, channels, width, width), batch),
            pl.BlockSpec((2, width, width), fixed),
            pl.BlockSpec((2, width, width), fixed),
            pl.BlockSpec(left_tables.shape, fixed),
            pl.BlockSpec(right_tables.shape, fixed),
            pl.BlockSpec(border.shape, fixed),
        ],
        out_specs=[pl.BlockSpec((channels, tile, tile), fixed), line, line, line, line],
    )
    edge = jax.ShapeDtypeStruct((channels, tile), jnp.float32)
    return pl.pallas_call(
        _backward_kernel,
        grid_spec=grid_spec,
        out_shape=[jax.ShapeDtypeStruct((channels, tile, tile), jnp.float32), edge, edge, edge, edge],
    )(scalars, amplitudes, far, incoming, windows, probe, kernel, left_tables, right_tables, border)


def per_device(object_init, probe, propagator_phase, measured, corners, owner_column):
    width = probe.shape[-1]
    field = object_init
    tile = field.shape[1]
    capacity = measured.shape[3]
    columns = lax.axis_size("ty")
    tops = corners[0, 0, :, 0]
    lefts = corners[0, 0, :, 1]
    owner = owner_column[0, 0, :, 0]
    slot = slot_table(owner)
    target = jnp.clip(owner * capacity + slot, 0, columns * capacity - 1)
    gathered = lax.all_to_all(measured[0, 0], "ty", split_axis=0, concat_axis=0, tiled=True)
    gathered = gathered.reshape(columns * capacity, width, width)
    offsets = jnp.arange(width)
    cells = jnp.arange(tile)
    row_pick = (cells[None, None, :] == (tops[:, None, None] + offsets[None, :, None])).astype(
        jnp.bfloat16
    )
    col_pick = (cells[None, :, None] == (lefts[:, None, None] + offsets[None, None, :])).astype(
        jnp.bfloat16
    )
    field_low = field.astype(jnp.bfloat16)
    rows = jnp.einsum(
        "kir,crs->kcis", row_pick, field_low, preferred_element_type=jnp.float32
    ).astype(jnp.bfloat16)
    windows = jnp.einsum(
        "kcis,ksj->kcij", rows, col_pick, preferred_element_type=jnp.float32
    ).astype(jnp.bfloat16)
    tables = block_tables(width)
    kernel = jnp.stack([jnp.cos(propagator_phase), jnp.sin(propagator_phase)])
    far, incoming = forward_waves(windows, probe, kernel, tables)
    parity = jnp.stack([lax.axis_index("tx") % 2, lax.axis_index("ty") % 2])
    scalars = jnp.concatenate([target, tops, lefts, parity]).astype(jnp.int32)
    border = jnp.stack([field[:, 0, :], field[:, -1, :], field[:, :, 0], field[:, :, -1]])
    total, *payloads = backward_gradients(
        scalars, gathered, far, incoming, windows, probe, kernel, tables, border
    )
    received = _swap("tx", payloads[0], payloads[1]) + _swap("ty", payloads[2], payloads[3])
    return smooth_update(field, total, scalars, payloads, received)


def solution(mesh):
    placed = (
        P(None, "tx", "ty"),
        P(),
        P(),
        P("tx", "ty", None, None, None, None),
        P("tx", "ty", None, None),
        P("tx", "ty", None, None),
    )
    return jax.shard_map(
        per_device, mesh=mesh, in_specs=placed, out_specs=P(None, "tx", "ty"), check_vma=False
    )
```

```python
import math

import jax
import numpy as np
import jax.numpy as jnp
from jax import lax
from jax.experimental import pallas as pl
from jax.experimental.pallas import tpu as pltpu
from jax.sharding import PartitionSpec as P

step_rate = 0.5
smooth_rate = 0.2


def slot_table(owner):
    order = jnp.arange(owner.shape[0])
    same = owner[:, None] == owner[None, :]
    earlier = order[None, :] < order[:, None]
    return jnp.sum(jnp.where(same & earlier, 1, 0), axis=1).astype(jnp.int32)


def _swap(axis, even_payload, odd_payload):
    size = lax.axis_size(axis)
    even = [(i, i + 1) for i in range(0, size - 1, 2)] + [(i + 1, i) for i in range(0, size - 1, 2)]
    odd = [(i, i + 1) for i in range(1, size - 1, 2)] + [(i + 1, i) for i in range(1, size - 1, 2)]
    return lax.ppermute(even_payload, axis, even), lax.ppermute(odd_payload, axis, odd)


def _bend(real, imag):
    weight = 1.0 / jnp.sqrt(1.0 + real * real + imag * imag)
    return real * weight, imag * weight


def _inner_kernel(field_ref, total_ref, out_ref):
    size = field_ref.shape[-1]
    rows = lax.broadcasted_iota(jnp.int32, (size, size), 0)
    cols = lax.broadcasted_iota(jnp.int32, (size, size), 1)
    centers = [field_ref[p] - step_rate * total_ref[p] for p in range(2)]
    views = []
    for v in centers:
        views.append((
            jnp.where(rows == size - 1, v, pltpu.roll(v, size - 1, 0)),
            jnp.where(rows == 0, v, pltpu.roll(v, 1, 0)),
            jnp.where(cols == size - 1, v, pltpu.roll(v, size - 1, 1)),
            jnp.where(cols == 0, v, pltpu.roll(v, 1, 1)),
        ))
    total_r = jnp.zeros_like(centers[0])
    total_i = jnp.zeros_like(centers[1])
    for n in range(4):
        bent = _bend(views[0][n] - centers[0], views[1][n] - centers[1])
        total_r = total_r + bent[0]
        total_i = total_i + bent[1]
    out_ref[0] = centers[0] + smooth_rate * total_r
    out_ref[1] = centers[1] + smooth_rate * total_i


def _edge_kernel(parity_ref, inner_ref, row_even_ref, row_odd_ref, col_even_ref, col_odd_ref,
                 got_row_even_ref, got_row_odd_ref, got_col_even_ref, got_col_odd_ref, out_ref):
    size, lanes = inner_ref.shape[1], inner_ref.shape[2]
    block = pl.program_id(0)
    row_parity = parity_ref[parity_ref.shape[0] - 2]
    col_parity = parity_ref[parity_ref.shape[0] - 1]
    row_even, row_odd = row_even_ref[...], row_odd_ref[...]
    col_even, col_odd = col_even_ref[...], col_odd_ref[...]
    got_row_even, got_row_odd = got_row_even_ref[...], got_row_odd_ref[...]
    got_col_even, got_col_odd = got_col_even_ref[...], got_col_odd_ref[...]
    top = jnp.where(row_parity == 0, row_odd, row_even)
    bottom = jnp.where(row_parity == 0, row_even, row_odd)
    first = jnp.where(col_parity == 0, col_odd, col_even)
    last = jnp.where(col_parity == 0, col_even, col_odd)
    above = jnp.where(row_parity == 1, got_row_even, got_row_odd)
    below = jnp.where(row_parity == 0, got_row_even, got_row_odd)
    left = jnp.where(col_parity == 1, got_col_even, got_col_odd)
    right = jnp.where(col_parity == 0, got_col_even, got_col_odd)
    rows = lax.broadcasted_iota(jnp.int32, (size, lanes), 0)
    cols = lax.broadcasted_iota(jnp.int32, (size, lanes), 1)
    square = lax.broadcasted_iota(jnp.int32, (lanes, lanes), 0) == lax.broadcasted_iota(
        jnp.int32, (lanes, lanes), 1)

    def as_column(line):
        return jnp.concatenate(
            [
                jnp.sum(jnp.where(square, line[:, h * lanes:(h + 1) * lanes], 0.0), axis=1,
                        keepdims=True)
                for h in range(size // lanes)
            ],
            axis=0,
        )

    edge_col = jnp.where(block == 0, 0, lanes - 1)
    for s in range(inner_ref.shape[0] // 2):
        c0, c1 = 2 * s, 2 * s + 1
        north = _bend(above[c0:c0 + 1] - top[c0:c0 + 1], above[c1:c1 + 1] - top[c1:c1 + 1])
        south = _bend(below[c0:c0 + 1] - bottom[c0:c0 + 1],
                      below[c1:c1 + 1] - bottom[c1:c1 + 1])
        west = _bend(left[c0:c0 + 1] - first[c0:c0 + 1], left[c1:c1 + 1] - first[c1:c1 + 1])
        east = _bend(right[c0:c0 + 1] - last[c0:c0 + 1], right[c1:c1 + 1] - last[c1:c1 + 1])
        for part, c in ((0, c0), (1, c1)):
            side = as_column(jnp.where(block == 0, west[part], east[part]))
            extra = (
                jnp.where(rows == 0, north[part], 0.0)
                + jnp.where(rows == size - 1, south[part], 0.0)
                + jnp.where(cols == edge_col, side, 0.0)
            )
            out_ref[c] = inner_ref[c] + smooth_rate * extra


def smooth_update(field, total, parity, payloads, received):
    channels, size, _ = field.shape
    plane = pl.BlockSpec((2, size, size), lambda s: (s, 0, 0))
    inner = pl.pallas_call(
        _inner_kernel,
        grid=(channels // 2,),
        in_specs=[plane, plane],
        out_specs=plane,
        out_shape=jax.ShapeDtypeStruct(field.shape, jnp.float32),
    )(field, total)
    lanes = 128
    half = pl.BlockSpec((channels, size, lanes), lambda b: (0, 0, b))
    row_part = pl.BlockSpec((channels, lanes), lambda b: (0, b))
    whole = pl.BlockSpec((channels, size), lambda b: (0, 0))
    scalars = pl.BlockSpec(memory_space=pltpu.SMEM)
    return pl.pallas_call(
        _edge_kernel,
        grid=(size // lanes,),
        in_specs=[scalars, half, row_part, row_part, whole, whole, row_part, row_part, whole, whole],
        out_specs=half,
        out_shape=jax.ShapeDtypeStruct(field.shape, jnp.float32),
        input_output_aliases={1: 0},
    )(parity, inner, *payloads, *received)


def block_tables(width):
    index = np.arange(width)
    angles = (index[:, None] * index[None, :] % width) * (2.0 * math.pi / width)
    scale = 1.0 / math.sqrt(width)
    cosine, sine = np.cos(angles) * scale, np.sin(angles) * scale
    plus = np.block([[cosine, -sine], [sine, cosine]])
    minus = np.block([[cosine, sine], [-sine, cosine]])
    lefts, rights = [], []
    for table in (plus, minus):
        high = table.astype(jnp.bfloat16)
        low = (table - high.astype(np.float64)).astype(jnp.bfloat16)
        lefts.append(np.concatenate([high, low, high], axis=1))
        rights.append(np.concatenate([high, low, high], axis=0))
    return jnp.asarray(np.stack(lefts)), jnp.asarray(np.stack(rights))


def _split(x):
    high = x.astype(jnp.bfloat16)
    low = (x - high.astype(jnp.float32)).astype(jnp.bfloat16)
    return high, low


def _dot(a, b):
    return jnp.dot(a, b, preferred_element_type=jnp.float32)


def _times(a, b):
    return (a[0] * b[0] - a[1] * b[1], a[0] * b[1] + a[1] * b[0])


def _conj_times(a, b):
    return (a[0] * b[0] + a[1] * b[1], a[0] * b[1] - a[1] * b[0])


def _transformer(left_ref, right_ref, group, width):
    def transform(pair, sign):
        first, second = (1, 0) if sign < 0 else (0, 1)
        stacked = jnp.concatenate(
            [jnp.concatenate([pair[0][g], pair[1][g]], axis=0) for g in range(group)], axis=1
        )
        high, low = _split(stacked)
        rows = _dot(left_ref[first], jnp.concatenate([high, high, low], axis=0))
        joined = jnp.concatenate(
            [
                jnp.concatenate(
                    [rows[:width, g * width:(g + 1) * width], rows[width:, g * width:(g + 1) * width]],
                    axis=1,
                )
                for g in range(group)
            ],
            axis=0,
        )
        high, low = _split(joined)
        out = _dot(jnp.concatenate([high, high, low], axis=1), right_ref[second])
        return (
            out[:, :width].reshape(group, width, width),
            out[:, width:].reshape(group, width, width),
        )

    return transform


def _layers(win_ref):
    slices = win_ref.shape[1] // 2
    return [
        (win_ref[:, 2 * s].astype(jnp.float32), win_ref[:, 2 * s + 1].astype(jnp.float32))
        for s in range(slices)
    ]


def _forward_kernel(win_ref, probe_ref, prop_ref, left_ref, right_ref, far_ref, inc_ref):
    group, width = win_ref.shape[0], probe_ref.shape[-1]
    transform = _transformer(left_ref, right_ref, group, width)
    layers = _layers(win_ref)
    probe = (probe_ref[0][None], probe_ref[1][None])
    kernel = (prop_ref[0][None], prop_ref[1][None])
    wave = _times(probe, layers[0])
    for s in range(1, len(layers)):
        moved = transform(_times(kernel, transform(wave, -1)), 1)
        inc_ref[:, 2 * (s - 1)] = moved[0]
        inc_ref[:, 2 * (s - 1) + 1] = moved[1]
        wave = _times(layers[s], moved)
    far = transform(wave, -1)
    far_ref[:, 0] = far[0]
    far_ref[:, 1] = far[1]


def _backward_kernel(
    scalar_ref, amp_ref, far_ref, inc_ref, win_ref, probe_ref,
    prop_ref, left_ref, right_ref, border_ref, out_ref, row_even_ref, row_odd_ref, col_even_ref,
    col_odd_ref
):
    group, width = win_ref.shape[0], probe_ref.shape[-1]
    step = pl.program_id(0)
    count = group * pl.num_programs(0)
    transform = _transformer(left_ref, right_ref, group, width)
    layers = _layers(win_ref)
    slices = len(layers)
    probe = (probe_ref[0][None], probe_ref[1][None])
    kernel_conj = (prop_ref[0][None], -prop_ref[1][None])
    amplitude = jnp.stack(
        [amp_ref[scalar_ref[step * group + g]].astype(jnp.float32) for g in range(group)]
    )
    far = (far_ref[:, 0], far_ref[:, 1])
    magnitude = jnp.sqrt(far[0] * far[0] + far[1] * far[1] + 1.0)
    factor = 1.0 - amplitude / magnitude
    back = transform((far[0] * factor, far[1] * factor), 1)
    grads = [None] * slices
    for s in range(slices - 1, 0, -1):
        grads[s] = _conj_times((inc_ref[:, 2 * (s - 1)], inc_ref[:, 2 * (s - 1) + 1]), back)
        back = transform(_times(kernel_conj, transform(_conj_times(layers[s], back), -1)), 1)
    grads[0] = _conj_times(probe, back)
    planes = [part.astype(jnp.bfloat16) for pair in grads for part in pair]
    channels, tile = out_ref.shape[0], out_ref.shape[-1]
    down = lax.broadcasted_iota(jnp.int32, (tile, width), 0) - lax.broadcasted_iota(
        jnp.int32, (tile, width), 1)
    across = lax.broadcasted_iota(jnp.int32, (width, tile), 1) - lax.broadcasted_iota(
        jnp.int32, (width, tile), 0)
    placed, col_picks = [], []
    for g in range(group):
        top = scalar_ref[count + step * group + g]
        left = scalar_ref[2 * count + step * group + g]
        row_pick = (down == top).astype(jnp.bfloat16)
        col_picks.append((across == left).astype(jnp.bfloat16))
        stacked = jnp.concatenate([plane[g] for plane in planes], axis=1)
        placed.append(_dot(row_pick, stacked).astype(jnp.bfloat16))
    spread = jnp.concatenate(
        [
            jnp.concatenate([rows[:, c * width:(c + 1) * width] for rows in placed], axis=1)
            for c in range(channels)
        ],
        axis=0,
    )
    contribution = _dot(spread, jnp.concatenate(col_picks, axis=0)).reshape(channels, tile, tile)

    @pl.when(step == 0)
    def _():
        out_ref[...] = jnp.zeros_like(out_ref)

    out_ref[...] += contribution

    @pl.when(step == pl.num_programs(0) - 1)
    def _():
        lanes = lax.broadcasted_iota(jnp.int32, (8, tile), 1)
        which = jnp.where(lax.broadcasted_iota(jnp.int32, (8, tile), 0) == 0, 0, tile - 1)
        pick = (lanes == which).astype(jnp.bfloat16)
        row_parity = scalar_ref[3 * count]
        col_parity = scalar_ref[3 * count + 1]
        for c in range(channels):
            plane = out_ref[c]
            top = border_ref[0, c:c + 1, :] - step_rate * plane[0:1, :]
            bottom = border_ref[1, c:c + 1, :] - step_rate * plane[tile - 1:tile, :]
            row_even_ref[c:c + 1, :] = jnp.where(row_parity == 0, bottom, top)
            row_odd_ref[c:c + 1, :] = jnp.where(row_parity == 1, bottom, top)
            high = plane.astype(jnp.bfloat16)
            rest = plane - high.astype(jnp.float32)
            middle = rest.astype(jnp.bfloat16)
            low = (rest - middle.astype(jnp.float32)).astype(jnp.bfloat16)
            cols = None
            for part in (high, middle, low):
                term = lax.dot_general(
                    pick, part, (((1,), (1,)), ((), ())), preferred_element_type=jnp.float32
                )
                cols = term if cols is None else cols + term
            first = border_ref[2, c:c + 1, :] - step_rate * cols[0:1]
            last = border_ref[3, c:c + 1, :] - step_rate * cols[1:2]
            col_even_ref[c:c + 1, :] = jnp.where(col_parity == 0, last, first)
            col_odd_ref[c:c + 1, :] = jnp.where(col_parity == 1, last, first)


def forward_waves(windows, probe, kernel, tables, group=4):
    count, channels, width, _ = windows.shape
    group = math.gcd(count, group)
    left_tables, right_tables = tables
    fixed = lambda k: (0, 0, 0)
    return pl.pallas_call(
        _forward_kernel,
        grid=(count // group,),
        in_specs=[
            pl.BlockSpec((group, channels, width, width), lambda k: (k, 0, 0, 0)),
            pl.BlockSpec((2, width, width), fixed),
            pl.BlockSpec((2, width, width), fixed),
            pl.BlockSpec(left_tables.shape, fixed),
            pl.BlockSpec(right_tables.shape, fixed),
        ],
        out_specs=[
            pl.BlockSpec((group, 2, width, width), lambda k: (k, 0, 0, 0)),
            pl.BlockSpec((group, channels - 2, width, width), lambda k: (k, 0, 0, 0)),
        ],
        out_shape=[
            jax.ShapeDtypeStruct((count, 2, width, width), jnp.float32),
            jax.ShapeDtypeStruct((count, channels - 2, width, width), jnp.float32),
        ],
    )(windows, probe, kernel, left_tables, right_tables)


def backward_gradients(scalars, amplitudes, far, incoming, windows, probe, kernel, tables, border,
                       group=4):
    count, channels, width, _ = windows.shape
    tile = border.shape[-1]
    group = math.gcd(count, group)
    left_tables, right_tables = tables
    fixed = lambda k, *_: (0, 0, 0)
    batch = lambda k, *_: (k, 0, 0, 0)
    line = pl.BlockSpec((channels, tile), lambda k, *_: (0, 0))
    grid_spec = pltpu.PrefetchScalarGridSpec(
        num_scalar_prefetch=1,
        grid=(count // group,),
        in_specs=[
            pl.BlockSpec(amplitudes.shape, fixed),
            pl.BlockSpec((group, 2, width, width), batch),
            pl.BlockSpec((group, channels - 2, width, width), batch),
            pl.BlockSpec((group, channels, width, width), batch),
            pl.BlockSpec((2, width, width), fixed),
            pl.BlockSpec((2, width, width), fixed),
            pl.BlockSpec(left_tables.shape, fixed),
            pl.BlockSpec(right_tables.shape, fixed),
            pl.BlockSpec(border.shape, fixed),
        ],
        out_specs=[pl.BlockSpec((channels, tile, tile), fixed), line, line, line, line],
    )
    edge = jax.ShapeDtypeStruct((channels, tile), jnp.float32)
    return pl.pallas_call(
        _backward_kernel,
        grid_spec=grid_spec,
        out_shape=[jax.ShapeDtypeStruct((channels, tile, tile), jnp.float32), edge, edge, edge, edge],
    )(scalars, amplitudes, far, incoming, windows, probe, kernel, left_tables, right_tables, border)


def per_device(object_init, probe, propagator_phase, measured, corners, owner_column):
    width = probe.shape[-1]
    field = object_init
    tile = field.shape[1]
    capacity = measured.shape[3]
    columns = lax.axis_size("ty")
    tops = corners[0, 0, :, 0]
    lefts = corners[0, 0, :, 1]
    owner = owner_column[0, 0, :, 0]
    slot = slot_table(owner)
    target = jnp.clip(owner * capacity + slot, 0, columns * capacity - 1)
    gathered = lax.all_to_all(measured[0, 0], "ty", split_axis=0, concat_axis=0, tiled=True)
    gathered = gathered.reshape(columns * capacity, width, width)
    offsets = jnp.arange(width)
    cells = jnp.arange(tile)
    row_pick = (cells[None, None, :] == (tops[:, None, None] + offsets[None, :, None])).astype(
        jnp.bfloat16
    )
    col_pick = (cells[None, :, None] == (lefts[:, None, None] + offsets[None, None, :])).astype(
        jnp.bfloat16
    )
    field_low = field.astype(jnp.bfloat16)
    rows = jnp.einsum(
        "kir,crs->kcis", row_pick, field_low, preferred_element_type=jnp.float32
    ).astype(jnp.bfloat16)
    windows = jnp.einsum(
        "kcis,ksj->kcij", rows, col_pick, preferred_element_type=jnp.float32
    ).astype(jnp.bfloat16)
    tables = block_tables(width)
    kernel = jnp.stack([jnp.cos(propagator_phase), jnp.sin(propagator_phase)])
    far, incoming = forward_waves(windows, probe, kernel, tables)
    parity = jnp.stack([lax.axis_index("tx") % 2, lax.axis_index("ty") % 2])
    scalars = jnp.concatenate([target, tops, lefts, parity]).astype(jnp.int32)
    border = jnp.stack([field[:, 0, :], field[:, -1, :], field[:, :, 0], field[:, :, -1]])
    total, *payloads = backward_gradients(
        scalars, gathered, far, incoming, windows, probe, kernel, tables, border
    )
    received = _swap("tx", payloads[0], payloads[1]) + _swap("ty", payloads[2], payloads[3])
    return smooth_update(field, total, scalars, payloads, received)


def solution(mesh):
    placed = (
        P(None, "tx", "ty"),
        P(),
        P(),
        P("tx", "ty", None, None, None, None),
        P("tx", "ty", None, None),
        P("tx", "ty", None, None),
    )
    return jax.shard_map(
        per_device, mesh=mesh, in_specs=placed, out_specs=P(None, "tx", "ty"), check_vma=False
    )
```

```python
import math

import jax
import numpy as np
import jax.numpy as jnp
from jax import lax
from jax.experimental import pallas as pl
from jax.experimental.pallas import tpu as pltpu
from jax.sharding import PartitionSpec as P

step_rate = 0.5
smooth_rate = 0.2


def slot_table(owner):
    order = jnp.arange(owner.shape[0])
    same = owner[:, None] == owner[None, :]
    earlier = order[None, :] < order[:, None]
    return jnp.sum(jnp.where(same & earlier, 1, 0), axis=1).astype(jnp.int32)


def _swap(axis, even_payload, odd_payload):
    size = lax.axis_size(axis)
    even = [(i, i + 1) for i in range(0, size - 1, 2)] + [(i + 1, i) for i in range(0, size - 1, 2)]
    odd = [(i, i + 1) for i in range(1, size - 1, 2)] + [(i + 1, i) for i in range(1, size - 1, 2)]
    return lax.ppermute(even_payload, axis, even), lax.ppermute(odd_payload, axis, odd)


def _bend(real, imag):
    weight = 1.0 / jnp.sqrt(1.0 + real * real + imag * imag)
    return real * weight, imag * weight


def _inner_kernel(field_ref, total_ref, out_ref):
    size = field_ref.shape[-1]
    rows = lax.broadcasted_iota(jnp.int32, (size, size), 0)
    cols = lax.broadcasted_iota(jnp.int32, (size, size), 1)
    centers = [field_ref[p] - step_rate * total_ref[p] for p in range(2)]
    views = []
    for v in centers:
        views.append((
            jnp.where(rows == size - 1, v, pltpu.roll(v, size - 1, 0)),
            jnp.where(rows == 0, v, pltpu.roll(v, 1, 0)),
            jnp.where(cols == size - 1, v, pltpu.roll(v, size - 1, 1)),
            jnp.where(cols == 0, v, pltpu.roll(v, 1, 1)),
        ))
    total_r = jnp.zeros_like(centers[0])
    total_i = jnp.zeros_like(centers[1])
    for n in range(4):
        bent = _bend(views[0][n] - centers[0], views[1][n] - centers[1])
        total_r = total_r + bent[0]
        total_i = total_i + bent[1]
    out_ref[0] = centers[0] + smooth_rate * total_r
    out_ref[1] = centers[1] + smooth_rate * total_i


def _edge_kernel(parity_ref, inner_ref, row_even_ref, row_odd_ref, col_even_ref, col_odd_ref,
                 got_row_even_ref, got_row_odd_ref, got_col_even_ref, got_col_odd_ref, out_ref):
    size, lanes = inner_ref.shape[1], inner_ref.shape[2]
    block = pl.program_id(0)
    row_parity = parity_ref[parity_ref.shape[0] - 2]
    col_parity = parity_ref[parity_ref.shape[0] - 1]
    row_even, row_odd = row_even_ref[...], row_odd_ref[...]
    col_even, col_odd = col_even_ref[...], col_odd_ref[...]
    got_row_even, got_row_odd = got_row_even_ref[...], got_row_odd_ref[...]
    got_col_even, got_col_odd = got_col_even_ref[...], got_col_odd_ref[...]
    top = jnp.where(row_parity == 0, row_odd, row_even)
    bottom = jnp.where(row_parity == 0, row_even, row_odd)
    first = jnp.where(col_parity == 0, col_odd, col_even)
    last = jnp.where(col_parity == 0, col_even, col_odd)
    above = jnp.where(row_parity == 1, got_row_even, got_row_odd)
    below = jnp.where(row_parity == 0, got_row_even, got_row_odd)
    left = jnp.where(col_parity == 1, got_col_even, got_col_odd)
    right = jnp.where(col_parity == 0, got_col_even, got_col_odd)
    rows = lax.broadcasted_iota(jnp.int32, (size, lanes), 0)
    cols = lax.broadcasted_iota(jnp.int32, (size, lanes), 1)
    square = lax.broadcasted_iota(jnp.int32, (lanes, lanes), 0) == lax.broadcasted_iota(
        jnp.int32, (lanes, lanes), 1)

    def as_column(line):
        return jnp.concatenate(
            [
                jnp.sum(jnp.where(square, line[:, h * lanes:(h + 1) * lanes], 0.0), axis=1,
                        keepdims=True)
                for h in range(size // lanes)
            ],
            axis=0,
        )

    edge_col = jnp.where(block == 0, 0, lanes - 1)
    for s in range(inner_ref.shape[0] // 2):
        c0, c1 = 2 * s, 2 * s + 1
        north = _bend(above[c0:c0 + 1] - top[c0:c0 + 1], above[c1:c1 + 1] - top[c1:c1 + 1])
        south = _bend(below[c0:c0 + 1] - bottom[c0:c0 + 1],
                      below[c1:c1 + 1] - bottom[c1:c1 + 1])
        west = _bend(left[c0:c0 + 1] - first[c0:c0 + 1], left[c1:c1 + 1] - first[c1:c1 + 1])
        east = _bend(right[c0:c0 + 1] - last[c0:c0 + 1], right[c1:c1 + 1] - last[c1:c1 + 1])
        for part, c in ((0, c0), (1, c1)):
            side = as_column(jnp.where(block == 0, west[part], east[part]))
            extra = (
                jnp.where(rows == 0, north[part], 0.0)
                + jnp.where(rows == size - 1, south[part], 0.0)
                + jnp.where(cols == edge_col, side, 0.0)
            )
            out_ref[c] = inner_ref[c] + smooth_rate * extra


def smooth_update(field, total, parity, payloads, received):
    channels, size, _ = field.shape
    plane = pl.BlockSpec((2, size, size), lambda s: (s, 0, 0))
    inner = pl.pallas_call(
        _inner_kernel,
        grid=(channels // 2,),
        in_specs=[plane, plane],
        out_specs=plane,
        out_shape=jax.ShapeDtypeStruct(field.shape, jnp.float32),
    )(field, total)
    lanes = 128
    half = pl.BlockSpec((channels, size, lanes), lambda b: (0, 0, b))
    row_part = pl.BlockSpec((channels, lanes), lambda b: (0, b))
    whole = pl.BlockSpec((channels, size), lambda b: (0, 0))
    scalars = pl.BlockSpec(memory_space=pltpu.SMEM)
    return pl.pallas_call(
        _edge_kernel,
        grid=(size // lanes,),
        in_specs=[scalars, half, row_part, row_part, whole, whole, row_part, row_part, whole, whole],
        out_specs=half,
        out_shape=jax.ShapeDtypeStruct(field.shape, jnp.float32),
        input_output_aliases={1: 0},
    )(parity, inner, *payloads, *received)


def block_tables(width):
    index = np.arange(width)
    angles = (index[:, None] * index[None, :] % width) * (2.0 * math.pi / width)
    scale = 1.0 / math.sqrt(width)
    cosine, sine = np.cos(angles) * scale, np.sin(angles) * scale
    plus = np.block([[cosine, -sine], [sine, cosine]])
    minus = np.block([[cosine, sine], [-sine, cosine]])
    lefts, rights = [], []
    for table in (plus, minus):
        high = table.astype(jnp.bfloat16)
        low = (table - high.astype(np.float64)).astype(jnp.bfloat16)
        lefts.append(np.concatenate([high, low, high], axis=1))
        rights.append(np.concatenate([high, low, high], axis=0))
    return jnp.asarray(np.stack(lefts)), jnp.asarray(np.stack(rights))


def _split(x):
    high = x.astype(jnp.bfloat16)
    low = (x - high.astype(jnp.float32)).astype(jnp.bfloat16)
    return high, low


def _dot(a, b):
    return jnp.dot(a, b, preferred_element_type=jnp.float32)


def _times(a, b):
    return (a[0] * b[0] - a[1] * b[1], a[0] * b[1] + a[1] * b[0])


def _conj_times(a, b):
    return (a[0] * b[0] + a[1] * b[1], a[0] * b[1] - a[1] * b[0])


def _transformer(left_ref, right_ref, group, width):
    def transform(pair, sign):
        first, second = (1, 0) if sign < 0 else (0, 1)
        stacked = jnp.concatenate(
            [jnp.concatenate([pair[0][g], pair[1][g]], axis=0) for g in range(group)], axis=1
        )
        high, low = _split(stacked)
        rows = _dot(left_ref[first], jnp.concatenate([high, high, low], axis=0))
        joined = jnp.concatenate(
            [
                jnp.concatenate(
                    [rows[:width, g * width:(g + 1) * width], rows[width:, g * width:(g + 1) * width]],
                    axis=1,
                )
                for g in range(group)
            ],
            axis=0,
        )
        high, low = _split(joined)
        out = _dot(jnp.concatenate([high, high, low], axis=1), right_ref[second])
        return (
            out[:, :width].reshape(group, width, width),
            out[:, width:].reshape(group, width, width),
        )

    return transform


def _layers(win_ref):
    slices = win_ref.shape[1] // 2
    return [
        (win_ref[:, 2 * s].astype(jnp.float32), win_ref[:, 2 * s + 1].astype(jnp.float32))
        for s in range(slices)
    ]


def _forward_kernel(win_ref, probe_ref, prop_ref, left_ref, right_ref, far_ref, inc_ref):
    group, width = win_ref.shape[0], probe_ref.shape[-1]
    transform = _transformer(left_ref, right_ref, group, width)
    layers = _layers(win_ref)
    probe = (probe_ref[0][None], probe_ref[1][None])
    kernel = (prop_ref[0][None], prop_ref[1][None])
    wave = _times(probe, layers[0])
    for s in range(1, len(layers)):
        moved = transform(_times(kernel, transform(wave, -1)), 1)
        inc_ref[:, 2 * (s - 1)] = moved[0]
        inc_ref[:, 2 * (s - 1) + 1] = moved[1]
        wave = _times(layers[s], moved)
    far = transform(wave, -1)
    far_ref[:, 0] = far[0]
    far_ref[:, 1] = far[1]


def _backward_kernel(
    scalar_ref, amp_ref, far_ref, inc_ref, win_ref, probe_ref,
    prop_ref, left_ref, right_ref, border_ref, out_ref, row_even_ref, row_odd_ref, col_even_ref,
    col_odd_ref
):
    group, width = win_ref.shape[0], probe_ref.shape[-1]
    step = pl.program_id(0)
    count = group * pl.num_programs(0)
    transform = _transformer(left_ref, right_ref, group, width)
    layers = _layers(win_ref)
    slices = len(layers)
    probe = (probe_ref[0][None], probe_ref[1][None])
    kernel_conj = (prop_ref[0][None], -prop_ref[1][None])
    amplitude = jnp.stack(
        [amp_ref[scalar_ref[step * group + g]].astype(jnp.float32) for g in range(group)]
    )
    far = (far_ref[:, 0], far_ref[:, 1])
    magnitude = jnp.sqrt(far[0] * far[0] + far[1] * far[1] + 1.0)
    factor = 1.0 - amplitude / magnitude
    back = transform((far[0] * factor, far[1] * factor), 1)
    grads = [None] * slices
    for s in range(slices - 1, 0, -1):
        grads[s] = _conj_times((inc_ref[:, 2 * (s - 1)], inc_ref[:, 2 * (s - 1) + 1]), back)
        back = transform(_times(kernel_conj, transform(_conj_times(layers[s], back), -1)), 1)
    grads[0] = _conj_times(probe, back)
    planes = [part.astype(jnp.bfloat16) for pair in grads for part in pair]
    channels, tile = out_ref.shape[0], out_ref.shape[-1]
    down = lax.broadcasted_iota(jnp.int32, (tile, width), 0) - lax.broadcasted_iota(
        jnp.int32, (tile, width), 1)
    across = lax.broadcasted_iota(jnp.int32, (width, tile), 1) - lax.broadcasted_iota(
        jnp.int32, (width, tile), 0)
    placed, col_picks = [], []
    for g in range(group):
        top = scalar_ref[count + step * group + g]
        left = scalar_ref[2 * count + step * group + g]
        row_pick = (down == top).astype(jnp.bfloat16)
        col_picks.append((across == left).astype(jnp.bfloat16))
        stacked = jnp.concatenate([plane[g] for plane in planes], axis=1)
        placed.append(_dot(row_pick, stacked).astype(jnp.bfloat16))
    spread = jnp.concatenate(
        [
            jnp.concatenate([rows[:, c * width:(c + 1) * width] for rows in placed], axis=1)
            for c in range(channels)
        ],
        axis=0,
    )
    contribution = _dot(spread, jnp.concatenate(col_picks, axis=0)).reshape(channels, tile, tile)

    @pl.when(step == 0)
    def _():
        out_ref[...] = jnp.zeros_like(out_ref)

    out_ref[...] += contribution

    @pl.when(step == pl.num_programs(0) - 1)
    def _():
        lanes = lax.broadcasted_iota(jnp.int32, (8, tile), 1)
        which = jnp.where(lax.broadcasted_iota(jnp.int32, (8, tile), 0) == 0, 0, tile - 1)
        pick = (lanes == which).astype(jnp.bfloat16)
        row_parity = scalar_ref[3 * count]
        col_parity = scalar_ref[3 * count + 1]
        for c in range(channels):
            plane = out_ref[c]
            top = border_ref[0, c:c + 1, :] - step_rate * plane[0:1, :]
            bottom = border_ref[1, c:c + 1, :] - step_rate * plane[tile - 1:tile, :]
            row_even_ref[c:c + 1, :] = jnp.where(row_parity == 0, bottom, top)
            row_odd_ref[c:c + 1, :] = jnp.where(row_parity == 1, bottom, top)
            high = plane.astype(jnp.bfloat16)
            rest = plane - high.astype(jnp.float32)
            middle = rest.astype(jnp.bfloat16)
            low = (rest - middle.astype(jnp.float32)).astype(jnp.bfloat16)
            cols = None
            for part in (high, middle, low):
                term = lax.dot_general(
                    pick, part, (((1,), (1,)), ((), ())), preferred_element_type=jnp.float32
                )
                cols = term if cols is None else cols + term
            first = border_ref[2, c:c + 1, :] - step_rate * cols[0:1]
            last = border_ref[3, c:c + 1, :] - step_rate * cols[1:2]
            col_even_ref[c:c + 1, :] = jnp.where(col_parity == 0, last, first)
            col_odd_ref[c:c + 1, :] = jnp.where(col_parity == 1, last, first)


def forward_waves(windows, probe, kernel, tables, group=16):
    count, channels, width, _ = windows.shape
    group = math.gcd(count, group)
    left_tables, right_tables = tables
    fixed = lambda k: (0, 0, 0)
    return pl.pallas_call(
        _forward_kernel,
        grid=(count // group,),
        in_specs=[
            pl.BlockSpec((group, channels, width, width), lambda k: (k, 0, 0, 0)),
            pl.BlockSpec((2, width, width), fixed),
            pl.BlockSpec((2, width, width), fixed),
            pl.BlockSpec(left_tables.shape, fixed),
            pl.BlockSpec(right_tables.shape, fixed),
        ],
        out_specs=[
            pl.BlockSpec((group, 2, width, width), lambda k: (k, 0, 0, 0)),
            pl.BlockSpec((group, channels - 2, width, width), lambda k: (k, 0, 0, 0)),
        ],
        out_shape=[
            jax.ShapeDtypeStruct((count, 2, width, width), jnp.float32),
            jax.ShapeDtypeStruct((count, channels - 2, width, width), jnp.float32),
        ],
    )(windows, probe, kernel, left_tables, right_tables)


def backward_gradients(scalars, amplitudes, far, incoming, windows, probe, kernel, tables, border,
                       group=16):
    count, channels, width, _ = windows.shape
    tile = border.shape[-1]
    group = math.gcd(count, group)
    left_tables, right_tables = tables
    fixed = lambda k, *_: (0, 0, 0)
    batch = lambda k, *_: (k, 0, 0, 0)
    line = pl.BlockSpec((channels, tile), lambda k, *_: (0, 0))
    grid_spec = pltpu.PrefetchScalarGridSpec(
        num_scalar_prefetch=1,
        grid=(count // group,),
        in_specs=[
            pl.BlockSpec(amplitudes.shape, fixed),
            pl.BlockSpec((group, 2, width, width), batch),
            pl.BlockSpec((group, channels - 2, width, width), batch),
            pl.BlockSpec((group, channels, width, width), batch),
            pl.BlockSpec((2, width, width), fixed),
            pl.BlockSpec((2, width, width), fixed),
            pl.BlockSpec(left_tables.shape, fixed),
            pl.BlockSpec(right_tables.shape, fixed),
            pl.BlockSpec(border.shape, fixed),
        ],
        out_specs=[pl.BlockSpec((channels, tile, tile), fixed), line, line, line, line],
    )
    edge = jax.ShapeDtypeStruct((channels, tile), jnp.float32)
    return pl.pallas_call(
        _backward_kernel,
        grid_spec=grid_spec,
        out_shape=[jax.ShapeDtypeStruct((channels, tile, tile), jnp.float32), edge, edge, edge, edge],
    )(scalars, amplitudes, far, incoming, windows, probe, kernel, left_tables, right_tables, border)


def per_device(object_init, probe, propagator_phase, measured, corners, owner_column):
    width = probe.shape[-1]
    field = object_init
    tile = field.shape[1]
    capacity = measured.shape[3]
    columns = lax.axis_size("ty")
    tops = corners[0, 0, :, 0]
    lefts = corners[0, 0, :, 1]
    owner = owner_column[0, 0, :, 0]
    slot = slot_table(owner)
    target = jnp.clip(owner * capacity + slot, 0, columns * capacity - 1)
    gathered = lax.all_to_all(measured[0, 0], "ty", split_axis=0, concat_axis=0, tiled=True)
    gathered = gathered.reshape(columns * capacity, width, width)
    offsets = jnp.arange(width)
    cells = jnp.arange(tile)
    row_pick = (cells[None, None, :] == (tops[:, None, None] + offsets[None, :, None])).astype(
        jnp.bfloat16
    )
    col_pick = (cells[None, :, None] == (lefts[:, None, None] + offsets[None, None, :])).astype(
        jnp.bfloat16
    )
    field_low = field.astype(jnp.bfloat16)
    rows = jnp.einsum(
        "kir,crs->kcis", row_pick, field_low, preferred_element_type=jnp.float32
    ).astype(jnp.bfloat16)
    windows = jnp.einsum(
        "kcis,ksj->kcij", rows, col_pick, preferred_element_type=jnp.float32
    ).astype(jnp.bfloat16)
    tables = block_tables(width)
    kernel = jnp.stack([jnp.cos(propagator_phase), jnp.sin(propagator_phase)])
    far, incoming = forward_waves(windows, probe, kernel, tables)
    parity = jnp.stack([lax.axis_index("tx") % 2, lax.axis_index("ty") % 2])
    scalars = jnp.concatenate([target, tops, lefts, parity]).astype(jnp.int32)
    border = jnp.stack([field[:, 0, :], field[:, -1, :], field[:, :, 0], field[:, :, -1]])
    total, *payloads = backward_gradients(
        scalars, gathered, far, incoming, windows, probe, kernel, tables, border
    )
    received = _swap("tx", payloads[0], payloads[1]) + _swap("ty", payloads[2], payloads[3])
    return smooth_update(field, total, scalars, payloads, received)


def solution(mesh):
    placed = (
        P(None, "tx", "ty"),
        P(),
        P(),
        P("tx", "ty", None, None, None, None),
        P("tx", "ty", None, None),
        P("tx", "ty", None, None),
    )
    return jax.shard_map(
        per_device, mesh=mesh, in_specs=placed, out_specs=P(None, "tx", "ty"), check_vma=False
    )
```

```python
import math

import jax
import numpy as np
import jax.numpy as jnp
from jax import lax
from jax.experimental import pallas as pl
from jax.experimental.pallas import tpu as pltpu
from jax.sharding import PartitionSpec as P

step_rate = 0.5
smooth_rate = 0.2


def slot_table(owner):
    order = jnp.arange(owner.shape[0])
    same = owner[:, None] == owner[None, :]
    earlier = order[None, :] < order[:, None]
    return jnp.sum(jnp.where(same & earlier, 1, 0), axis=1).astype(jnp.int32)


def _swap(axis, even_payload, odd_payload):
    size = lax.axis_size(axis)
    even = [(i, i + 1) for i in range(0, size - 1, 2)] + [(i + 1, i) for i in range(0, size - 1, 2)]
    odd = [(i, i + 1) for i in range(1, size - 1, 2)] + [(i + 1, i) for i in range(1, size - 1, 2)]
    return lax.ppermute(even_payload, axis, even), lax.ppermute(odd_payload, axis, odd)


def _bend(real, imag):
    weight = 1.0 / jnp.sqrt(1.0 + real * real + imag * imag)
    return real * weight, imag * weight


def _inner_kernel(field_ref, total_ref, out_ref):
    size = field_ref.shape[-1]
    rows = lax.broadcasted_iota(jnp.int32, (size, size), 0)
    cols = lax.broadcasted_iota(jnp.int32, (size, size), 1)
    for s in range(field_ref.shape[0] // 2):
        centers = [field_ref[2 * s + p] - step_rate * total_ref[2 * s + p] for p in range(2)]
        views = []
        for v in centers:
            views.append((
                jnp.where(rows == size - 1, v, pltpu.roll(v, size - 1, 0)),
                jnp.where(rows == 0, v, pltpu.roll(v, 1, 0)),
                jnp.where(cols == size - 1, v, pltpu.roll(v, size - 1, 1)),
                jnp.where(cols == 0, v, pltpu.roll(v, 1, 1)),
            ))
        total_r = jnp.zeros_like(centers[0])
        total_i = jnp.zeros_like(centers[1])
        for n in range(4):
            bent = _bend(views[0][n] - centers[0], views[1][n] - centers[1])
            total_r = total_r + bent[0]
            total_i = total_i + bent[1]
        out_ref[2 * s] = centers[0] + smooth_rate * total_r
        out_ref[2 * s + 1] = centers[1] + smooth_rate * total_i


def _edge_kernel(parity_ref, inner_ref, row_even_ref, row_odd_ref, col_even_ref, col_odd_ref,
                 got_row_even_ref, got_row_odd_ref, got_col_even_ref, got_col_odd_ref, out_ref):
    size, lanes = inner_ref.shape[1], inner_ref.shape[2]
    block = pl.program_id(0)
    row_parity = parity_ref[parity_ref.shape[0] - 2]
    col_parity = parity_ref[parity_ref.shape[0] - 1]
    row_even, row_odd = row_even_ref[...], row_odd_ref[...]
    col_even, col_odd = col_even_ref[...], col_odd_ref[...]
    got_row_even, got_row_odd = got_row_even_ref[...], got_row_odd_ref[...]
    got_col_even, got_col_odd = got_col_even_ref[...], got_col_odd_ref[...]
    top = jnp.where(row_parity == 0, row_odd, row_even)
    bottom = jnp.where(row_parity == 0, row_even, row_odd)
    first = jnp.where(col_parity == 0, col_odd, col_even)
    last = jnp.where(col_parity == 0, col_even, col_odd)
    above = jnp.where(row_parity == 1, got_row_even, got_row_odd)
    below = jnp.where(row_parity == 0, got_row_even, got_row_odd)
    left = jnp.where(col_parity == 1, got_col_even, got_col_odd)
    right = jnp.where(col_parity == 0, got_col_even, got_col_odd)
    rows = lax.broadcasted_iota(jnp.int32, (size, lanes), 0)
    cols = lax.broadcasted_iota(jnp.int32, (size, lanes), 1)
    square = lax.broadcasted_iota(jnp.int32, (lanes, lanes), 0) == lax.broadcasted_iota(
        jnp.int32, (lanes, lanes), 1)

    def as_column(line):
        return jnp.concatenate(
            [
                jnp.sum(jnp.where(square, line[:, h * lanes:(h + 1) * lanes], 0.0), axis=1,
                        keepdims=True)
                for h in range(size // lanes)
            ],
            axis=0,
        )

    edge_col = jnp.where(block == 0, 0, lanes - 1)
    for s in range(inner_ref.shape[0] // 2):
        c0, c1 = 2 * s, 2 * s + 1
        north = _bend(above[c0:c0 + 1] - top[c0:c0 + 1], above[c1:c1 + 1] - top[c1:c1 + 1])
        south = _bend(below[c0:c0 + 1] - bottom[c0:c0 + 1],
                      below[c1:c1 + 1] - bottom[c1:c1 + 1])
        west = _bend(left[c0:c0 + 1] - first[c0:c0 + 1], left[c1:c1 + 1] - first[c1:c1 + 1])
        east = _bend(right[c0:c0 + 1] - last[c0:c0 + 1], right[c1:c1 + 1] - last[c1:c1 + 1])
        for part, c in ((0, c0), (1, c1)):
            side = as_column(jnp.where(block == 0, west[part], east[part]))
            extra = (
                jnp.where(rows == 0, north[part], 0.0)
                + jnp.where(rows == size - 1, south[part], 0.0)
                + jnp.where(cols == edge_col, side, 0.0)
            )
            out_ref[c] = inner_ref[c] + smooth_rate * extra


def smooth_update(field, total, parity, payloads, received):
    channels, size, _ = field.shape
    plane = pl.BlockSpec((channels, size, size), lambda s: (0, 0, 0))
    inner = pl.pallas_call(
        _inner_kernel,
        grid=(1,),
        in_specs=[plane, plane],
        out_specs=plane,
        out_shape=jax.ShapeDtypeStruct(field.shape, jnp.float32),
    )(field, total)
    lanes = 128
    half = pl.BlockSpec((channels, size, lanes), lambda b: (0, 0, b))
    row_part = pl.BlockSpec((channels, lanes), lambda b: (0, b))
    whole = pl.BlockSpec((channels, size), lambda b: (0, 0))
    scalars = pl.BlockSpec(memory_space=pltpu.SMEM)
    return pl.pallas_call(
        _edge_kernel,
        grid=(size // lanes,),
        in_specs=[scalars, half, row_part, row_part, whole, whole, row_part, row_part, whole, whole],
        out_specs=half,
        out_shape=jax.ShapeDtypeStruct(field.shape, jnp.float32),
        input_output_aliases={1: 0},
    )(parity, inner, *payloads, *received)


def block_tables(width):
    index = np.arange(width)
    angles = (index[:, None] * index[None, :] % width) * (2.0 * math.pi / width)
    scale = 1.0 / math.sqrt(width)
    cosine, sine = np.cos(angles) * scale, np.sin(angles) * scale
    plus = np.block([[cosine, -sine], [sine, cosine]])
    minus = np.block([[cosine, sine], [-sine, cosine]])
    lefts, rights = [], []
    for table in (plus, minus):
        high = table.astype(jnp.bfloat16)
        low = (table - high.astype(np.float64)).astype(jnp.bfloat16)
        lefts.append(np.concatenate([high, low, high], axis=1))
        rights.append(np.concatenate([high, low, high], axis=0))
    return jnp.asarray(np.stack(lefts)), jnp.asarray(np.stack(rights))


def _split(x):
    high = x.astype(jnp.bfloat16)
    low = (x - high.astype(jnp.float32)).astype(jnp.bfloat16)
    return high, low


def _dot(a, b):
    return jnp.dot(a, b, preferred_element_type=jnp.float32)


def _times(a, b):
    return (a[0] * b[0] - a[1] * b[1], a[0] * b[1] + a[1] * b[0])


def _conj_times(a, b):
    return (a[0] * b[0] + a[1] * b[1], a[0] * b[1] - a[1] * b[0])


def _transformer(left_ref, right_ref, group, width):
    def transform(pair, sign):
        first, second = (1, 0) if sign < 0 else (0, 1)
        stacked = jnp.concatenate(
            [jnp.concatenate([pair[0][g], pair[1][g]], axis=0) for g in range(group)], axis=1
        )
        high, low = _split(stacked)
        rows = _dot(left_ref[first], jnp.concatenate([high, high, low], axis=0))
        joined = jnp.concatenate(
            [
                jnp.concatenate(
                    [rows[:width, g * width:(g + 1) * width], rows[width:, g * width:(g + 1) * width]],
                    axis=1,
                )
                for g in range(group)
            ],
            axis=0,
        )
        high, low = _split(joined)
        out = _dot(jnp.concatenate([high, high, low], axis=1), right_ref[second])
        return (
            out[:, :width].reshape(group, width, width),
            out[:, width:].reshape(group, width, width),
        )

    return transform


def _layers(win_ref):
    slices = win_ref.shape[1] // 2
    return [
        (win_ref[:, 2 * s].astype(jnp.float32), win_ref[:, 2 * s + 1].astype(jnp.float32))
        for s in range(slices)
    ]


def _forward_kernel(win_ref, probe_ref, prop_ref, left_ref, right_ref, far_ref, inc_ref):
    group, width = win_ref.shape[0], probe_ref.shape[-1]
    transform = _transformer(left_ref, right_ref, group, width)
    layers = _layers(win_ref)
    probe = (probe_ref[0][None], probe_ref[1][None])
    kernel = (prop_ref[0][None], prop_ref[1][None])
    wave = _times(probe, layers[0])
    for s in range(1, len(layers)):
        moved = transform(_times(kernel, transform(wave, -1)), 1)
        inc_ref[:, 2 * (s - 1)] = moved[0]
        inc_ref[:, 2 * (s - 1) + 1] = moved[1]
        wave = _times(layers[s], moved)
    far = transform(wave, -1)
    far_ref[:, 0] = far[0]
    far_ref[:, 1] = far[1]


def _backward_kernel(
    scalar_ref, amp_ref, far_ref, inc_ref, win_ref, probe_ref,
    prop_ref, left_ref, right_ref, border_ref, out_ref, row_even_ref, row_odd_ref, col_even_ref,
    col_odd_ref
):
    group, width = win_ref.shape[0], probe_ref.shape[-1]
    step = pl.program_id(0)
    count = group * pl.num_programs(0)
    transform = _transformer(left_ref, right_ref, group, width)
    layers = _layers(win_ref)
    slices = len(layers)
    probe = (probe_ref[0][None], probe_ref[1][None])
    kernel_conj = (prop_ref[0][None], -prop_ref[1][None])
    amplitude = jnp.stack(
        [amp_ref[scalar_ref[step * group + g]].astype(jnp.float32) for g in range(group)]
    )
    far = (far_ref[:, 0], far_ref[:, 1])
    magnitude = jnp.sqrt(far[0] * far[0] + far[1] * far[1] + 1.0)
    factor = 1.0 - amplitude / magnitude
    back = transform((far[0] * factor, far[1] * factor), 1)
    grads = [None] * slices
    for s in range(slices - 1, 0, -1):
        grads[s] = _conj_times((inc_ref[:, 2 * (s - 1)], inc_ref[:, 2 * (s - 1) + 1]), back)
        back = transform(_times(kernel_conj, transform(_conj_times(layers[s], back), -1)), 1)
    grads[0] = _conj_times(probe, back)
    planes = [part.astype(jnp.bfloat16) for pair in grads for part in pair]
    channels, tile = out_ref.shape[0], out_ref.shape[-1]
    down = lax.broadcasted_iota(jnp.int32, (tile, width), 0) - lax.broadcasted_iota(
        jnp.int32, (tile, width), 1)
    across = lax.broadcasted_iota(jnp.int32, (width, tile), 1) - lax.broadcasted_iota(
        jnp.int32, (width, tile), 0)
    placed, col_picks = [], []
    for g in range(group):
        top = scalar_ref[count + step * group + g]
        left = scalar_ref[2 * count + step * group + g]
        row_pick = (down == top).astype(jnp.bfloat16)
        col_picks.append((across == left).astype(jnp.bfloat16))
        stacked = jnp.concatenate([plane[g] for plane in planes], axis=1)
        placed.append(_dot(row_pick, stacked).astype(jnp.bfloat16))
    spread = jnp.concatenate(
        [
            jnp.concatenate([rows[:, c * width:(c + 1) * width] for rows in placed], axis=1)
            for c in range(channels)
        ],
        axis=0,
    )
    contribution = _dot(spread, jnp.concatenate(col_picks, axis=0)).reshape(channels, tile, tile)

    @pl.when(step == 0)
    def _():
        out_ref[...] = jnp.zeros_like(out_ref)

    out_ref[...] += contribution

    @pl.when(step == pl.num_programs(0) - 1)
    def _():
        lanes = lax.broadcasted_iota(jnp.int32, (8, tile), 1)
        which = jnp.where(lax.broadcasted_iota(jnp.int32, (8, tile), 0) == 0, 0, tile - 1)
        pick = (lanes == which).astype(jnp.bfloat16)
        row_parity = scalar_ref[3 * count]
        col_parity = scalar_ref[3 * count + 1]
        for c in range(channels):
            plane = out_ref[c]
            top = border_ref[0, c:c + 1, :] - step_rate * plane[0:1, :]
            bottom = border_ref[1, c:c + 1, :] - step_rate * plane[tile - 1:tile, :]
            row_even_ref[c:c + 1, :] = jnp.where(row_parity == 0, bottom, top)
            row_odd_ref[c:c + 1, :] = jnp.where(row_parity == 1, bottom, top)
            high = plane.astype(jnp.bfloat16)
            rest = plane - high.astype(jnp.float32)
            middle = rest.astype(jnp.bfloat16)
            low = (rest - middle.astype(jnp.float32)).astype(jnp.bfloat16)
            cols = None
            for part in (high, middle, low):
                term = lax.dot_general(
                    pick, part, (((1,), (1,)), ((), ())), preferred_element_type=jnp.float32
                )
                cols = term if cols is None else cols + term
            first = border_ref[2, c:c + 1, :] - step_rate * cols[0:1]
            last = border_ref[3, c:c + 1, :] - step_rate * cols[1:2]
            col_even_ref[c:c + 1, :] = jnp.where(col_parity == 0, last, first)
            col_odd_ref[c:c + 1, :] = jnp.where(col_parity == 1, last, first)


def forward_waves(windows, probe, kernel, tables, group=16):
    count, channels, width, _ = windows.shape
    group = math.gcd(count, group)
    left_tables, right_tables = tables
    fixed = lambda k: (0, 0, 0)
    return pl.pallas_call(
        _forward_kernel,
        grid=(count // group,),
        in_specs=[
            pl.BlockSpec((group, channels, width, width), lambda k: (k, 0, 0, 0)),
            pl.BlockSpec((2, width, width), fixed),
            pl.BlockSpec((2, width, width), fixed),
            pl.BlockSpec(left_tables.shape, fixed),
            pl.BlockSpec(right_tables.shape, fixed),
        ],
        out_specs=[
            pl.BlockSpec((group, 2, width, width), lambda k: (k, 0, 0, 0)),
            pl.BlockSpec((group, channels - 2, width, width), lambda k: (k, 0, 0, 0)),
        ],
        out_shape=[
            jax.ShapeDtypeStruct((count, 2, width, width), jnp.float32),
            jax.ShapeDtypeStruct((count, channels - 2, width, width), jnp.float32),
        ],
    )(windows, probe, kernel, left_tables, right_tables)


def backward_gradients(scalars, amplitudes, far, incoming, windows, probe, kernel, tables, border,
                       group=16):
    count, channels, width, _ = windows.shape
    tile = border.shape[-1]
    group = math.gcd(count, group)
    left_tables, right_tables = tables
    fixed = lambda k, *_: (0, 0, 0)
    batch = lambda k, *_: (k, 0, 0, 0)
    line = pl.BlockSpec((channels, tile), lambda k, *_: (0, 0))
    grid_spec = pltpu.PrefetchScalarGridSpec(
        num_scalar_prefetch=1,
        grid=(count // group,),
        in_specs=[
            pl.BlockSpec(amplitudes.shape, fixed),
            pl.BlockSpec((group, 2, width, width), batch),
            pl.BlockSpec((group, channels - 2, width, width), batch),
            pl.BlockSpec((group, channels, width, width), batch),
            pl.BlockSpec((2, width, width), fixed),
            pl.BlockSpec((2, width, width), fixed),
            pl.BlockSpec(left_tables.shape, fixed),
            pl.BlockSpec(right_tables.shape, fixed),
            pl.BlockSpec(border.shape, fixed),
        ],
        out_specs=[pl.BlockSpec((channels, tile, tile), fixed), line, line, line, line],
    )
    edge = jax.ShapeDtypeStruct((channels, tile), jnp.float32)
    return pl.pallas_call(
        _backward_kernel,
        grid_spec=grid_spec,
        out_shape=[jax.ShapeDtypeStruct((channels, tile, tile), jnp.float32), edge, edge, edge, edge],
    )(scalars, amplitudes, far, incoming, windows, probe, kernel, left_tables, right_tables, border)


def per_device(object_init, probe, propagator_phase, measured, corners, owner_column):
    width = probe.shape[-1]
    field = object_init
    tile = field.shape[1]
    capacity = measured.shape[3]
    columns = lax.axis_size("ty")
    tops = corners[0, 0, :, 0]
    lefts = corners[0, 0, :, 1]
    owner = owner_column[0, 0, :, 0]
    slot = slot_table(owner)
    target = jnp.clip(owner * capacity + slot, 0, columns * capacity - 1)
    gathered = lax.all_to_all(measured[0, 0], "ty", split_axis=0, concat_axis=0, tiled=True)
    gathered = gathered.reshape(columns * capacity, width, width)
    offsets = jnp.arange(width)
    cells = jnp.arange(tile)
    row_pick = (cells[None, None, :] == (tops[:, None, None] + offsets[None, :, None])).astype(
        jnp.bfloat16
    )
    col_pick = (cells[None, :, None] == (lefts[:, None, None] + offsets[None, None, :])).astype(
        jnp.bfloat16
    )
    field_low = field.astype(jnp.bfloat16)
    rows = jnp.einsum(
        "kir,crs->kcis", row_pick, field_low, preferred_element_type=jnp.float32
    ).astype(jnp.bfloat16)
    windows = jnp.einsum(
        "kcis,ksj->kcij", rows, col_pick, preferred_element_type=jnp.float32
    ).astype(jnp.bfloat16)
    tables = block_tables(width)
    kernel = jnp.stack([jnp.cos(propagator_phase), jnp.sin(propagator_phase)])
    far, incoming = forward_waves(windows, probe, kernel, tables)
    parity = jnp.stack([lax.axis_index("tx") % 2, lax.axis_index("ty") % 2])
    scalars = jnp.concatenate([target, tops, lefts, parity]).astype(jnp.int32)
    border = jnp.stack([field[:, 0, :], field[:, -1, :], field[:, :, 0], field[:, :, -1]])
    total, *payloads = backward_gradients(
        scalars, gathered, far, incoming, windows, probe, kernel, tables, border
    )
    received = _swap("tx", payloads[0], payloads[1]) + _swap("ty", payloads[2], payloads[3])
    return smooth_update(field, total, scalars, payloads, received)


def solution(mesh):
    placed = (
        P(None, "tx", "ty"),
        P(),
        P(),
        P("tx", "ty", None, None, None, None),
        P("tx", "ty", None, None),
        P("tx", "ty", None, None),
    )
    return jax.shard_map(
        per_device, mesh=mesh, in_specs=placed, out_specs=P(None, "tx", "ty"), check_vma=False
    )
```

```python
import math

import jax
import numpy as np
import jax.numpy as jnp
from jax import lax
from jax.experimental import pallas as pl
from jax.experimental.pallas import tpu as pltpu
from jax.sharding import PartitionSpec as P

step_rate = 0.5
smooth_rate = 0.2


def slot_table(owner):
    order = jnp.arange(owner.shape[0])
    same = owner[:, None] == owner[None, :]
    earlier = order[None, :] < order[:, None]
    return jnp.sum(jnp.where(same & earlier, 1, 0), axis=1).astype(jnp.int32)


def _swap(axis, even_payload, odd_payload):
    size = lax.axis_size(axis)
    even = [(i, i + 1) for i in range(0, size - 1, 2)] + [(i + 1, i) for i in range(0, size - 1, 2)]
    odd = [(i, i + 1) for i in range(1, size - 1, 2)] + [(i + 1, i) for i in range(1, size - 1, 2)]
    return lax.ppermute(even_payload, axis, even), lax.ppermute(odd_payload, axis, odd)


def _bend(real, imag):
    weight = 1.0 / jnp.sqrt(1.0 + real * real + imag * imag)
    return real * weight, imag * weight


def _inner_kernel(field_ref, total_ref, out_ref):
    size = field_ref.shape[-1]
    rows = lax.broadcasted_iota(jnp.int32, (size, size), 0)
    cols = lax.broadcasted_iota(jnp.int32, (size, size), 1)
    centers = [field_ref[p] - step_rate * total_ref[p] for p in range(2)]
    views = []
    for v in centers:
        views.append((
            jnp.where(rows == size - 1, v, pltpu.roll(v, size - 1, 0)),
            jnp.where(rows == 0, v, pltpu.roll(v, 1, 0)),
            jnp.where(cols == size - 1, v, pltpu.roll(v, size - 1, 1)),
            jnp.where(cols == 0, v, pltpu.roll(v, 1, 1)),
        ))
    total_r = jnp.zeros_like(centers[0])
    total_i = jnp.zeros_like(centers[1])
    for n in range(4):
        bent = _bend(views[0][n] - centers[0], views[1][n] - centers[1])
        total_r = total_r + bent[0]
        total_i = total_i + bent[1]
    out_ref[0] = centers[0] + smooth_rate * total_r
    out_ref[1] = centers[1] + smooth_rate * total_i


def _edge_kernel(parity_ref, inner_ref, row_even_ref, row_odd_ref, col_even_ref, col_odd_ref,
                 got_row_even_ref, got_row_odd_ref, got_col_even_ref, got_col_odd_ref, out_ref):
    size, lanes = inner_ref.shape[1], inner_ref.shape[2]
    block = pl.program_id(0)
    row_parity = parity_ref[parity_ref.shape[0] - 2]
    col_parity = parity_ref[parity_ref.shape[0] - 1]
    row_even, row_odd = row_even_ref[...], row_odd_ref[...]
    col_even, col_odd = col_even_ref[...], col_odd_ref[...]
    got_row_even, got_row_odd = got_row_even_ref[...], got_row_odd_ref[...]
    got_col_even, got_col_odd = got_col_even_ref[...], got_col_odd_ref[...]
    top = jnp.where(row_parity == 0, row_odd, row_even)
    bottom = jnp.where(row_parity == 0, row_even, row_odd)
    first = jnp.where(col_parity == 0, col_odd, col_even)
    last = jnp.where(col_parity == 0, col_even, col_odd)
    above = jnp.where(row_parity == 1, got_row_even, got_row_odd)
    below = jnp.where(row_parity == 0, got_row_even, got_row_odd)
    left = jnp.where(col_parity == 1, got_col_even, got_col_odd)
    right = jnp.where(col_parity == 0, got_col_even, got_col_odd)
    rows = lax.broadcasted_iota(jnp.int32, (size, lanes), 0)
    cols = lax.broadcasted_iota(jnp.int32, (size, lanes), 1)
    square = lax.broadcasted_iota(jnp.int32, (lanes, lanes), 0) == lax.broadcasted_iota(
        jnp.int32, (lanes, lanes), 1)

    def as_column(line):
        return jnp.concatenate(
            [
                jnp.sum(jnp.where(square, line[:, h * lanes:(h + 1) * lanes], 0.0), axis=1,
                        keepdims=True)
                for h in range(size // lanes)
            ],
            axis=0,
        )

    edge_col = jnp.where(block == 0, 0, lanes - 1)
    for s in range(inner_ref.shape[0] // 2):
        c0, c1 = 2 * s, 2 * s + 1
        north = _bend(above[c0:c0 + 1] - top[c0:c0 + 1], above[c1:c1 + 1] - top[c1:c1 + 1])
        south = _bend(below[c0:c0 + 1] - bottom[c0:c0 + 1],
                      below[c1:c1 + 1] - bottom[c1:c1 + 1])
        west = _bend(left[c0:c0 + 1] - first[c0:c0 + 1], left[c1:c1 + 1] - first[c1:c1 + 1])
        east = _bend(right[c0:c0 + 1] - last[c0:c0 + 1], right[c1:c1 + 1] - last[c1:c1 + 1])
        for part, c in ((0, c0), (1, c1)):
            side = as_column(jnp.where(block == 0, west[part], east[part]))
            extra = (
                jnp.where(rows == 0, north[part], 0.0)
                + jnp.where(rows == size - 1, south[part], 0.0)
                + jnp.where(cols == edge_col, side, 0.0)
            )
            out_ref[c] = inner_ref[c] + smooth_rate * extra


def smooth_update(field, total, parity, payloads, received):
    channels, size, _ = field.shape
    plane = pl.BlockSpec((2, size, size), lambda s: (s, 0, 0))
    inner = pl.pallas_call(
        _inner_kernel,
        grid=(channels // 2,),
        in_specs=[plane, plane],
        out_specs=plane,
        out_shape=jax.ShapeDtypeStruct(field.shape, jnp.float32),
    )(field, total)
    lanes = 128
    half = pl.BlockSpec((channels, size, lanes), lambda b: (0, 0, b))
    row_part = pl.BlockSpec((channels, lanes), lambda b: (0, b))
    whole = pl.BlockSpec((channels, size), lambda b: (0, 0))
    scalars = pl.BlockSpec(memory_space=pltpu.SMEM)
    return pl.pallas_call(
        _edge_kernel,
        grid=(size // lanes,),
        in_specs=[scalars, half, row_part, row_part, whole, whole, row_part, row_part, whole, whole],
        out_specs=half,
        out_shape=jax.ShapeDtypeStruct(field.shape, jnp.float32),
        input_output_aliases={1: 0},
    )(parity, inner, *payloads, *received)


def block_tables(width):
    index = np.arange(width)
    angles = (index[:, None] * index[None, :] % width) * (2.0 * math.pi / width)
    scale = 1.0 / math.sqrt(width)
    cosine, sine = np.cos(angles) * scale, np.sin(angles) * scale
    plus = np.block([[cosine, -sine], [sine, cosine]])
    minus = np.block([[cosine, sine], [-sine, cosine]])
    lefts, rights = [], []
    for table in (plus, minus):
        high = table.astype(jnp.bfloat16)
        low = (table - high.astype(np.float64)).astype(jnp.bfloat16)
        lefts.append(np.concatenate([high, low, high], axis=1))
        rights.append(np.concatenate([high, low, high], axis=0))
    return jnp.asarray(np.stack(lefts)), jnp.asarray(np.stack(rights))


def _split(x):
    high = x.astype(jnp.bfloat16)
    low = (x - high.astype(jnp.float32)).astype(jnp.bfloat16)
    return high, low


def _dot(a, b):
    return jnp.dot(a, b, preferred_element_type=jnp.float32)


def _times(a, b):
    return (a[0] * b[0] - a[1] * b[1], a[0] * b[1] + a[1] * b[0])


def _conj_times(a, b):
    return (a[0] * b[0] + a[1] * b[1], a[0] * b[1] - a[1] * b[0])


def _transformer(left_ref, right_ref, group, width):
    def transform(pair, sign):
        first, second = (1, 0) if sign < 0 else (0, 1)
        stacked = jnp.concatenate(
            [jnp.concatenate([pair[0][g], pair[1][g]], axis=0) for g in range(group)], axis=1
        )
        high, low = _split(stacked)
        rows = _dot(left_ref[first], jnp.concatenate([high, high, low], axis=0))
        joined = jnp.concatenate(
            [
                jnp.concatenate(
                    [rows[:width, g * width:(g + 1) * width], rows[width:, g * width:(g + 1) * width]],
                    axis=1,
                )
                for g in range(group)
            ],
            axis=0,
        )
        high, low = _split(joined)
        out = _dot(jnp.concatenate([high, high, low], axis=1), right_ref[second])
        return (
            out[:, :width].reshape(group, width, width),
            out[:, width:].reshape(group, width, width),
        )

    return transform


def _layers(win_ref):
    slices = win_ref.shape[1] // 2
    return [
        (win_ref[:, 2 * s].astype(jnp.float32), win_ref[:, 2 * s + 1].astype(jnp.float32))
        for s in range(slices)
    ]


def _forward_kernel(win_ref, probe_ref, prop_ref, left_ref, right_ref, far_ref, inc_ref):
    group, width = win_ref.shape[0], probe_ref.shape[-1]
    transform = _transformer(left_ref, right_ref, group, width)
    layers = _layers(win_ref)
    probe = (probe_ref[0][None], probe_ref[1][None])
    kernel = (prop_ref[0][None], prop_ref[1][None])
    wave = _times(probe, layers[0])
    for s in range(1, len(layers)):
        moved = transform(_times(kernel, transform(wave, -1)), 1)
        inc_ref[:, 2 * (s - 1)] = moved[0]
        inc_ref[:, 2 * (s - 1) + 1] = moved[1]
        wave = _times(layers[s], moved)
    far = transform(wave, -1)
    far_ref[:, 0] = far[0]
    far_ref[:, 1] = far[1]


def _backward_kernel(
    scalar_ref, amp_ref, far_ref, inc_ref, win_ref, probe_ref,
    prop_ref, left_ref, right_ref, border_ref, out_ref, row_even_ref, row_odd_ref, col_even_ref,
    col_odd_ref
):
    group, width = win_ref.shape[0], probe_ref.shape[-1]
    step = pl.program_id(0)
    count = group * pl.num_programs(0)
    transform = _transformer(left_ref, right_ref, group, width)
    layers = _layers(win_ref)
    slices = len(layers)
    probe = (probe_ref[0][None], probe_ref[1][None])
    kernel_conj = (prop_ref[0][None], -prop_ref[1][None])
    amplitude = jnp.stack(
        [amp_ref[scalar_ref[step * group + g]].astype(jnp.float32) for g in range(group)]
    )
    far = (far_ref[:, 0], far_ref[:, 1])
    magnitude = jnp.sqrt(far[0] * far[0] + far[1] * far[1] + 1.0)
    factor = 1.0 - amplitude / magnitude
    back = transform((far[0] * factor, far[1] * factor), 1)
    grads = [None] * slices
    for s in range(slices - 1, 0, -1):
        grads[s] = _conj_times((inc_ref[:, 2 * (s - 1)], inc_ref[:, 2 * (s - 1) + 1]), back)
        back = transform(_times(kernel_conj, transform(_conj_times(layers[s], back), -1)), 1)
    grads[0] = _conj_times(probe, back)
    planes = [part.astype(jnp.bfloat16) for pair in grads for part in pair]
    channels, tile = out_ref.shape[0], out_ref.shape[-1]
    down = lax.broadcasted_iota(jnp.int32, (tile, width), 0) - lax.broadcasted_iota(
        jnp.int32, (tile, width), 1)
    across = lax.broadcasted_iota(jnp.int32, (width, tile), 1) - lax.broadcasted_iota(
        jnp.int32, (width, tile), 0)
    placed, col_picks = [], []
    for g in range(group):
        top = scalar_ref[count + step * group + g]
        left = scalar_ref[2 * count + step * group + g]
        row_pick = (down == top).astype(jnp.bfloat16)
        col_picks.append((across == left).astype(jnp.bfloat16))
        stacked = jnp.concatenate([plane[g] for plane in planes], axis=1)
        placed.append(_dot(row_pick, stacked).astype(jnp.bfloat16))
    spread = jnp.concatenate(
        [
            jnp.concatenate([rows[:, c * width:(c + 1) * width] for rows in placed], axis=1)
            for c in range(channels)
        ],
        axis=0,
    )
    contribution = _dot(spread, jnp.concatenate(col_picks, axis=0)).reshape(channels, tile, tile)

    @pl.when(step == 0)
    def _():
        out_ref[...] = jnp.zeros_like(out_ref)

    out_ref[...] += contribution

    @pl.when(step == pl.num_programs(0) - 1)
    def _():
        lanes = lax.broadcasted_iota(jnp.int32, (8, tile), 1)
        which = jnp.where(lax.broadcasted_iota(jnp.int32, (8, tile), 0) == 0, 0, tile - 1)
        pick = (lanes == which).astype(jnp.bfloat16)
        row_parity = scalar_ref[3 * count]
        col_parity = scalar_ref[3 * count + 1]
        for c in range(channels):
            plane = out_ref[c]
            top = border_ref[0, c:c + 1, :] - step_rate * plane[0:1, :]
            bottom = border_ref[1, c:c + 1, :] - step_rate * plane[tile - 1:tile, :]
            row_even_ref[c:c + 1, :] = jnp.where(row_parity == 0, bottom, top)
            row_odd_ref[c:c + 1, :] = jnp.where(row_parity == 1, bottom, top)
            high = plane.astype(jnp.bfloat16)
            rest = plane - high.astype(jnp.float32)
            middle = rest.astype(jnp.bfloat16)
            low = (rest - middle.astype(jnp.float32)).astype(jnp.bfloat16)
            cols = None
            for part in (high, middle, low):
                term = lax.dot_general(
                    pick, part, (((1,), (1,)), ((), ())), preferred_element_type=jnp.float32
                )
                cols = term if cols is None else cols + term
            first = border_ref[2, c:c + 1, :] - step_rate * cols[0:1]
            last = border_ref[3, c:c + 1, :] - step_rate * cols[1:2]
            col_even_ref[c:c + 1, :] = jnp.where(col_parity == 0, last, first)
            col_odd_ref[c:c + 1, :] = jnp.where(col_parity == 1, last, first)


def forward_waves(windows, probe, kernel, tables, group=16):
    count, channels, width, _ = windows.shape
    group = math.gcd(count, group)
    left_tables, right_tables = tables
    fixed = lambda k: (0, 0, 0)
    return pl.pallas_call(
        _forward_kernel,
        grid=(count // group,),
        in_specs=[
            pl.BlockSpec((group, channels, width, width), lambda k: (k, 0, 0, 0)),
            pl.BlockSpec((2, width, width), fixed),
            pl.BlockSpec((2, width, width), fixed),
            pl.BlockSpec(left_tables.shape, fixed),
            pl.BlockSpec(right_tables.shape, fixed),
        ],
        out_specs=[
            pl.BlockSpec((group, 2, width, width), lambda k: (k, 0, 0, 0)),
            pl.BlockSpec((group, channels - 2, width, width), lambda k: (k, 0, 0, 0)),
        ],
        out_shape=[
            jax.ShapeDtypeStruct((count, 2, width, width), jnp.float32),
            jax.ShapeDtypeStruct((count, channels - 2, width, width), jnp.float32),
        ],
    )(windows, probe, kernel, left_tables, right_tables)


def backward_gradients(scalars, amplitudes, far, incoming, windows, probe, kernel, tables, border,
                       group=8):
    count, channels, width, _ = windows.shape
    tile = border.shape[-1]
    group = math.gcd(count, group)
    left_tables, right_tables = tables
    fixed = lambda k, *_: (0, 0, 0)
    batch = lambda k, *_: (k, 0, 0, 0)
    line = pl.BlockSpec((channels, tile), lambda k, *_: (0, 0))
    grid_spec = pltpu.PrefetchScalarGridSpec(
        num_scalar_prefetch=1,
        grid=(count // group,),
        in_specs=[
            pl.BlockSpec(amplitudes.shape, fixed),
            pl.BlockSpec((group, 2, width, width), batch),
            pl.BlockSpec((group, channels - 2, width, width), batch),
            pl.BlockSpec((group, channels, width, width), batch),
            pl.BlockSpec((2, width, width), fixed),
            pl.BlockSpec((2, width, width), fixed),
            pl.BlockSpec(left_tables.shape, fixed),
            pl.BlockSpec(right_tables.shape, fixed),
            pl.BlockSpec(border.shape, fixed),
        ],
        out_specs=[pl.BlockSpec((channels, tile, tile), fixed), line, line, line, line],
    )
    edge = jax.ShapeDtypeStruct((channels, tile), jnp.float32)
    return pl.pallas_call(
        _backward_kernel,
        grid_spec=grid_spec,
        out_shape=[jax.ShapeDtypeStruct((channels, tile, tile), jnp.float32), edge, edge, edge, edge],
    )(scalars, amplitudes, far, incoming, windows, probe, kernel, left_tables, right_tables, border)


def per_device(object_init, probe, propagator_phase, measured, corners, owner_column):
    width = probe.shape[-1]
    field = object_init
    tile = field.shape[1]
    capacity = measured.shape[3]
    columns = lax.axis_size("ty")
    tops = corners[0, 0, :, 0]
    lefts = corners[0, 0, :, 1]
    owner = owner_column[0, 0, :, 0]
    slot = slot_table(owner)
    target = jnp.clip(owner * capacity + slot, 0, columns * capacity - 1)
    gathered = lax.all_to_all(measured[0, 0], "ty", split_axis=0, concat_axis=0, tiled=True)
    gathered = gathered.reshape(columns * capacity, width, width)
    offsets = jnp.arange(width)
    cells = jnp.arange(tile)
    row_pick = (cells[None, None, :] == (tops[:, None, None] + offsets[None, :, None])).astype(
        jnp.bfloat16
    )
    col_pick = (cells[None, :, None] == (lefts[:, None, None] + offsets[None, None, :])).astype(
        jnp.bfloat16
    )
    field_low = field.astype(jnp.bfloat16)
    rows = jnp.einsum(
        "kir,crs->kcis", row_pick, field_low, preferred_element_type=jnp.float32
    ).astype(jnp.bfloat16)
    windows = jnp.einsum(
        "kcis,ksj->kcij", rows, col_pick, preferred_element_type=jnp.float32
    ).astype(jnp.bfloat16)
    tables = block_tables(width)
    kernel = jnp.stack([jnp.cos(propagator_phase), jnp.sin(propagator_phase)])
    far, incoming = forward_waves(windows, probe, kernel, tables)
    parity = jnp.stack([lax.axis_index("tx") % 2, lax.axis_index("ty") % 2])
    scalars = jnp.concatenate([target, tops, lefts, parity]).astype(jnp.int32)
    border = jnp.stack([field[:, 0, :], field[:, -1, :], field[:, :, 0], field[:, :, -1]])
    total, *payloads = backward_gradients(
        scalars, gathered, far, incoming, windows, probe, kernel, tables, border
    )
    received = _swap("tx", payloads[0], payloads[1]) + _swap("ty", payloads[2], payloads[3])
    return smooth_update(field, total, scalars, payloads, received)


def solution(mesh):
    placed = (
        P(None, "tx", "ty"),
        P(),
        P(),
        P("tx", "ty", None, None, None, None),
        P("tx", "ty", None, None),
        P("tx", "ty", None, None),
    )
    return jax.shard_map(
        per_device, mesh=mesh, in_specs=placed, out_specs=P(None, "tx", "ty"), check_vma=False
    )
```
